32 devices in a mesh: sky: 8 (over z, x), visit: 4 (over y, core).
Axes of the slice: x: 2, y: 2, z: 4, core: 2. Of those that a mesh axis runs over, the one named last changes fastest.
Arguments:
- tile_image: bfloat16 [4, 256, 128, 128], P('visit', 'sky'), may hold values from -1.1953125 to 1.1953125
- tile_variance: bfloat16 [4, 256, 128, 128], P('visit', 'sky'), may hold values from 0.099609375 to 10
- match_coeffs: bfloat16 [4, 256, 9], P('visit', 'sky'), may hold values from 0.25 to 9
- tile_patch: int32 [4, 256, 1], P('visit', 'sky'), may hold values from 0 to 7; in each aligned block of 32 rows (0 to 31, 32 to 63, ..., all dimensions but the last counted through in order) at most 8 rows name the same one
- tile_offset: int32 [4, 256], P('visit', 'sky'), may hold values from 0 to 63
- row_taps: bfloat16 [9, 41], replicated, may hold values from -1.1953125 to 1.1953125
- col_taps: bfloat16 [9, 41], replicated, may hold values from -1.1953125 to 1.1953125
Outputs:
- coadd_image: float32 [8192, 1024], P('sky', 'visit')
- coadd_variance: float32 [8192, 1024], P('sky', 'visit')
- coadd_psf: float32 [8, 41, 41], P('sky')
The draws below stay inside these ranges and needn't reach their ends.
Inputs may be any that keep to these rules, and one draw needn't show every extreme that they name: `tile_patch`: among the 32 tiles of one device, at most 8 intersect any one patch.
All inputs are finite; a program needn't handle non-finite values.
Results may differ from the reference program's by a relative error of at most 0.0029.
Values may be sent and summed in bfloat16 or wider, within the bound.
No kernel may reach another device: no remote copies, remote signals or barrier semaphores. Data moves between devices by JAX's collectives and lax.ppermute only.
A program may use at most 64 MiB of HBM per device.

```python
import math
import jax
import jax.numpy as jnp
import numpy as np
from jax import lax

TILE = 128
GRID = 8
TAPS = 41
BASIS = 9
TILES_DEV = 32
CAP = 8
PATCH = 1024
ROWS = 256
N_SKY = 8
N_VISIT = 4


def draw_match_coeffs(key, part):
    base = jax.random.uniform(key, (N_VISIT, ROWS, BASIS), jnp.float32, 0.25, 1.0)
    level = jnp.arange(N_VISIT, dtype=jnp.float32) / max(N_VISIT - 1, 1)
    ramp = 1.0 + 2.0 * level
    return (base * ramp[:, None, None]).astype(jnp.bfloat16)


def set_ends(values, rng, least, top_value):
    dims = values.shape
    place = [jax.random.randint(jax.random.fold_in(rng, axis), (), 0, dims[axis]) for axis in range(len(dims))]
    values = values.at[tuple(place)].set(least)
    longest = dims.index(max(dims))
    place[longest] = (place[longest] + 1) % dims[longest]
    return values.at[tuple(place)].set(top_value)


def steps_of(own_key, extent, shards, least, largest):
    gain, own = 1.0, jax.random.fold_in(own_key, 6)
    for position, blocks in shards:
        heights = jnp.exp(jax.random.uniform(jax.random.fold_in(own, position), (blocks,), jnp.float32, least / len(shards), largest / len(shards)))
        gain = gain * jnp.repeat(heights, extent[position] // blocks).reshape([-1 if axis == position else 1 for axis in range(len(extent))])
    return gain


def deal_out(rng, own, number, rows, amount, top, reach, slope):
    ranking = jax.random.permutation(rng, amount)
    heavy_load, usual = portions_of(amount, rows * top, reach, slope, True), portions_of(amount, rows * top, reach, slope, False)
    places = jnp.arange(amount)

    def named(tallies, rotation):
        used = int((tallies > 0).sum())
        fixed = max(1, used // 4)
        moved = fixed + (places - fixed + rotation * (used - fixed)) % max(1, amount - fixed)
        return jnp.zeros((amount,), jnp.int32).at[ranking[jnp.where(places < fixed, places, moved)]].set(jnp.asarray(tallies, jnp.int32))

    tallies = jnp.where(number % 4 == 0, named(heavy_load, number // 4), named(usual, number - number // 4 - 1))
    mixed = jax.random.permutation(jax.random.fold_in(own, 3), amount)
    donor, taker = mixed[0:amount // 2 * 2:2], mixed[1:amount // 2 * 2:2]
    margin = jnp.minimum(tallies[donor] - 1, reach - tallies[taker]) // 2
    margin = jnp.where((donor == ranking[0]) | (taker == ranking[0]) | (tallies[taker] == 0), 0, jnp.maximum(margin, 0))
    moved = jax.random.randint(jax.random.fold_in(own, 4), (amount // 2,), 0, 1 << 20) % (margin + 1)
    tallies = tallies.at[donor].add(-moved).at[taker].add(moved)
    labels = jnp.searchsorted(jnp.cumsum(tallies), jnp.arange(rows * top), side="right").astype(jnp.int32)
    listing = labels.reshape(top, rows).T
    listing = listing[jax.random.permutation(jax.random.fold_in(own, 1), rows)]
    rotation = jax.random.randint(jax.random.fold_in(own, 2), (rows, 1), 0, top)
    return jnp.take_along_axis(listing, (jnp.arange(top)[None, :] + rotation) % top, axis=1)


def portions_of(number_of, total, reach, skew, full):
    weights = [(1 << 20) // math.isqrt(grade ** skew) + 1 for grade in range(1, number_of + 1)]
    largest = reach if full else min(reach, max(-(-total // number_of), total * weights[0] // sum(weights)))
    least = 1 if total - largest >= number_of - 1 else 0
    counts, spare = [largest] + [least] * (number_of - 1), total - largest - least * (number_of - 1)
    while spare > 0:
        candidates = [i for i in range(1, number_of) if counts[i] < largest] or [i for i in range(1, number_of) if counts[i] < reach]
        mass, budget = sum([weights[i] for i in candidates]), spare
        for i in candidates:
            addition = min(reach - counts[i], max(1, budget * weights[i] // mass), spare)
            counts[i] = counts[i] + addition
            spare = spare - addition
    return np.array(counts)


def gaussian(own_key, shape, deviation, limit, cuts=(), kind=jnp.bfloat16):
    result = deviation * jax.random.normal(own_key, shape, jnp.float32)
    if cuts:
        result = result * steps_of(own_key, shape, cuts, -0.22, 0.18)
    return jnp.clip(result, -limit, limit).astype(kind)


def setup_inputs(seed: int = 0) -> dict:
    key_list = jax.random.split(jax.random.key(seed), 8)
    tile_image = gaussian(key_list[0], (N_VISIT, ROWS, TILE, TILE), 0.2, 1.1953125, ((0, 4), (1, 8)))
    tile_variance = jnp.clip(jnp.exp(math.log(10.0) - 4.609084 * jax.random.uniform(key_list[1], (N_VISIT, ROWS, TILE, TILE), jnp.float32) ** steps_of(key_list[1], (N_VISIT, ROWS, TILE, TILE), ((0, 4), (1, 8)), -0.2, 0.2)), 0.099609375, 10.0).astype(jnp.bfloat16)
    match_coeffs = draw_match_coeffs(jax.random.fold_in(key_list[7], 71), 0)
    tile_patch_keys = jax.random.split(jax.random.fold_in(key_list[3], 1), N_VISIT * ROWS // TILES_DEV)
    tile_patch_turns = jax.random.permutation(jax.random.fold_in(key_list[3], 3), N_VISIT * ROWS // TILES_DEV)
    tile_patch = jax.vmap(lambda own, number: deal_out(jax.random.fold_in(key_list[3], 2), own, number, TILES_DEV, N_SKY, 1, CAP, 2))(tile_patch_keys, tile_patch_turns).reshape((N_VISIT, ROWS, 1))
    tile_offset = set_ends(jax.random.randint(key_list[4], (N_VISIT, ROWS), 0, GRID * GRID), jax.random.fold_in(key_list[4], 1), 0, (GRID * GRID) - 1).astype(jnp.int32)
    row_taps = gaussian(key_list[5], (BASIS, TAPS), 0.2, 1.1953125)
    col_taps = gaussian(key_list[6], (BASIS, TAPS), 0.2, 1.1953125)
    return dict(tile_image=tile_image, tile_variance=tile_variance, match_coeffs=match_coeffs, tile_patch=tile_patch, tile_offset=tile_offset, row_taps=row_taps, col_taps=col_taps)


weight_floor = 0.5


def band_table(taps):
    rows_index = jnp.arange(TILE)[:, None]
    cols_index = jnp.arange(TILE)[None, :]
    offset = rows_index - cols_index + (TAPS - 1) // 2
    inside = (offset >= 0) & (offset < TAPS)
    picked = taps[:, jnp.clip(offset, 0, TAPS - 1)]
    return jnp.where(inside[None], picked, jnp.zeros_like(picked))


def tile_match(images, coeffs, row_side, col_side):
    count = images.shape[0]
    first = jnp.dot(images.reshape(count * TILE, TILE), row_side, preferred_element_type=jnp.float32)
    first = first.reshape(count, TILE, BASIS, TILE)
    scaled = (first * coeffs.astype(jnp.float32)[:, None, :, None]).astype(jnp.bfloat16)
    scaled = scaled.reshape(count, TILE * BASIS, TILE)
    return jnp.einsum("ia,naz->niz", col_side.astype(jnp.float32), scaled.astype(jnp.float32),
                      precision=lax.Precision.HIGHEST)


def reference(tile_image, tile_variance, match_coeffs, tile_patch, tile_offset, row_taps, col_taps):
    band_row = band_table(row_taps)
    band_col = band_table(col_taps)
    row_side = band_row.transpose(1, 0, 2).reshape(TILE, BASIS * TILE)
    col_side = band_col.transpose(2, 1, 0).reshape(TILE, TILE * BASIS)
    blocks = N_VISIT * N_SKY
    images = tile_image.reshape(blocks, TILES_DEV, TILE, TILE)
    variance = tile_variance.reshape(blocks, TILES_DEV, TILE, TILE)
    coeffs = match_coeffs.reshape(blocks, TILES_DEV, BASIS)
    patches = tile_patch.reshape(blocks, TILES_DEV).astype(jnp.int32)
    offsets = tile_offset.reshape(blocks, TILES_DEV).astype(jnp.int32)
    places = N_SKY * GRID * GRID
    start = (jnp.zeros((places, TILE, TILE), jnp.float32), jnp.zeros((places, TILE, TILE), jnp.float32),
             jnp.zeros((places,), jnp.float32), jnp.zeros((N_SKY, BASIS), jnp.float32),
             jnp.zeros((N_SKY,), jnp.float32))

    def absorb(carry, block):
        image_sum, variance_sum, weight_pos, psf_sum, weight_tot = carry
        block_images, block_var, block_coef, block_patch, block_offset = block
        matched = tile_match(block_images, block_coef, row_side, col_side)
        var_wide = block_var.astype(jnp.float32)
        weight = 1.0 / jnp.mean(var_wide, axis=(1, 2))
        target = block_patch * (GRID * GRID) + block_offset
        image_sum = image_sum.at[target].add(weight[:, None, None] * matched)
        variance_sum = variance_sum.at[target].add((weight * weight)[:, None, None] * var_wide)
        weight_pos = weight_pos.at[target].add(weight)
        psf_sum = psf_sum.at[block_patch].add(weight[:, None] * block_coef.astype(jnp.float32))
        weight_tot = weight_tot.at[block_patch].add(weight)
        return (image_sum, variance_sum, weight_pos, psf_sum, weight_tot), None

    final, unused = lax.scan(absorb, start, (images, variance, coeffs, patches, offsets))
    image_sum, variance_sum, weight_pos, psf_sum, weight_tot = final

    def layout(field):
        return field.reshape(N_SKY, GRID, GRID, TILE, TILE).transpose(0, 1, 3, 2, 4).reshape(N_SKY * PATCH, PATCH)

    weight_pix = jnp.broadcast_to(weight_pos.reshape(N_SKY, GRID, 1, GRID, 1), (N_SKY, GRID, TILE, GRID, TILE))
    denom = jnp.maximum(weight_pix.reshape(N_SKY * PATCH, PATCH), weight_floor)
    coadd_image = layout(image_sum) / denom
    coadd_variance = layout(variance_sum) / (denom * denom)
    share = psf_sum / weight_tot[:, None]
    coadd_psf = jnp.einsum("pk,ka,kb->pab", share, col_taps.astype(jnp.float32), row_taps.astype(jnp.float32),
                           precision=lax.Precision.HIGHEST)
    return coadd_image, coadd_variance, coadd_psf
```

```python
import jax
import jax.numpy as jnp
from jax import lax
from jax.experimental import pallas as pl
from jax.experimental.pallas import tpu as pltpu
from jax.sharding import PartitionSpec as P

GRID = 8
BASIS = 9
META = 16
EXTRA = 8


weight_floor = 0.5


def band_table(taps, tile):
    span = taps.shape[1]
    offset = jnp.arange(tile)[:, None] - jnp.arange(tile)[None, :] + (span - 1) // 2
    select = (offset[None, :, :] == jnp.arange(span)[:, None, None]).astype(jnp.float32)
    return jnp.einsum("kt,tij->kij", taps.astype(jnp.float32), select).astype(jnp.bfloat16)


def variance_kernel(place_ref, w2_ref, var_ref, extra_ref, out_ref):
    slots = var_ref.shape[0]
    tile = var_ref.shape[2]
    positions = out_ref.shape[0]
    out_ref[:, :tile, :] = jnp.zeros((positions, tile, tile), jnp.float32)
    out_ref[:, tile:, :] = extra_ref[...]

    def body(t, carry):
        q = place_ref[t]

        @pl.when(q >= 0)
        def _():
            out_ref[q, :tile, :] += w2_ref[t] * var_ref[t, :tile, :].astype(jnp.float32)

        return carry

    lax.fori_loop(0, slots, body, 0)


def image_kernel(place_ref, w_ref, coef_ref, img_ref, row_ref, col_ref, out_ref):
    slots = img_ref.shape[0]
    tile = img_ref.shape[2]
    out_ref[...] = jnp.zeros(out_ref.shape, jnp.float32)

    def body(t, carry):
        q = place_ref[t]

        @pl.when(q >= 0)
        def _():
            first = jnp.dot(img_ref[t], row_ref[...], preferred_element_type=jnp.float32)
            scaled = jnp.concatenate(
                [
                    (first[:, k * tile:(k + 1) * tile] * coef_ref[t * BASIS + k]).astype(jnp.bfloat16)
                    for k in range(BASIS)
                ],
                axis=0,
            )
            matched = jnp.dot(col_ref[...], scaled, preferred_element_type=jnp.float32)
            out_ref[q] += w_ref[t] * matched

        return carry

    lax.fori_loop(0, slots, body, 0)


def smem():
    return pl.BlockSpec(memory_space=pltpu.SMEM)


def vmem():
    return pl.BlockSpec(memory_space=pltpu.VMEM)


def variance_field(place, w2, var_meta, extra):
    positions, extra_rows, tile = extra.shape
    return pl.pallas_call(
        variance_kernel,
        out_shape=jax.ShapeDtypeStruct((positions, tile + extra_rows, tile), jnp.float32),
        in_specs=[smem(), smem(), vmem(), vmem()],
        out_specs=vmem(),
    )(place, w2, var_meta, extra)


def image_field(place, w, coef, images, row_side, col_side, positions):
    tile = images.shape[2]
    return pl.pallas_call(
        image_kernel,
        out_shape=jax.ShapeDtypeStruct((positions, tile, tile), jnp.float32),
        in_specs=[smem(), smem(), smem(), vmem(), vmem(), vmem()],
        out_specs=vmem(),
    )(place, w, coef, images, row_side, col_side)


def shards(tile_image, tile_variance, match_coeffs, tile_patch, tile_offset, row_taps, col_taps):
    n_sky = lax.axis_size("sky")
    n_visit = lax.axis_size("visit")
    images = tile_image[0]
    variance = tile_variance[0]
    coeffs = match_coeffs[0]
    count = images.shape[0]
    tile = images.shape[1]
    held_most = max(2, 2 * count // n_sky)
    positions = GRID * GRID
    dest = tile_patch[0, :, 0]
    offsets = tile_offset[0]
    band_row = band_table(row_taps, tile)
    band_col = band_table(col_taps, tile)
    row_side = band_row.transpose(1, 0, 2).reshape(tile, BASIS * tile)
    col_side = band_col.transpose(2, 0, 1).reshape(tile, BASIS * tile)
    order = jnp.arange(count)
    earlier = (dest[:, None] == dest[None, :]) & (order[None, :] < order[:, None])
    rank = jnp.sum(earlier.astype(jnp.int32), axis=1)
    slot = dest * held_most + rank
    slots_all = n_sky * held_most
    pick = (jnp.arange(slots_all)[:, None] == slot[None, :]).astype(jnp.bfloat16)
    column_major = (offsets % GRID) * GRID + offsets // GRID
    meta_row = jnp.concatenate(
        [
            coeffs.astype(jnp.float32),
            (column_major + 1).astype(jnp.float32)[:, None],
            jnp.zeros((count, tile - BASIS - 1), jnp.float32),
        ],
        axis=1,
    )
    meta = jnp.concatenate(
        [meta_row[:, None, :], jnp.zeros((count, META - 1, tile), jnp.float32)], axis=1
    ).astype(jnp.bfloat16)
    var_meta = jnp.concatenate([variance, meta], axis=1)
    send_vm = jnp.dot(
        pick, var_meta.reshape(count, (tile + META) * tile), preferred_element_type=jnp.float32
    )
    send_vm = send_vm.astype(jnp.bfloat16).reshape(n_sky, held_most, tile + META, tile)
    send_image = jnp.dot(
        pick, images.reshape(count, tile * tile), preferred_element_type=jnp.float32
    )
    send_image = send_image.astype(jnp.bfloat16).reshape(n_sky, held_most, tile, tile)

    part_vm = lax.all_to_all(send_vm, "sky", split_axis=0, concat_axis=0, tiled=True)
    part_vm = part_vm.reshape(slots_all, tile + META, tile)
    got_meta = part_vm[:, tile, :].astype(jnp.float32)
    got_coef = got_meta[:, :BASIS]
    place = got_meta[:, BASIS].astype(jnp.int32) - 1
    valid = place >= 0
    mean_var = jnp.mean(part_vm[:, :tile, :].astype(jnp.float32), axis=(1, 2))
    weight = jnp.where(valid, 1.0 / jnp.where(valid, mean_var, 1.0), 0.0)
    psf_part = jnp.sum(weight[:, None] * got_coef, axis=0)
    weight_part = jnp.sum(weight)
    weight_pos = jnp.sum(
        jnp.where(jnp.arange(positions)[:, None] == place[None, :], weight[None, :], 0.0), axis=1
    )
    psf_row = jnp.concatenate(
        [psf_part, weight_part[None], jnp.zeros((tile - BASIS - 1,), jnp.float32)]
    )
    extra = jnp.concatenate(
        [
            jnp.broadcast_to(weight_pos[:, None, None], (positions, 1, tile)),
            jnp.broadcast_to(psf_row[None, None, :], (positions, 1, tile)),
            jnp.zeros((positions, EXTRA - 2, tile), jnp.float32),
        ],
        axis=1,
    )
    var_pos = variance_field(place, weight * weight, part_vm, extra)
    var_share = lax.psum_scatter(
        var_pos.reshape(GRID, GRID, tile + EXTRA, tile), "visit", scatter_dimension=0, tiled=True
    )

    part_image = lax.all_to_all(send_image, "sky", split_axis=0, concat_axis=0, tiled=True)
    part_image = part_image.reshape(slots_all, tile, tile)
    coef_flat = got_coef.reshape(slots_all * BASIS)
    image_pos = image_field(place, weight, coef_flat, part_image, row_side, col_side, positions)
    image_share = lax.psum_scatter(
        image_pos.reshape(GRID, GRID, tile, tile), "visit", scatter_dimension=0, tiled=True
    )

    per_dev = GRID // n_visit
    denom = jnp.maximum(var_share[:, :, tile, 0], weight_floor)[:, :, None, None]
    coadd_image = image_share / denom
    coadd_variance = var_share[:, :, :tile, :] / (denom * denom)

    def layout(field):
        return field.transpose(1, 2, 0, 3).reshape(GRID * tile, per_dev * tile)

    psf_total = var_share[0, 0, tile + 1, :BASIS]
    weight_total = var_share[0, 0, tile + 1, BASIS]
    share = psf_total / weight_total
    high = lax.Precision.HIGHEST
    coadd_psf = jnp.einsum(
        "k,ka,kb->ab",
        share,
        col_taps.astype(jnp.float32),
        row_taps.astype(jnp.float32),
        precision=high,
    )[None]
    return (layout(coadd_image), layout(coadd_variance), coadd_psf)


def solution(mesh):
    return jax.shard_map(
        shards,
        mesh=mesh,
        in_specs=(
            P("visit", "sky", None, None),
            P("visit", "sky", None, None),
            P("visit", "sky", None),
            P("visit", "sky", None),
            P("visit", "sky"),
            P(),
            P(),
        ),
        out_specs=(P("sky", "visit"), P("sky", "visit"), P("sky", None, None)),
        check_vma=False,
    )
```

```python
import jax
import jax.numpy as jnp
from jax import lax
from jax.experimental import pallas as pl
from jax.experimental.pallas import tpu as pltpu
from jax.sharding import PartitionSpec as P

GRID = 8
BASIS = 9
META = 16
EXTRA = 8


weight_floor = 0.5


def band_table(taps, tile):
    span = taps.shape[1]
    offset = jnp.arange(tile)[:, None] - jnp.arange(tile)[None, :] + (span - 1) // 2
    select = (offset[None, :, :] == jnp.arange(span)[:, None, None]).astype(jnp.float32)
    return jnp.einsum("kt,tij->kij", taps.astype(jnp.float32), select).astype(jnp.bfloat16)


def place_tile(out_ref, row, group, sub, contrib):
    tile = contrib.shape[0]
    per_dev = out_ref.shape[2] // tile
    start = pl.multiple_of(row * tile, tile)
    for c in range(per_dev):

        @pl.when(sub == c)
        def _():
            out_ref[group, pl.ds(start, tile), c * tile:(c + 1) * tile] += contrib


def variance_kernel(row_ref, group_ref, sub_ref, w2_ref, var_ref, out_ref):
    slots = var_ref.shape[0]
    out_ref[...] = jnp.zeros(out_ref.shape, jnp.float32)

    def body(t, carry):
        row = row_ref[t]

        @pl.when(row >= 0)
        def _():
            contrib = w2_ref[t] * var_ref[t].astype(jnp.float32)
            place_tile(out_ref, row, group_ref[t], sub_ref[t], contrib)

        return carry

    lax.fori_loop(0, slots, body, 0)


def image_kernel(row_ref, group_ref, sub_ref, w_ref, coef_ref, img_ref, row_side_ref, col_side_ref,
                 extra_ref, out_ref):
    slots = img_ref.shape[0]
    tile = img_ref.shape[2]
    body_rows = out_ref.shape[1] - extra_ref.shape[1]
    out_ref[:, :body_rows, :] = jnp.zeros((out_ref.shape[0], body_rows, out_ref.shape[2]), jnp.float32)
    out_ref[:, body_rows:, :] = extra_ref[...]

    def body(t, carry):
        row = row_ref[t]

        @pl.when(row >= 0)
        def _():
            first = jnp.dot(img_ref[t, :tile, :], row_side_ref[...], preferred_element_type=jnp.float32)
            scaled = jnp.concatenate(
                [
                    (first[:, k * tile:(k + 1) * tile] * coef_ref[t * BASIS + k]).astype(jnp.bfloat16)
                    for k in range(BASIS)
                ],
                axis=0,
            )
            matched = jnp.dot(col_side_ref[...], scaled, preferred_element_type=jnp.float32)
            place_tile(out_ref, row, group_ref[t], sub_ref[t], w_ref[t] * matched)

        return carry

    lax.fori_loop(0, slots, body, 0)


def smem():
    return pl.BlockSpec(memory_space=pltpu.SMEM)


def vmem():
    return pl.BlockSpec(memory_space=pltpu.VMEM)


def variance_field(where, w2, var, field_shape):
    return pl.pallas_call(
        variance_kernel,
        out_shape=jax.ShapeDtypeStruct(field_shape, jnp.float32),
        in_specs=[smem(), smem(), smem(), smem(), vmem()],
        out_specs=vmem(),
    )(*where, w2, var)


def image_field(where, w, coef, images, row_side, col_side, extra, field_shape):
    return pl.pallas_call(
        image_kernel,
        out_shape=jax.ShapeDtypeStruct(field_shape, jnp.float32),
        in_specs=[smem(), smem(), smem(), smem(), smem(), vmem(), vmem(), vmem(), vmem()],
        out_specs=vmem(),
        cost_estimate=pl.CostEstimate(
            flops=4 * images.shape[0] * images.shape[2] ** 3 * BASIS,
            transcendentals=0,
            bytes_accessed=images.size * 2 + 4 * (field_shape[0] * field_shape[1] * field_shape[2]),
        ),
    )(*where, w, coef, images, row_side, col_side, extra)


def split_exact(value):
    high = value.astype(jnp.bfloat16)
    rest = value - high.astype(jnp.float32)
    middle = rest.astype(jnp.bfloat16)
    low = (rest - middle.astype(jnp.float32)).astype(jnp.bfloat16)
    return high, middle, low


def shards(tile_image, tile_variance, match_coeffs, tile_patch, tile_offset, row_taps, col_taps):
    n_sky = lax.axis_size("sky")
    n_visit = lax.axis_size("visit")
    images = tile_image[0]
    variance = tile_variance[0]
    coeffs = match_coeffs[0]
    count = images.shape[0]
    tile = images.shape[1]
    held_most = max(2, 2 * count // n_sky)
    positions = GRID * GRID
    per_dev = GRID // n_visit
    dest = tile_patch[0, :, 0]
    offsets = tile_offset[0]
    band_row = band_table(row_taps, tile)
    band_col = band_table(col_taps, tile)
    row_side = band_row.transpose(1, 0, 2).reshape(tile, BASIS * tile)
    col_side = band_col.transpose(2, 0, 1).reshape(tile, BASIS * tile)
    order = jnp.arange(count)
    earlier = (dest[:, None] == dest[None, :]) & (order[None, :] < order[:, None])
    rank = jnp.sum(earlier.astype(jnp.int32), axis=1)
    slot = dest * held_most + rank
    slots_all = n_sky * held_most
    pick = (jnp.arange(slots_all)[:, None] == slot[None, :]).astype(jnp.bfloat16)
    weight_src = 1.0 / jnp.mean(variance.astype(jnp.float32), axis=(1, 2))
    w_parts = split_exact(weight_src)
    meta_row = jnp.concatenate(
        [coeffs, (offsets + 1).astype(jnp.bfloat16)[:, None]]
        + [part[:, None] for part in w_parts]
        + [jnp.zeros((count, tile - BASIS - 4), jnp.bfloat16)],
        axis=1,
    )
    meta = jnp.concatenate(
        [meta_row[:, None, :], jnp.zeros((count, META - 1, tile), jnp.bfloat16)], axis=1
    )
    image_meta = jnp.concatenate([images, meta], axis=1)
    send_im = jnp.dot(
        pick, image_meta.reshape(count, (tile + META) * tile), preferred_element_type=jnp.float32
    )
    send_im = send_im.astype(jnp.bfloat16).reshape(n_sky, held_most, tile + META, tile)
    me = lax.axis_index("sky")
    shift = (dest - me) % n_sky
    pick_shift = (jnp.arange(slots_all)[:, None] == (shift * held_most + rank)[None, :])
    send_var = jnp.dot(
        pick_shift.astype(jnp.bfloat16), variance.reshape(count, tile * tile),
        preferred_element_type=jnp.float32,
    )
    send_var = send_var.astype(jnp.bfloat16).reshape(n_sky, held_most, tile, tile)

    part_im = lax.all_to_all(send_im, "sky", split_axis=0, concat_axis=0, tiled=True)
    part_im = part_im.reshape(slots_all, tile + META, tile)
    got_meta = part_im[:, tile, :].astype(jnp.float32)
    got_coef = got_meta[:, :BASIS]
    place = got_meta[:, BASIS].astype(jnp.int32) - 1
    valid = place >= 0
    weight = (got_meta[:, BASIS + 1] + got_meta[:, BASIS + 2]) + got_meta[:, BASIS + 3]
    weight = jnp.where(valid, weight, 0.0)
    tile_row = jnp.where(valid, place // GRID, -1)
    tile_col = place % GRID
    where = (tile_row, tile_col // per_dev, tile_col % per_dev)
    psf_part = jnp.sum(weight[:, None] * got_coef, axis=0)
    weight_part = jnp.sum(weight)
    weight_pos = jnp.sum(
        jnp.where(jnp.arange(positions)[:, None] == place[None, :], weight[None, :], 0.0), axis=1
    )
    pos_lanes = weight_pos.reshape(GRID, n_visit, per_dev).transpose(1, 2, 0)
    pos_lanes = jnp.concatenate(
        [pos_lanes, jnp.zeros((n_visit, per_dev, tile - GRID), jnp.float32)], axis=2
    ).reshape(n_visit, 1, per_dev * tile)
    psf_row = jnp.concatenate(
        [psf_part, weight_part[None], jnp.zeros((per_dev * tile - BASIS - 1,), jnp.float32)]
    )
    extra = jnp.concatenate(
        [
            pos_lanes,
            jnp.broadcast_to(psf_row[None, None, :], (n_visit, 1, per_dev * tile)),
            jnp.zeros((n_visit, EXTRA - 2, per_dev * tile), jnp.float32),
        ],
        axis=1,
    )
    image_pos = image_field(
        where, weight, got_coef.reshape(slots_all * BASIS), part_im, row_side, col_side, extra,
        (n_visit, GRID * tile + EXTRA, per_dev * tile),
    )
    image_share = lax.psum_scatter(image_pos, "visit", scatter_dimension=0, tiled=True)[0]

    got_var = [send_var[0]]
    for step in range(1, n_sky):
        pairs = [(src, (src + step) % n_sky) for src in range(n_sky)]
        got_var.append(lax.ppermute(send_var[step], "sky", perm=pairs))
    part_var = jnp.stack(got_var).reshape(slots_all, tile, tile)
    source = (me - jnp.arange(n_sky)) % n_sky

    def by_shift(values):
        return jnp.take(values.reshape(n_sky, held_most), source, axis=0).reshape(slots_all)

    var_where = tuple(by_shift(values) for values in where)
    var_pos = variance_field(
        var_where, by_shift(weight * weight), part_var, (n_visit, GRID * tile, per_dev * tile)
    )
    var_share = lax.psum_scatter(var_pos, "visit", scatter_dimension=0, tiled=True)[0]

    body_rows = GRID * tile
    pos_weight = image_share[body_rows, :].reshape(per_dev, tile)[:, :GRID]
    denom = jnp.maximum(pos_weight, weight_floor).T
    denom = jnp.broadcast_to(denom[:, None, :, None], (GRID, tile, per_dev, tile))
    denom = denom.reshape(body_rows, per_dev * tile)
    coadd_image = image_share[:body_rows, :] / denom
    coadd_variance = var_share / (denom * denom)

    psf_total = image_share[body_rows + 1, :BASIS]
    weight_total = image_share[body_rows + 1, BASIS]
    share = psf_total / weight_total
    high = lax.Precision.HIGHEST
    coadd_psf = jnp.einsum(
        "k,ka,kb->ab",
        share,
        col_taps.astype(jnp.float32),
        row_taps.astype(jnp.float32),
        precision=high,
    )[None]
    return (coadd_image, coadd_variance, coadd_psf)


def solution(mesh):
    return jax.shard_map(
        shards,
        mesh=mesh,
        in_specs=(
            P("visit", "sky", None, None),
            P("visit", "sky", None, None),
            P("visit", "sky", None),
            P("visit", "sky", None),
            P("visit", "sky"),
            P(),
            P(),
        ),
        out_specs=(P("sky", "visit"), P("sky", "visit"), P("sky", None, None)),
        check_vma=False,
    )
```

```python
import jax
import jax.numpy as jnp
from jax import lax
from jax.experimental import pallas as pl
from jax.experimental.pallas import tpu as pltpu
from jax.sharding import PartitionSpec as P

GRID = 8
BASIS = 9
META = 16
EXTRA = 8


weight_floor = 0.5


def band_table(taps, tile):
    span = taps.shape[1]
    offset = jnp.arange(tile)[:, None] - jnp.arange(tile)[None, :] + (span - 1) // 2
    select = (offset[None, :, :] == jnp.arange(span)[:, None, None]).astype(jnp.float32)
    return jnp.einsum("kt,tij->kij", taps.astype(jnp.float32), select).astype(jnp.bfloat16)


def place_tile(out_ref, row, group, sub, contrib):
    tile = contrib.shape[0]
    per_dev = out_ref.shape[2] // tile
    start = pl.multiple_of(row * tile, tile)
    for c in range(per_dev):

        @pl.when(sub == c)
        def _():
            out_ref[group, pl.ds(start, tile), c * tile:(c + 1) * tile] += contrib


def variance_kernel(row_ref, group_ref, sub_ref, w2_ref, var_ref, out_ref):
    slots = var_ref.shape[0]
    out_ref[...] = jnp.zeros(out_ref.shape, jnp.float32)

    def body(t, carry):
        row = row_ref[t]

        @pl.when(row >= 0)
        def _():
            contrib = w2_ref[t] * var_ref[t].astype(jnp.float32)
            place_tile(out_ref, row, group_ref[t], sub_ref[t], contrib)

        return carry

    lax.fori_loop(0, slots, body, 0)


def image_kernel(row_ref, group_ref, sub_ref, w_ref, coef_ref, img_ref, row_side_ref, col_side_ref,
                 extra_ref, out_ref):
    slots = img_ref.shape[0]
    tile = img_ref.shape[2]
    body_rows = out_ref.shape[1] - extra_ref.shape[1]
    out_ref[:, :body_rows, :] = jnp.zeros((out_ref.shape[0], body_rows, out_ref.shape[2]), jnp.float32)
    out_ref[:, body_rows:, :] = extra_ref[...]

    def body(t, carry):
        row = row_ref[t]

        @pl.when(row >= 0)
        def _():
            first = jnp.dot(img_ref[t, :tile, :], row_side_ref[...], preferred_element_type=jnp.float32)
            scaled = jnp.concatenate(
                [
                    (first[:, k * tile:(k + 1) * tile] * coef_ref[t * BASIS + k]).astype(jnp.bfloat16)
                    for k in range(BASIS)
                ],
                axis=0,
            )
            matched = jnp.dot(col_side_ref[...], scaled, preferred_element_type=jnp.float32)
            place_tile(out_ref, row, group_ref[t], sub_ref[t], w_ref[t] * matched)

        return carry

    lax.fori_loop(0, slots, body, 0)


def smem():
    return pl.BlockSpec(memory_space=pltpu.SMEM)


def vmem():
    return pl.BlockSpec(memory_space=pltpu.VMEM)


def variance_field(where, w2, var, field_shape):
    return pl.pallas_call(
        variance_kernel,
        out_shape=jax.ShapeDtypeStruct(field_shape, jnp.float32),
        in_specs=[smem(), smem(), smem(), smem(), vmem()],
        out_specs=vmem(),
    )(*where, w2, var)


def image_field(where, w, coef, images, row_side, col_side, extra, field_shape):
    return pl.pallas_call(
        image_kernel,
        out_shape=jax.ShapeDtypeStruct(field_shape, jnp.float32),
        in_specs=[smem(), smem(), smem(), smem(), smem(), vmem(), vmem(), vmem(), vmem()],
        out_specs=vmem(),
        cost_estimate=pl.CostEstimate(
            flops=4 * images.shape[0] * images.shape[2] ** 3 * BASIS,
            transcendentals=0,
            bytes_accessed=images.size * 2 + 4 * (field_shape[0] * field_shape[1] * field_shape[2]),
        ),
    )(*where, w, coef, images, row_side, col_side, extra)


def split_exact(value):
    high = lax.reduce_precision(value, exponent_bits=8, mantissa_bits=7)
    rest = value - high
    middle = lax.reduce_precision(rest, exponent_bits=8, mantissa_bits=7)
    low = rest - middle
    return tuple(part.astype(jnp.bfloat16) for part in (high, middle, low))


def bit_reverse(values, bits):
    out = jnp.zeros_like(values)
    for b in range(bits):
        out = out | (((values >> b) & 1) << (bits - 1 - b))
    return out


def reduce_scatter_visit(field, n_visit):
    me = lax.axis_index("visit")
    bits = n_visit.bit_length() - 1
    for b in range(bits):
        halves = field.reshape(2, field.shape[0] // 2, *field.shape[1:])
        mine = (me >> b) & 1
        keep = jnp.where(mine == 0, halves[0], halves[1])
        send = jnp.where(mine == 0, halves[1], halves[0])
        pairs = [(i, i ^ (1 << b)) for i in range(n_visit)]
        field = keep + lax.ppermute(send, "visit", perm=pairs)
    return field[0]


def shards(tile_image, tile_variance, match_coeffs, tile_patch, tile_offset, row_taps, col_taps):
    n_sky = lax.axis_size("sky")
    n_visit = lax.axis_size("visit")
    images = tile_image[0]
    variance = tile_variance[0]
    coeffs = match_coeffs[0]
    count = images.shape[0]
    tile = images.shape[1]
    held_most = max(2, 2 * count // n_sky)
    positions = GRID * GRID
    per_dev = GRID // n_visit
    dest = tile_patch[0, :, 0]
    offsets = tile_offset[0]
    band_row = band_table(row_taps, tile)
    band_col = band_table(col_taps, tile)
    row_side = band_row.transpose(1, 0, 2).reshape(tile, BASIS * tile)
    col_side = band_col.transpose(2, 0, 1).reshape(tile, BASIS * tile)
    order = jnp.arange(count)
    earlier = (dest[:, None] == dest[None, :]) & (order[None, :] < order[:, None])
    rank = jnp.sum(earlier.astype(jnp.int32), axis=1)
    slot = dest * held_most + rank
    slots_all = n_sky * held_most
    pick = (jnp.arange(slots_all)[:, None] == slot[None, :]).astype(jnp.bfloat16)
    weight_src = 1.0 / jnp.mean(variance.astype(jnp.float32), axis=(1, 2))
    w_parts = split_exact(weight_src)
    meta_row = jnp.concatenate(
        [coeffs, (offsets + 1).astype(jnp.bfloat16)[:, None]]
        + [part[:, None] for part in w_parts]
        + [jnp.zeros((count, tile - BASIS - 4), jnp.bfloat16)],
        axis=1,
    )
    meta = jnp.concatenate(
        [meta_row[:, None, :], jnp.zeros((count, META - 1, tile), jnp.bfloat16)], axis=1
    )
    image_meta = jnp.concatenate([images, meta], axis=1)
    send_im = jnp.dot(
        pick, image_meta.reshape(count, (tile + META) * tile), preferred_element_type=jnp.float32
    )
    send_im = send_im.astype(jnp.bfloat16).reshape(n_sky, held_most, tile + META, tile)
    me = lax.axis_index("sky")
    shift = (dest - me) % n_sky
    pick_shift = (jnp.arange(slots_all)[:, None] == (shift * held_most + rank)[None, :])
    send_var = jnp.dot(
        pick_shift.astype(jnp.bfloat16), variance.reshape(count, tile * tile),
        preferred_element_type=jnp.float32,
    )
    send_var = send_var.astype(jnp.bfloat16).reshape(n_sky, held_most, tile, tile)

    part_im = lax.all_to_all(send_im, "sky", split_axis=0, concat_axis=0, tiled=True)
    part_im = part_im.reshape(slots_all, tile + META, tile)
    got_meta = part_im[:, tile, :].astype(jnp.float32)
    got_coef = got_meta[:, :BASIS]
    place = got_meta[:, BASIS].astype(jnp.int32) - 1
    valid = place >= 0
    weight = (got_meta[:, BASIS + 1] + got_meta[:, BASIS + 2]) + got_meta[:, BASIS + 3]
    weight = jnp.where(valid, weight, 0.0)
    tile_row = jnp.where(valid, place // GRID, -1)
    tile_col = place % GRID
    bits = n_visit.bit_length() - 1
    where = (tile_row, bit_reverse(tile_col // per_dev, bits), tile_col % per_dev)
    psf_part = jnp.sum(weight[:, None] * got_coef, axis=0)
    weight_part = jnp.sum(weight)
    weight_pos = jnp.sum(
        jnp.where(jnp.arange(positions)[:, None] == place[None, :], weight[None, :], 0.0), axis=1
    )
    pos_lanes = weight_pos.reshape(GRID, n_visit, per_dev).transpose(1, 2, 0)
    pos_lanes = jnp.take(pos_lanes, bit_reverse(jnp.arange(n_visit), bits), axis=0)
    pos_lanes = jnp.concatenate(
        [pos_lanes, jnp.zeros((n_visit, per_dev, tile - GRID), jnp.float32)], axis=2
    ).reshape(n_visit, 1, per_dev * tile)
    psf_row = jnp.concatenate(
        [psf_part, weight_part[None], jnp.zeros((per_dev * tile - BASIS - 1,), jnp.float32)]
    )
    extra = jnp.concatenate(
        [
            pos_lanes,
            jnp.broadcast_to(psf_row[None, None, :], (n_visit, 1, per_dev * tile)),
            jnp.zeros((n_visit, EXTRA - 2, per_dev * tile), jnp.float32),
        ],
        axis=1,
    )
    image_pos = image_field(
        where, weight, got_coef.reshape(slots_all * BASIS), part_im, row_side, col_side, extra,
        (n_visit, GRID * tile + EXTRA, per_dev * tile),
    )
    image_share = reduce_scatter_visit(image_pos, n_visit)

    got_var = [send_var[0]]
    for step in range(1, n_sky):
        pairs = [(src, (src + step) % n_sky) for src in range(n_sky)]
        got_var.append(lax.ppermute(send_var[step], "sky", perm=pairs))
    part_var = jnp.stack(got_var).reshape(slots_all, tile, tile)
    source = (me - jnp.arange(n_sky)) % n_sky

    def by_shift(values):
        return jnp.take(values.reshape(n_sky, held_most), source, axis=0).reshape(slots_all)

    var_where = tuple(by_shift(values) for values in where)
    var_pos = variance_field(
        var_where, by_shift(weight * weight), part_var, (n_visit, GRID * tile, per_dev * tile)
    )
    var_share = reduce_scatter_visit(var_pos, n_visit)

    body_rows = GRID * tile
    pos_weight = image_share[body_rows, :].reshape(per_dev, tile)[:, :GRID]
    denom = jnp.maximum(pos_weight, weight_floor).T
    denom = jnp.broadcast_to(denom[:, None, :, None], (GRID, tile, per_dev, tile))
    denom = denom.reshape(body_rows, per_dev * tile)
    coadd_image = image_share[:body_rows, :] / denom
    coadd_variance = var_share / (denom * denom)

    psf_total = image_share[body_rows + 1, :BASIS]
    weight_total = image_share[body_rows + 1, BASIS]
    share = psf_total / weight_total
    high = lax.Precision.HIGHEST
    coadd_psf = jnp.einsum(
        "k,ka,kb->ab",
        share,
        col_taps.astype(jnp.float32),
        row_taps.astype(jnp.float32),
        precision=high,
    )[None]
    return (coadd_image, coadd_variance, coadd_psf)


def solution(mesh):
    return jax.shard_map(
        shards,
        mesh=mesh,
        in_specs=(
            P("visit", "sky", None, None),
            P("visit", "sky", None, None),
            P("visit", "sky", None),
            P("visit", "sky", None),
            P("visit", "sky"),
            P(),
            P(),
        ),
        out_specs=(P("sky", "visit"), P("sky", "visit"), P("sky", None, None)),
        check_vma=False,
    )
```

```python
import jax
import jax.numpy as jnp
from jax import lax
from jax.experimental import pallas as pl
from jax.experimental.pallas import tpu as pltpu
from jax.sharding import PartitionSpec as P

GRID = 8
BASIS = 9
META = 16
EXTRA = 8


weight_floor = 0.5


def band_table(taps, tile):
    span = taps.shape[1]
    offset = jnp.arange(tile)[:, None] - jnp.arange(tile)[None, :] + (span - 1) // 2
    select = (offset[None, :, :] == jnp.arange(span)[:, None, None]).astype(jnp.float32)
    return jnp.einsum("kt,tij->kij", taps.astype(jnp.float32), select).astype(jnp.bfloat16)


def place_tile(out_ref, row, group, sub, contrib):
    tile = contrib.shape[0]
    per_dev = out_ref.shape[2] // tile
    start = pl.multiple_of(row * tile, tile)
    for c in range(per_dev):

        @pl.when(sub == c)
        def _():
            out_ref[group, pl.ds(start, tile), c * tile:(c + 1) * tile] += contrib


def variance_kernel(row_ref, group_ref, sub_ref, w2_ref, var_ref, out_ref):
    slots = var_ref.shape[0]
    out_ref[...] = jnp.zeros(out_ref.shape, jnp.float32)

    def body(t, carry):
        row = row_ref[t]

        @pl.when(row >= 0)
        def _():
            contrib = w2_ref[t] * var_ref[t].astype(jnp.float32)
            place_tile(out_ref, row, group_ref[t], sub_ref[t], contrib)

        return carry

    lax.fori_loop(0, slots, body, 0)


def image_kernel(row_ref, group_ref, sub_ref, w_ref, coef_ref, img_ref, row_side_ref, col_side_ref,
                 extra_ref, out_ref):
    slots = img_ref.shape[0]
    tile = img_ref.shape[2]
    body_rows = out_ref.shape[1] - extra_ref.shape[1]
    out_ref[:, :body_rows, :] = jnp.zeros((out_ref.shape[0], body_rows, out_ref.shape[2]), jnp.float32)
    out_ref[:, body_rows:, :] = extra_ref[...]

    def body(t, carry):
        row = row_ref[t]

        @pl.when(row >= 0)
        def _():
            first = jnp.dot(img_ref[t, :tile, :], row_side_ref[...], preferred_element_type=jnp.float32)
            scaled = jnp.concatenate(
                [
                    (first[:, k * tile:(k + 1) * tile] * coef_ref[t * BASIS + k]).astype(jnp.bfloat16)
                    for k in range(BASIS)
                ],
                axis=0,
            )
            matched = jnp.dot(col_side_ref[...], scaled, preferred_element_type=jnp.float32)
            place_tile(out_ref, row, group_ref[t], sub_ref[t], w_ref[t] * matched)

        return carry

    lax.fori_loop(0, slots, body, 0)


def smem():
    return pl.BlockSpec(memory_space=pltpu.SMEM)


def vmem():
    return pl.BlockSpec(memory_space=pltpu.VMEM)


def variance_field(where, w2, var, field_shape):
    return pl.pallas_call(
        variance_kernel,
        out_shape=jax.ShapeDtypeStruct(field_shape, jnp.float32),
        in_specs=[smem(), smem(), smem(), smem(), vmem()],
        out_specs=vmem(),
    )(*where, w2, var)


def image_field(where, w, coef, images, row_side, col_side, extra, field_shape):
    return pl.pallas_call(
        image_kernel,
        out_shape=jax.ShapeDtypeStruct(field_shape, jnp.float32),
        in_specs=[smem(), smem(), smem(), smem(), smem(), vmem(), vmem(), vmem(), vmem()],
        out_specs=vmem(),
        cost_estimate=pl.CostEstimate(
            flops=4 * images.shape[0] * images.shape[2] ** 3 * BASIS,
            transcendentals=0,
            bytes_accessed=images.size * 2 + 4 * (field_shape[0] * field_shape[1] * field_shape[2]),
        ),
    )(*where, w, coef, images, row_side, col_side, extra)


def split_exact(value):
    high = lax.reduce_precision(value, exponent_bits=8, mantissa_bits=7)
    rest = value - high
    middle = lax.reduce_precision(rest, exponent_bits=8, mantissa_bits=7)
    low = rest - middle
    return tuple(part.astype(jnp.bfloat16) for part in (high, middle, low))


def bit_reverse(values, bits):
    out = jnp.zeros_like(values)
    for b in range(bits):
        out = out | (((values >> b) & 1) << (bits - 1 - b))
    return out


def reduce_scatter_visit(field, n_visit):
    me = lax.axis_index("visit")
    bits = n_visit.bit_length() - 1
    for b in range(bits):
        halves = field.reshape(2, field.shape[0] // 2, *field.shape[1:])
        mine = (me >> b) & 1
        keep = jnp.where(mine == 0, halves[0], halves[1])
        send = jnp.where(mine == 0, halves[1], halves[0])
        pairs = [(i, i ^ (1 << b)) for i in range(n_visit)]
        field = keep + lax.ppermute(send, "visit", perm=pairs)
    return field[0]


def shards(tile_image, tile_variance, match_coeffs, tile_patch, tile_offset, row_taps, col_taps):
    n_sky = lax.axis_size("sky")
    n_visit = lax.axis_size("visit")
    images = tile_image[0]
    variance = tile_variance[0]
    coeffs = match_coeffs[0]
    count = images.shape[0]
    tile = images.shape[1]
    held_most = max(2, 2 * count // n_sky)
    positions = GRID * GRID
    per_dev = GRID // n_visit
    dest = tile_patch[0, :, 0]
    offsets = tile_offset[0]
    band_row = band_table(row_taps, tile)
    band_col = band_table(col_taps, tile)
    row_side = band_row.transpose(1, 0, 2).reshape(tile, BASIS * tile)
    col_side = band_col.transpose(2, 0, 1).reshape(tile, BASIS * tile)
    order = jnp.arange(count)
    earlier = (dest[:, None] == dest[None, :]) & (order[None, :] < order[:, None])
    rank = jnp.sum(earlier.astype(jnp.int32), axis=1)
    slot = dest * held_most + rank
    slots_all = n_sky * held_most
    pick = (jnp.arange(slots_all)[:, None] == slot[None, :]).astype(jnp.bfloat16)
    weight_src = 1.0 / jnp.mean(variance.astype(jnp.float32), axis=(1, 2))
    w_parts = split_exact(weight_src)
    meta_row = jnp.concatenate(
        [coeffs, (offsets + 1).astype(jnp.bfloat16)[:, None]]
        + [part[:, None] for part in w_parts]
        + [jnp.zeros((count, tile - BASIS - 4), jnp.bfloat16)],
        axis=1,
    )
    meta = jnp.concatenate(
        [meta_row[:, None, :], jnp.zeros((count, META - 1, tile), jnp.bfloat16)], axis=1
    )
    image_meta = jnp.concatenate([images, meta], axis=1)
    send_im = jnp.dot(
        pick, image_meta.reshape(count, (tile + META) * tile), preferred_element_type=jnp.float32
    )
    send_im = send_im.astype(jnp.bfloat16).reshape(n_sky, held_most, tile + META, tile)
    me = lax.axis_index("sky")
    shift = (dest - me) % n_sky
    pick_shift = (jnp.arange(slots_all)[:, None] == (shift * held_most + rank)[None, :])
    send_var = jnp.dot(
        pick_shift.astype(jnp.bfloat16), variance.reshape(count, tile * tile),
        preferred_element_type=jnp.float32,
    )
    send_var = send_var.astype(jnp.bfloat16).reshape(n_sky, held_most, tile, tile)

    part_im = lax.all_to_all(send_im, "sky", split_axis=0, concat_axis=0, tiled=True)
    part_im, send_var = lax.optimization_barrier((part_im, send_var))
    part_im = part_im.reshape(slots_all, tile + META, tile)
    got_meta = part_im[:, tile, :].astype(jnp.float32)
    got_coef = got_meta[:, :BASIS]
    place = got_meta[:, BASIS].astype(jnp.int32) - 1
    valid = place >= 0
    weight = (got_meta[:, BASIS + 1] + got_meta[:, BASIS + 2]) + got_meta[:, BASIS + 3]
    weight = jnp.where(valid, weight, 0.0)
    tile_row = jnp.where(valid, place // GRID, -1)
    tile_col = place % GRID
    bits = n_visit.bit_length() - 1
    where = (tile_row, bit_reverse(tile_col // per_dev, bits), tile_col % per_dev)
    psf_part = jnp.sum(weight[:, None] * got_coef, axis=0)
    weight_part = jnp.sum(weight)
    weight_pos = jnp.sum(
        jnp.where(jnp.arange(positions)[:, None] == place[None, :], weight[None, :], 0.0), axis=1
    )
    pos_lanes = weight_pos.reshape(GRID, n_visit, per_dev).transpose(1, 2, 0)
    pos_lanes = jnp.take(pos_lanes, bit_reverse(jnp.arange(n_visit), bits), axis=0)
    pos_lanes = jnp.concatenate(
        [pos_lanes, jnp.zeros((n_visit, per_dev, tile - GRID), jnp.float32)], axis=2
    ).reshape(n_visit, 1, per_dev * tile)
    psf_row = jnp.concatenate(
        [psf_part, weight_part[None], jnp.zeros((per_dev * tile - BASIS - 1,), jnp.float32)]
    )
    extra = jnp.concatenate(
        [
            pos_lanes,
            jnp.broadcast_to(psf_row[None, None, :], (n_visit, 1, per_dev * tile)),
            jnp.zeros((n_visit, EXTRA - 2, per_dev * tile), jnp.float32),
        ],
        axis=1,
    )
    image_pos = image_field(
        where, weight, got_coef.reshape(slots_all * BASIS), part_im, row_side, col_side, extra,
        (n_visit, GRID * tile + EXTRA, per_dev * tile),
    )
    image_share = reduce_scatter_visit(image_pos, n_visit)

    got_var = [send_var[0]]
    for step in range(1, n_sky):
        pairs = [(src, (src + step) % n_sky) for src in range(n_sky)]
        got_var.append(lax.ppermute(send_var[step], "sky", perm=pairs))
    part_var = jnp.stack(got_var).reshape(slots_all, tile, tile)
    source = (me - jnp.arange(n_sky)) % n_sky

    def by_shift(values):
        return jnp.take(values.reshape(n_sky, held_most), source, axis=0).reshape(slots_all)

    var_where = tuple(by_shift(values) for values in where)
    image_share, part_var = lax.optimization_barrier((image_share, part_var))
    var_pos = variance_field(
        var_where, by_shift(weight * weight), part_var, (n_visit, GRID * tile, per_dev * tile)
    )
    var_share = reduce_scatter_visit(var_pos, n_visit)

    body_rows = GRID * tile
    pos_weight = image_share[body_rows, :].reshape(per_dev, tile)[:, :GRID]
    denom = jnp.maximum(pos_weight, weight_floor).T
    denom = jnp.broadcast_to(denom[:, None, :, None], (GRID, tile, per_dev, tile))
    denom = denom.reshape(body_rows, per_dev * tile)
    coadd_image = image_share[:body_rows, :] / denom
    coadd_variance = var_share / (denom * denom)

    psf_total = image_share[body_rows + 1, :BASIS]
    weight_total = image_share[body_rows + 1, BASIS]
    share = psf_total / weight_total
    high = lax.Precision.HIGHEST
    coadd_psf = jnp.einsum(
        "k,ka,kb->ab",
        share,
        col_taps.astype(jnp.float32),
        row_taps.astype(jnp.float32),
        precision=high,
    )[None]
    return (coadd_image, coadd_variance, coadd_psf)


def solution(mesh):
    return jax.shard_map(
        shards,
        mesh=mesh,
        in_specs=(
            P("visit", "sky", None, None),
            P("visit", "sky", None, None),
            P("visit", "sky", None),
            P("visit", "sky", None),
            P("visit", "sky"),
            P(),
            P(),
        ),
        out_specs=(P("sky", "visit"), P("sky", "visit"), P("sky", None, None)),
        check_vma=False,
    )
```

```python
import jax
import jax.numpy as jnp
from jax import lax
from jax.experimental import pallas as pl
from jax.experimental.pallas import tpu as pltpu
from jax.sharding import PartitionSpec as P

GRID = 8
BASIS = 9
META = 16
EXTRA = 8


weight_floor = 0.5


def band_table(taps, tile):
    span = taps.shape[1]
    offset = jnp.arange(tile)[:, None] - jnp.arange(tile)[None, :] + (span - 1) // 2
    select = (offset[None, :, :] == jnp.arange(span)[:, None, None]).astype(jnp.float32)
    return jnp.einsum("kt,tij->kij", taps.astype(jnp.float32), select).astype(jnp.bfloat16)


def place_tile(out_ref, row, group, sub, contrib):
    tile = contrib.shape[0]
    per_dev = out_ref.shape[2] // tile
    start = pl.multiple_of(row * tile, tile)
    for c in range(per_dev):

        @pl.when(sub == c)
        def _():
            out_ref[group, pl.ds(start, tile), c * tile:(c + 1) * tile] += contrib


def variance_kernel(row_ref, group_ref, sub_ref, w2_ref, var_ref, extra_ref, out_ref):
    slots = var_ref.shape[0]
    tile = var_ref.shape[2]
    body_rows = out_ref.shape[1] - extra_ref.shape[1]
    out_ref[:, :body_rows, :] = jnp.zeros((out_ref.shape[0], body_rows, out_ref.shape[2]), jnp.float32)
    out_ref[:, body_rows:, :] = extra_ref[...]

    def body(t, carry):
        row = row_ref[t]

        @pl.when(row >= 0)
        def _():
            contrib = w2_ref[t] * var_ref[t, :tile, :].astype(jnp.float32)
            place_tile(out_ref, row, group_ref[t], sub_ref[t], contrib)

        return carry

    lax.fori_loop(0, slots, body, 0)


def image_kernel(row_ref, group_ref, sub_ref, w_ref, coef_ref, img_ref, row_side_ref, col_side_ref,
                 out_ref):
    slots = img_ref.shape[0]
    tile = img_ref.shape[2]
    out_ref[...] = jnp.zeros(out_ref.shape, jnp.float32)

    def body(t, carry):
        row = row_ref[t]

        @pl.when(row >= 0)
        def _():
            first = jnp.dot(img_ref[t], row_side_ref[...], preferred_element_type=jnp.float32)
            scaled = jnp.concatenate(
                [
                    (first[:, k * tile:(k + 1) * tile] * coef_ref[t * BASIS + k]).astype(jnp.bfloat16)
                    for k in range(BASIS)
                ],
                axis=0,
            )
            matched = jnp.dot(col_side_ref[...], scaled, preferred_element_type=jnp.float32)
            place_tile(out_ref, row, group_ref[t], sub_ref[t], w_ref[t] * matched)

        return carry

    lax.fori_loop(0, slots, body, 0)


def smem():
    return pl.BlockSpec(memory_space=pltpu.SMEM)


def vmem():
    return pl.BlockSpec(memory_space=pltpu.VMEM)


def variance_field(where, w2, var, extra, field_shape):
    return pl.pallas_call(
        variance_kernel,
        out_shape=jax.ShapeDtypeStruct(field_shape, jnp.float32),
        in_specs=[smem(), smem(), smem(), smem(), vmem(), vmem()],
        out_specs=vmem(),
    )(*where, w2, var, extra)


def image_field(where, w, coef, images, row_side, col_side, field_shape):
    return pl.pallas_call(
        image_kernel,
        out_shape=jax.ShapeDtypeStruct(field_shape, jnp.float32),
        in_specs=[smem(), smem(), smem(), smem(), smem(), vmem(), vmem(), vmem()],
        out_specs=vmem(),
        cost_estimate=pl.CostEstimate(
            flops=4 * images.shape[0] * images.shape[2] ** 3 * BASIS,
            transcendentals=0,
            bytes_accessed=images.size * 2 + 4 * (field_shape[0] * field_shape[1] * field_shape[2]),
        ),
    )(*where, w, coef, images, row_side, col_side)


def split_exact(value):
    high = lax.reduce_precision(value, exponent_bits=8, mantissa_bits=7)
    rest = value - high
    middle = lax.reduce_precision(rest, exponent_bits=8, mantissa_bits=7)
    low = rest - middle
    return tuple(part.astype(jnp.bfloat16) for part in (high, middle, low))


def bit_reverse(values, bits):
    out = jnp.zeros_like(values)
    for b in range(bits):
        out = out | (((values >> b) & 1) << (bits - 1 - b))
    return out


def reduce_scatter_visit(field, n_visit):
    me = lax.axis_index("visit")
    bits = n_visit.bit_length() - 1
    for b in range(bits):
        halves = field.reshape(2, field.shape[0] // 2, *field.shape[1:])
        mine = (me >> b) & 1
        keep = jnp.where(mine == 0, halves[0], halves[1])
        send = jnp.where(mine == 0, halves[1], halves[0])
        pairs = [(i, i ^ (1 << b)) for i in range(n_visit)]
        field = keep + lax.ppermute(send, "visit", perm=pairs)
    return field[0]


def shards(tile_image, tile_variance, match_coeffs, tile_patch, tile_offset, row_taps, col_taps):
    n_sky = lax.axis_size("sky")
    n_visit = lax.axis_size("visit")
    images = tile_image[0]
    variance = tile_variance[0]
    coeffs = match_coeffs[0]
    count = images.shape[0]
    tile = images.shape[1]
    held_most = max(2, 2 * count // n_sky)
    positions = GRID * GRID
    per_dev = GRID // n_visit
    dest = tile_patch[0, :, 0]
    offsets = tile_offset[0]
    band_row = band_table(row_taps, tile)
    band_col = band_table(col_taps, tile)
    row_side = band_row.transpose(1, 0, 2).reshape(tile, BASIS * tile)
    col_side = band_col.transpose(2, 0, 1).reshape(tile, BASIS * tile)
    order = jnp.arange(count)
    earlier = (dest[:, None] == dest[None, :]) & (order[None, :] < order[:, None])
    rank = jnp.sum(earlier.astype(jnp.int32), axis=1)
    slot = dest * held_most + rank
    slots_all = n_sky * held_most
    pick = (jnp.arange(slots_all)[:, None] == slot[None, :]).astype(jnp.bfloat16)
    me = lax.axis_index("sky")
    shift = (dest - me) % n_sky
    pick_shift = (jnp.arange(slots_all)[:, None] == (shift * held_most + rank)[None, :])
    weight_src = 1.0 / jnp.mean(variance.astype(jnp.float32), axis=(1, 2))
    w_parts = split_exact(weight_src)
    meta_row = jnp.concatenate(
        [coeffs, (offsets + 1).astype(jnp.bfloat16)[:, None]]
        + [part[:, None] for part in w_parts]
        + [jnp.zeros((count, tile - BASIS - 4), jnp.bfloat16)],
        axis=1,
    )
    meta = jnp.concatenate(
        [meta_row[:, None, :], jnp.zeros((count, META - 1, tile), jnp.bfloat16)], axis=1
    )
    var_meta = jnp.concatenate([variance, meta], axis=1)
    send_vm = jnp.dot(
        pick_shift.astype(jnp.bfloat16), var_meta.reshape(count, (tile + META) * tile),
        preferred_element_type=jnp.float32,
    )
    send_vm = send_vm.astype(jnp.bfloat16).reshape(n_sky, held_most, tile + META, tile)
    send_im = jnp.dot(
        pick, images.reshape(count, tile * tile), preferred_element_type=jnp.float32
    )
    send_im = send_im.astype(jnp.bfloat16).reshape(n_sky, held_most, tile, tile)

    got_vm = [send_vm[0]]
    for step in range(1, n_sky):
        pairs = [(src, (src + step) % n_sky) for src in range(n_sky)]
        got_vm.append(lax.ppermute(send_vm[step], "sky", perm=pairs))
    part_vm = jnp.stack(got_vm)
    part_vm, send_im = lax.optimization_barrier((part_vm, send_im))
    part_vm = part_vm.reshape(slots_all, tile + META, tile)
    got_meta = part_vm[:, tile, :].astype(jnp.float32)
    got_coef = got_meta[:, :BASIS]
    place = got_meta[:, BASIS].astype(jnp.int32) - 1
    valid = place >= 0
    weight = (got_meta[:, BASIS + 1] + got_meta[:, BASIS + 2]) + got_meta[:, BASIS + 3]
    weight = jnp.where(valid, weight, 0.0)
    tile_row = jnp.where(valid, place // GRID, -1)
    tile_col = place % GRID
    bits = n_visit.bit_length() - 1
    where = (tile_row, bit_reverse(tile_col // per_dev, bits), tile_col % per_dev)
    psf_part = jnp.sum(weight[:, None] * got_coef, axis=0)
    weight_part = jnp.sum(weight)
    weight_pos = jnp.sum(
        jnp.where(jnp.arange(positions)[:, None] == place[None, :], weight[None, :], 0.0), axis=1
    )
    pos_lanes = weight_pos.reshape(GRID, n_visit, per_dev).transpose(1, 2, 0)
    pos_lanes = jnp.take(pos_lanes, bit_reverse(jnp.arange(n_visit), bits), axis=0)
    pos_lanes = jnp.concatenate(
        [pos_lanes, jnp.zeros((n_visit, per_dev, tile - GRID), jnp.float32)], axis=2
    ).reshape(n_visit, 1, per_dev * tile)
    psf_row = jnp.concatenate(
        [psf_part, weight_part[None], jnp.zeros((per_dev * tile - BASIS - 1,), jnp.float32)]
    )
    extra = jnp.concatenate(
        [
            pos_lanes,
            jnp.broadcast_to(psf_row[None, None, :], (n_visit, 1, per_dev * tile)),
            jnp.zeros((n_visit, EXTRA - 2, per_dev * tile), jnp.float32),
        ],
        axis=1,
    )
    var_pos = variance_field(
        where, weight * weight, part_vm, extra, (n_visit, GRID * tile + EXTRA, per_dev * tile)
    )
    var_share = reduce_scatter_visit(var_pos, n_visit)

    part_im = lax.all_to_all(send_im, "sky", split_axis=0, concat_axis=0, tiled=True)
    var_share, part_im = lax.optimization_barrier((var_share, part_im))
    part_im = part_im.reshape(slots_all, tile, tile)
    source = (me - jnp.arange(n_sky)) % n_sky

    def by_source(values):
        return jnp.take(values.reshape(n_sky, held_most, -1), source, axis=0).reshape(slots_all, -1)

    im_where = tuple(by_source(values)[:, 0] for values in where)
    image_pos = image_field(
        im_where, by_source(weight)[:, 0], by_source(got_coef).reshape(slots_all * BASIS), part_im,
        row_side, col_side, (n_visit, GRID * tile, per_dev * tile),
    )
    image_share = reduce_scatter_visit(image_pos, n_visit)

    body_rows = GRID * tile
    pos_weight = var_share[body_rows, :].reshape(per_dev, tile)[:, :GRID]
    denom = jnp.maximum(pos_weight, weight_floor).T
    denom = jnp.broadcast_to(denom[:, None, :, None], (GRID, tile, per_dev, tile))
    denom = denom.reshape(body_rows, per_dev * tile)
    coadd_image = image_share / denom
    coadd_variance = var_share[:body_rows, :] / (denom * denom)

    psf_total = var_share[body_rows + 1, :BASIS]
    weight_total = var_share[body_rows + 1, BASIS]
    share = psf_total / weight_total
    high = lax.Precision.HIGHEST
    coadd_psf = jnp.einsum(
        "k,ka,kb->ab",
        share,
        col_taps.astype(jnp.float32),
        row_taps.astype(jnp.float32),
        precision=high,
    )[None]
    return (coadd_image, coadd_variance, coadd_psf)


def solution(mesh):
    return jax.shard_map(
        shards,
        mesh=mesh,
        in_specs=(
            P("visit", "sky", None, None),
            P("visit", "sky", None, None),
            P("visit", "sky", None),
            P("visit", "sky", None),
            P("visit", "sky"),
            P(),
            P(),
        ),
        out_specs=(P("sky", "visit"), P("sky", "visit"), P("sky", None, None)),
        check_vma=False,
    )
```

```python
import jax
import jax.numpy as jnp
from jax import lax
from jax.experimental import pallas as pl
from jax.experimental.pallas import tpu as pltpu
from jax.sharding import PartitionSpec as P

GRID = 8
BASIS = 9
META = 16
EXTRA = 8


weight_floor = 0.5


def band_table(taps, tile):
    span = taps.shape[1]
    offset = jnp.arange(tile)[:, None] - jnp.arange(tile)[None, :] + (span - 1) // 2
    select = (offset[None, :, :] == jnp.arange(span)[:, None, None]).astype(jnp.float32)
    return jnp.einsum("kt,tij->kij", taps.astype(jnp.float32), select).astype(jnp.bfloat16)


def place_tile(out_ref, row, group, sub, contrib):
    tile = contrib.shape[0]
    per_dev = out_ref.shape[2] // tile
    start = pl.multiple_of(row * tile, tile)
    for c in range(per_dev):

        @pl.when(sub == c)
        def _():
            out_ref[group, pl.ds(start, tile), c * tile:(c + 1) * tile] += contrib


def variance_kernel(row_ref, group_ref, sub_ref, w2_ref, var_ref, extra_ref, out_ref):
    slots = var_ref.shape[0]
    tile = var_ref.shape[2]
    body_rows = out_ref.shape[1] - extra_ref.shape[1]
    out_ref[:, :body_rows, :] = jnp.zeros((out_ref.shape[0], body_rows, out_ref.shape[2]), jnp.float32)
    out_ref[:, body_rows:, :] = extra_ref[...]

    def body(t, carry):
        row = row_ref[t]

        @pl.when(row >= 0)
        def _():
            contrib = w2_ref[t] * var_ref[t, :tile, :].astype(jnp.float32)
            place_tile(out_ref, row, group_ref[t], sub_ref[t], contrib)

        return carry

    lax.fori_loop(0, slots, body, 0)


def image_kernel(order_ref, count_ref, row_ref, group_ref, sub_ref, w_ref, coef_ref, img_ref,
                 row_side_ref, col_side_ref, out_ref):
    tile = img_ref.shape[2]
    out_ref[...] = jnp.zeros(out_ref.shape, jnp.float32)

    def body(p, carry):
        pair = (order_ref[2 * p], order_ref[2 * p + 1])
        both = jnp.concatenate([img_ref[pair[0]], img_ref[pair[1]]], axis=0)
        first = jnp.dot(both, row_side_ref[...], preferred_element_type=jnp.float32)
        blocks = []
        for k in range(BASIS):
            halves = [
                (first[h * tile:(h + 1) * tile, k * tile:(k + 1) * tile]
                 * coef_ref[pair[h] * BASIS + k]).astype(jnp.bfloat16)
                for h in range(2)
            ]
            blocks.append(jnp.concatenate(halves, axis=1))
        scaled = jnp.concatenate(blocks, axis=0)
        matched = jnp.dot(col_side_ref[...], scaled, preferred_element_type=jnp.float32)
        for h in range(2):
            t = pair[h]
            row = row_ref[t]

            @pl.when(row >= 0)
            def _():
                place_tile(out_ref, row, group_ref[t], sub_ref[t],
                           w_ref[t] * matched[:, h * tile:(h + 1) * tile])

        return carry

    lax.fori_loop(0, (count_ref[0] + 1) // 2, body, 0)


def smem():
    return pl.BlockSpec(memory_space=pltpu.SMEM)


def vmem():
    return pl.BlockSpec(memory_space=pltpu.VMEM)


def variance_field(where, w2, var, extra, field_shape):
    return pl.pallas_call(
        variance_kernel,
        out_shape=jax.ShapeDtypeStruct(field_shape, jnp.float32),
        in_specs=[smem(), smem(), smem(), smem(), vmem(), vmem()],
        out_specs=vmem(),
    )(*where, w2, var, extra)


def image_field(where, w, coef, images, row_side, col_side, field_shape):
    filled = where[0] >= 0
    order = jnp.argsort(jnp.logical_not(filled), stable=True).astype(jnp.int32)
    count = jnp.sum(filled.astype(jnp.int32))[None]
    return pl.pallas_call(
        image_kernel,
        out_shape=jax.ShapeDtypeStruct(field_shape, jnp.float32),
        in_specs=[smem()] * 7 + [vmem()] * 3,
        out_specs=vmem(),
        cost_estimate=pl.CostEstimate(
            flops=4 * images.shape[0] * images.shape[2] ** 3 * BASIS,
            transcendentals=0,
            bytes_accessed=images.size * 2 + 4 * (field_shape[0] * field_shape[1] * field_shape[2]),
        ),
    )(order, count, *where, w, coef, images, row_side, col_side)


def split_exact(value):
    high = lax.reduce_precision(value, exponent_bits=8, mantissa_bits=7)
    rest = value - high
    middle = lax.reduce_precision(rest, exponent_bits=8, mantissa_bits=7)
    low = rest - middle
    return tuple(part.astype(jnp.bfloat16) for part in (high, middle, low))


def bit_reverse(values, bits):
    out = jnp.zeros_like(values)
    for b in range(bits):
        out = out | (((values >> b) & 1) << (bits - 1 - b))
    return out


def reduce_scatter_visit(field, n_visit):
    me = lax.axis_index("visit")
    bits = n_visit.bit_length() - 1
    for b in range(bits):
        halves = field.reshape(2, field.shape[0] // 2, *field.shape[1:])
        mine = (me >> b) & 1
        keep = jnp.where(mine == 0, halves[0], halves[1])
        send = jnp.where(mine == 0, halves[1], halves[0])
        pairs = [(i, i ^ (1 << b)) for i in range(n_visit)]
        field = keep + lax.ppermute(send, "visit", perm=pairs)
    return field[0]


def shards(tile_image, tile_variance, match_coeffs, tile_patch, tile_offset, row_taps, col_taps):
    n_sky = lax.axis_size("sky")
    n_visit = lax.axis_size("visit")
    images = tile_image[0]
    variance = tile_variance[0]
    coeffs = match_coeffs[0]
    count = images.shape[0]
    tile = images.shape[1]
    held_most = max(2, 2 * count // n_sky)
    positions = GRID * GRID
    per_dev = GRID // n_visit
    dest = tile_patch[0, :, 0]
    offsets = tile_offset[0]
    band_row = band_table(row_taps, tile)
    band_col = band_table(col_taps, tile)
    row_side = band_row.transpose(1, 0, 2).reshape(tile, BASIS * tile)
    col_side = band_col.transpose(2, 0, 1).reshape(tile, BASIS * tile)
    order = jnp.arange(count)
    earlier = (dest[:, None] == dest[None, :]) & (order[None, :] < order[:, None])
    rank = jnp.sum(earlier.astype(jnp.int32), axis=1)
    slot = dest * held_most + rank
    slots_all = n_sky * held_most
    pick = (jnp.arange(slots_all)[:, None] == slot[None, :]).astype(jnp.bfloat16)
    me = lax.axis_index("sky")
    shift = (dest - me) % n_sky
    pick_shift = (jnp.arange(slots_all)[:, None] == (shift * held_most + rank)[None, :])
    weight_src = 1.0 / jnp.mean(variance.astype(jnp.float32), axis=(1, 2))
    w_parts = split_exact(weight_src)
    meta_row = jnp.concatenate(
        [coeffs, (offsets + 1).astype(jnp.bfloat16)[:, None]]
        + [part[:, None] for part in w_parts]
        + [jnp.zeros((count, tile - BASIS - 4), jnp.bfloat16)],
        axis=1,
    )
    meta = jnp.concatenate(
        [meta_row[:, None, :], jnp.zeros((count, META - 1, tile), jnp.bfloat16)], axis=1
    )
    var_meta = jnp.concatenate([variance, meta], axis=1)
    send_vm = jnp.dot(
        pick_shift.astype(jnp.bfloat16), var_meta.reshape(count, (tile + META) * tile),
        preferred_element_type=jnp.float32,
    )
    send_vm = send_vm.astype(jnp.bfloat16).reshape(n_sky, held_most, tile + META, tile)
    send_im = jnp.dot(
        pick, images.reshape(count, tile * tile), preferred_element_type=jnp.float32
    )
    send_im = send_im.astype(jnp.bfloat16).reshape(n_sky, held_most, tile, tile)

    got_vm = [send_vm[0]]
    for step in range(1, n_sky):
        pairs = [(src, (src + step) % n_sky) for src in range(n_sky)]
        got_vm.append(lax.ppermute(send_vm[step], "sky", perm=pairs))
    part_vm = jnp.stack(got_vm)
    part_vm, send_im = lax.optimization_barrier((part_vm, send_im))
    part_vm = part_vm.reshape(slots_all, tile + META, tile)
    got_meta = part_vm[:, tile, :].astype(jnp.float32)
    got_coef = got_meta[:, :BASIS]
    place = got_meta[:, BASIS].astype(jnp.int32) - 1
    valid = place >= 0
    weight = (got_meta[:, BASIS + 1] + got_meta[:, BASIS + 2]) + got_meta[:, BASIS + 3]
    weight = jnp.where(valid, weight, 0.0)
    tile_row = jnp.where(valid, place // GRID, -1)
    tile_col = place % GRID
    bits = n_visit.bit_length() - 1
    where = (tile_row, bit_reverse(tile_col // per_dev, bits), tile_col % per_dev)
    psf_part = jnp.sum(weight[:, None] * got_coef, axis=0)
    weight_part = jnp.sum(weight)
    weight_pos = jnp.sum(
        jnp.where(jnp.arange(positions)[:, None] == place[None, :], weight[None, :], 0.0), axis=1
    )
    pos_lanes = weight_pos.reshape(GRID, n_visit, per_dev).transpose(1, 2, 0)
    pos_lanes = jnp.take(pos_lanes, bit_reverse(jnp.arange(n_visit), bits), axis=0)
    pos_lanes = jnp.concatenate(
        [pos_lanes, jnp.zeros((n_visit, per_dev, tile - GRID), jnp.float32)], axis=2
    ).reshape(n_visit, 1, per_dev * tile)
    psf_row = jnp.concatenate(
        [psf_part, weight_part[None], jnp.zeros((per_dev * tile - BASIS - 1,), jnp.float32)]
    )
    extra = jnp.concatenate(
        [
            pos_lanes,
            jnp.broadcast_to(psf_row[None, None, :], (n_visit, 1, per_dev * tile)),
            jnp.zeros((n_visit, EXTRA - 2, per_dev * tile), jnp.float32),
        ],
        axis=1,
    )
    var_pos = variance_field(
        where, weight * weight, part_vm, extra, (n_visit, GRID * tile + EXTRA, per_dev * tile)
    )
    var_share = reduce_scatter_visit(var_pos, n_visit)

    part_im = lax.all_to_all(send_im, "sky", split_axis=0, concat_axis=0, tiled=True)
    var_share, part_im = lax.optimization_barrier((var_share, part_im))
    part_im = part_im.reshape(slots_all, tile, tile)
    source = (me - jnp.arange(n_sky)) % n_sky

    def by_source(values):
        return jnp.take(values.reshape(n_sky, held_most, -1), source, axis=0).reshape(slots_all, -1)

    im_where = tuple(by_source(values)[:, 0] for values in where)
    image_pos = image_field(
        im_where, by_source(weight)[:, 0], by_source(got_coef).reshape(slots_all * BASIS), part_im,
        row_side, col_side, (n_visit, GRID * tile, per_dev * tile),
    )
    image_share = reduce_scatter_visit(image_pos, n_visit)

    body_rows = GRID * tile
    pos_weight = var_share[body_rows, :].reshape(per_dev, tile)[:, :GRID]
    denom = jnp.maximum(pos_weight, weight_floor).T
    denom = jnp.broadcast_to(denom[:, None, :, None], (GRID, tile, per_dev, tile))
    denom = denom.reshape(body_rows, per_dev * tile)
    coadd_image = image_share / denom
    coadd_variance = var_share[:body_rows, :] / (denom * denom)

    psf_total = var_share[body_rows + 1, :BASIS]
    weight_total = var_share[body_rows + 1, BASIS]
    share = psf_total / weight_total
    high = lax.Precision.HIGHEST
    coadd_psf = jnp.einsum(
        "k,ka,kb->ab",
        share,
        col_taps.astype(jnp.float32),
        row_taps.astype(jnp.float32),
        precision=high,
    )[None]
    return (coadd_image, coadd_variance, coadd_psf)


def solution(mesh):
    return jax.shard_map(
        shards,
        mesh=mesh,
        in_specs=(
            P("visit", "sky", None, None),
            P("visit", "sky", None, None),
            P("visit", "sky", None),
            P("visit", "sky", None),
            P("visit", "sky"),
            P(),
            P(),
        ),
        out_specs=(P("sky", "visit"), P("sky", "visit"), P("sky", None, None)),
        check_vma=False,
    )
```

```python
import jax
import jax.numpy as jnp
from jax import lax
from jax.experimental import pallas as pl
from jax.experimental.pallas import tpu as pltpu
from jax.sharding import PartitionSpec as P

GRID = 8
BASIS = 9
META = 16
EXTRA = 8


weight_floor = 0.5


def band_table(taps, tile):
    span = taps.shape[1]
    offset = jnp.arange(tile)[:, None] - jnp.arange(tile)[None, :] + (span - 1) // 2
    select = (offset[None, :, :] == jnp.arange(span)[:, None, None]).astype(jnp.float32)
    return jnp.einsum("kt,tij->kij", taps.astype(jnp.float32), select).astype(jnp.bfloat16)


def place_tile(out_ref, row, group, sub, contrib):
    tile = contrib.shape[0]
    per_dev = out_ref.shape[2] // tile
    start = pl.multiple_of(row * tile, tile)
    for c in range(per_dev):

        @pl.when(sub == c)
        def _():
            out_ref[group, pl.ds(start, tile), c * tile:(c + 1) * tile] += contrib


def variance_kernel(row_ref, group_ref, sub_ref, w2_ref, *refs):
    chunks, extra_ref, out_ref = refs[:-2], refs[-2], refs[-1]
    held = chunks[0].shape[0]
    tile = chunks[0].shape[2]
    body_rows = out_ref.shape[1] - extra_ref.shape[1]
    out_ref[:, :body_rows, :] = jnp.zeros((out_ref.shape[0], body_rows, out_ref.shape[2]), jnp.float32)
    out_ref[:, body_rows:, :] = extra_ref[...]
    for d, chunk in enumerate(chunks):

        def body(r, carry):
            t = d * held + r
            row = row_ref[t]

            @pl.when(row >= 0)
            def _():
                contrib = w2_ref[t] * chunk[r, :tile, :].astype(jnp.float32)
                place_tile(out_ref, row, group_ref[t], sub_ref[t], contrib)

            return carry

        lax.fori_loop(0, held, body, 0)


def image_kernel(order_ref, count_ref, row_ref, group_ref, sub_ref, w_ref, coef_ref, img_ref,
                 row_side_ref, col_side_ref, out_ref):
    tile = img_ref.shape[2]
    out_ref[...] = jnp.zeros(out_ref.shape, jnp.float32)

    def body(p, carry):
        pair = (order_ref[2 * p], order_ref[2 * p + 1])
        both = jnp.concatenate([img_ref[pair[0]], img_ref[pair[1]]], axis=0)
        first = jnp.dot(both, row_side_ref[...], preferred_element_type=jnp.float32)
        blocks = []
        for k in range(BASIS):
            halves = [
                (first[h * tile:(h + 1) * tile, k * tile:(k + 1) * tile]
                 * coef_ref[pair[h] * BASIS + k]).astype(jnp.bfloat16)
                for h in range(2)
            ]
            blocks.append(jnp.concatenate(halves, axis=1))
        scaled = jnp.concatenate(blocks, axis=0)
        matched = jnp.dot(col_side_ref[...], scaled, preferred_element_type=jnp.float32)
        for h in range(2):
            t = pair[h]
            row = row_ref[t]

            @pl.when(row >= 0)
            def _():
                place_tile(out_ref, row, group_ref[t], sub_ref[t],
                           w_ref[t] * matched[:, h * tile:(h + 1) * tile])

        return carry

    lax.fori_loop(0, (count_ref[0] + 1) // 2, body, 0)


def smem():
    return pl.BlockSpec(memory_space=pltpu.SMEM)


def vmem():
    return pl.BlockSpec(memory_space=pltpu.VMEM)


def variance_field(where, w2, chunks, extra, field_shape):
    return pl.pallas_call(
        variance_kernel,
        out_shape=jax.ShapeDtypeStruct(field_shape, jnp.float32),
        in_specs=[smem()] * 4 + [vmem()] * (len(chunks) + 1),
        out_specs=vmem(),
    )(*where, w2, *chunks, extra)


def image_field(where, w, coef, images, row_side, col_side, field_shape):
    filled = where[0] >= 0
    order = jnp.argsort(jnp.logical_not(filled), stable=True).astype(jnp.int32)
    count = jnp.sum(filled.astype(jnp.int32))[None]
    return pl.pallas_call(
        image_kernel,
        out_shape=jax.ShapeDtypeStruct(field_shape, jnp.float32),
        in_specs=[smem()] * 7 + [vmem()] * 3,
        out_specs=vmem(),
        cost_estimate=pl.CostEstimate(
            flops=4 * images.shape[0] * images.shape[2] ** 3 * BASIS,
            transcendentals=0,
            bytes_accessed=images.size * 2 + 4 * (field_shape[0] * field_shape[1] * field_shape[2]),
        ),
    )(order, count, *where, w, coef, images, row_side, col_side)


def split_exact(value):
    high = lax.reduce_precision(value, exponent_bits=8, mantissa_bits=7)
    rest = value - high
    middle = lax.reduce_precision(rest, exponent_bits=8, mantissa_bits=7)
    low = rest - middle
    return tuple(part.astype(jnp.bfloat16) for part in (high, middle, low))


def bit_reverse(values, bits):
    out = jnp.zeros_like(values)
    for b in range(bits):
        out = out | (((values >> b) & 1) << (bits - 1 - b))
    return out


def reduce_scatter_visit(field, n_visit):
    bits = n_visit.bit_length() - 1
    for b in range(bits):
        half = field.shape[0] // 2
        pairs = [(i, i ^ (1 << b)) for i in range(n_visit)]
        field = field[:half] + lax.ppermute(field[half:], "visit", perm=pairs)
    return field[0]


def shards(tile_image, tile_variance, match_coeffs, tile_patch, tile_offset, row_taps, col_taps):
    n_sky = lax.axis_size("sky")
    n_visit = lax.axis_size("visit")
    images = tile_image[0]
    variance = tile_variance[0]
    coeffs = match_coeffs[0]
    count = images.shape[0]
    tile = images.shape[1]
    held_most = max(2, 2 * count // n_sky)
    positions = GRID * GRID
    per_dev = GRID // n_visit
    dest = tile_patch[0, :, 0]
    offsets = tile_offset[0]
    band_row = band_table(row_taps, tile)
    band_col = band_table(col_taps, tile)
    row_side = band_row.transpose(1, 0, 2).reshape(tile, BASIS * tile)
    col_side = band_col.transpose(2, 0, 1).reshape(tile, BASIS * tile)
    order = jnp.arange(count)
    earlier = (dest[:, None] == dest[None, :]) & (order[None, :] < order[:, None])
    rank = jnp.sum(earlier.astype(jnp.int32), axis=1)
    slot = dest * held_most + rank
    slots_all = n_sky * held_most
    pick = (jnp.arange(slots_all)[:, None] == slot[None, :]).astype(jnp.bfloat16)
    me = lax.axis_index("sky")
    shift = (dest - me) % n_sky
    pick_shift = (jnp.arange(slots_all)[:, None] == (shift * held_most + rank)[None, :])
    weight_src = 1.0 / jnp.mean(variance.astype(jnp.float32), axis=(1, 2))
    w_parts = split_exact(weight_src)
    meta_row = jnp.concatenate(
        [coeffs, (offsets + 1).astype(jnp.bfloat16)[:, None]]
        + [part[:, None] for part in w_parts]
        + [jnp.zeros((count, tile - BASIS - 4), jnp.bfloat16)],
        axis=1,
    )
    meta = jnp.concatenate(
        [meta_row[:, None, :], jnp.zeros((count, META - 1, tile), jnp.bfloat16)], axis=1
    )
    var_meta = jnp.concatenate([variance, meta], axis=1)
    send_vm = jnp.dot(
        pick_shift.astype(jnp.bfloat16), var_meta.reshape(count, (tile + META) * tile),
        preferred_element_type=jnp.float32,
    )
    send_vm = send_vm.astype(jnp.bfloat16).reshape(n_sky, held_most, tile + META, tile)
    send_im = jnp.dot(
        pick, images.reshape(count, tile * tile), preferred_element_type=jnp.float32
    )
    send_im = send_im.astype(jnp.bfloat16).reshape(n_sky, held_most, tile, tile)

    got_vm = [send_vm[0]]
    for step in range(1, n_sky):
        pairs = [(src, (src + step) % n_sky) for src in range(n_sky)]
        got_vm.append(lax.ppermute(send_vm[step], "sky", perm=pairs))
    got_vm, send_im = lax.optimization_barrier((got_vm, send_im))
    got_meta = jnp.concatenate([chunk[:, tile, :] for chunk in got_vm]).astype(jnp.float32)
    got_coef = got_meta[:, :BASIS]
    place = got_meta[:, BASIS].astype(jnp.int32) - 1
    valid = place >= 0
    weight = (got_meta[:, BASIS + 1] + got_meta[:, BASIS + 2]) + got_meta[:, BASIS + 3]
    weight = jnp.where(valid, weight, 0.0)
    tile_row = jnp.where(valid, place // GRID, -1)
    tile_col = place % GRID
    bits = n_visit.bit_length() - 1
    me_visit = lax.axis_index("visit")
    where = (tile_row, bit_reverse((tile_col // per_dev) ^ me_visit, bits), tile_col % per_dev)
    psf_part = jnp.sum(weight[:, None] * got_coef, axis=0)
    weight_part = jnp.sum(weight)
    weight_pos = jnp.sum(
        jnp.where(jnp.arange(positions)[:, None] == place[None, :], weight[None, :], 0.0), axis=1
    )
    pos_lanes = weight_pos.reshape(GRID, n_visit, per_dev).transpose(1, 2, 0)
    pos_lanes = jnp.take(pos_lanes, bit_reverse(jnp.arange(n_visit), bits) ^ me_visit, axis=0)
    pos_lanes = jnp.concatenate(
        [pos_lanes, jnp.zeros((n_visit, per_dev, tile - GRID), jnp.float32)], axis=2
    ).reshape(n_visit, 1, per_dev * tile)
    psf_row = jnp.concatenate(
        [psf_part, weight_part[None], jnp.zeros((per_dev * tile - BASIS - 1,), jnp.float32)]
    )
    extra = jnp.concatenate(
        [
            pos_lanes,
            jnp.broadcast_to(psf_row[None, None, :], (n_visit, 1, per_dev * tile)),
            jnp.zeros((n_visit, EXTRA - 2, per_dev * tile), jnp.float32),
        ],
        axis=1,
    )
    var_pos = variance_field(
        where, weight * weight, got_vm, extra, (n_visit, GRID * tile + EXTRA, per_dev * tile)
    )
    var_share = reduce_scatter_visit(var_pos, n_visit)

    part_im = lax.all_to_all(send_im, "sky", split_axis=0, concat_axis=0, tiled=True)
    var_share, part_im = lax.optimization_barrier((var_share, part_im))
    part_im = part_im.reshape(slots_all, tile, tile)
    source = (me - jnp.arange(n_sky)) % n_sky

    def by_source(values):
        return jnp.take(values.reshape(n_sky, held_most, -1), source, axis=0).reshape(slots_all, -1)

    im_where = tuple(by_source(values)[:, 0] for values in where)
    image_pos = image_field(
        im_where, by_source(weight)[:, 0], by_source(got_coef).reshape(slots_all * BASIS), part_im,
        row_side, col_side, (n_visit, GRID * tile, per_dev * tile),
    )
    image_share = reduce_scatter_visit(image_pos, n_visit)

    body_rows = GRID * tile
    pos_weight = var_share[body_rows, :].reshape(per_dev, tile)[:, :GRID]
    denom = jnp.maximum(pos_weight, weight_floor).T
    denom = jnp.broadcast_to(denom[:, None, :, None], (GRID, tile, per_dev, tile))
    denom = denom.reshape(body_rows, per_dev * tile)
    coadd_image = image_share / denom
    coadd_variance = var_share[:body_rows, :] / (denom * denom)

    psf_total = var_share[body_rows + 1, :BASIS]
    weight_total = var_share[body_rows + 1, BASIS]
    share = psf_total / weight_total
    high = lax.Precision.HIGHEST
    coadd_psf = jnp.einsum(
        "k,ka,kb->ab",
        share,
        col_taps.astype(jnp.float32),
        row_taps.astype(jnp.float32),
        precision=high,
    )[None]
    return (coadd_image, coadd_variance, coadd_psf)


def solution(mesh):
    return jax.shard_map(
        shards,
        mesh=mesh,
        in_specs=(
            P("visit", "sky", None, None),
            P("visit", "sky", None, None),
            P("visit", "sky", None),
            P("visit", "sky", None),
            P("visit", "sky"),
            P(),
            P(),
        ),
        out_specs=(P("sky", "visit"), P("sky", "visit"), P("sky", None, None)),
        check_vma=False,
    )
```

```python
import jax
import jax.numpy as jnp
from jax import lax
from jax.experimental import pallas as pl
from jax.experimental.pallas import tpu as pltpu
from jax.sharding import PartitionSpec as P

GRID = 8
BASIS = 9
META = 16
EXTRA = 8


weight_floor = 0.5


def band_table(taps, tile):
    span = taps.shape[1]
    offset = jnp.arange(tile)[:, None] - jnp.arange(tile)[None, :] + (span - 1) // 2
    select = (offset[None, :, :] == jnp.arange(span)[:, None, None]).astype(jnp.float32)
    return jnp.einsum("kt,tij->kij", taps.astype(jnp.float32), select).astype(jnp.bfloat16)


def place_tile(out_ref, row, group, sub, contrib):
    tile = contrib.shape[0]
    per_dev = out_ref.shape[2] // tile
    start = pl.multiple_of(row * tile, tile)
    for c in range(per_dev):

        @pl.when(sub == c)
        def _():
            out_ref[group, pl.ds(start, tile), c * tile:(c + 1) * tile] += contrib


def variance_kernel(row_ref, group_ref, sub_ref, w2_ref, *refs):
    chunks, extra_ref, out_ref = refs[:-2], refs[-2], refs[-1]
    held = chunks[0].shape[0]
    tile = chunks[0].shape[2]
    body_rows = out_ref.shape[1] - extra_ref.shape[1]
    out_ref[:, :body_rows, :] = jnp.zeros((out_ref.shape[0], body_rows, out_ref.shape[2]), jnp.float32)
    out_ref[:, body_rows:, :] = extra_ref[...]
    for d, chunk in enumerate(chunks):

        def body(r, carry):
            t = d * held + r
            row = row_ref[t]

            @pl.when(row >= 0)
            def _():
                contrib = w2_ref[t] * chunk[r, :tile, :].astype(jnp.float32)
                place_tile(out_ref, row, group_ref[t], sub_ref[t], contrib)

            return carry

        lax.fori_loop(0, held, body, 0)


def image_kernel(order_ref, count_ref, row_ref, group_ref, sub_ref, w_ref, coef_ref, img_ref,
                 row_side_ref, col_side_ref, out_ref):
    tile = img_ref.shape[2]
    out_ref[...] = jnp.zeros(out_ref.shape, jnp.float32)

    def body(p, carry):
        pair = (order_ref[2 * p], order_ref[2 * p + 1])
        both = jnp.concatenate([img_ref[pair[0]], img_ref[pair[1]]], axis=0)
        first = jnp.dot(both, row_side_ref[...], preferred_element_type=jnp.float32)
        blocks = []
        for k in range(BASIS):
            halves = [
                (first[h * tile:(h + 1) * tile, k * tile:(k + 1) * tile]
                 * coef_ref[pair[h] * BASIS + k]).astype(jnp.bfloat16)
                for h in range(2)
            ]
            blocks.append(jnp.concatenate(halves, axis=1))
        scaled = jnp.concatenate(blocks, axis=0)
        matched = jnp.dot(col_side_ref[...], scaled, preferred_element_type=jnp.float32)
        for h in range(2):
            t = pair[h]
            row = row_ref[t]

            @pl.when(row >= 0)
            def _():
                place_tile(out_ref, row, group_ref[t], sub_ref[t],
                           w_ref[t] * matched[:, h * tile:(h + 1) * tile])

        return carry

    lax.fori_loop(0, (count_ref[0] + 1) // 2, body, 0)


def smem():
    return pl.BlockSpec(memory_space=pltpu.SMEM)


def vmem():
    return pl.BlockSpec(memory_space=pltpu.VMEM)


def variance_field(where, w2, chunks, extra, field_shape):
    return pl.pallas_call(
        variance_kernel,
        out_shape=jax.ShapeDtypeStruct(field_shape, jnp.float32),
        in_specs=[smem()] * 4 + [vmem()] * (len(chunks) + 1),
        out_specs=vmem(),
    )(*where, w2, *chunks, extra)


def image_field(where, w, coef, images, row_side, col_side, field_shape):
    filled = where[0] >= 0
    order = jnp.argsort(jnp.logical_not(filled), stable=True).astype(jnp.int32)
    count = jnp.sum(filled.astype(jnp.int32))[None]
    return pl.pallas_call(
        image_kernel,
        out_shape=jax.ShapeDtypeStruct(field_shape, jnp.float32),
        in_specs=[smem()] * 7 + [vmem()] * 3,
        out_specs=vmem(),
        cost_estimate=pl.CostEstimate(
            flops=4 * images.shape[0] * images.shape[2] ** 3 * BASIS,
            transcendentals=0,
            bytes_accessed=images.size * 2 + 4 * (field_shape[0] * field_shape[1] * field_shape[2]),
        ),
    )(order, count, *where, w, coef, images, row_side, col_side)


def split_exact(value):
    high = lax.reduce_precision(value, exponent_bits=8, mantissa_bits=7)
    rest = value - high
    middle = lax.reduce_precision(rest, exponent_bits=8, mantissa_bits=7)
    low = rest - middle
    return tuple(part.astype(jnp.bfloat16) for part in (high, middle, low))


def bit_reverse(values, bits):
    out = jnp.zeros_like(values)
    for b in range(bits):
        out = out | (((values >> b) & 1) << (bits - 1 - b))
    return out


def reduce_scatter_visit(field, n_visit):
    bits = n_visit.bit_length() - 1
    for b in range(bits):
        half = field.shape[0] // 2
        pairs = [(i, i ^ (1 << b)) for i in range(n_visit)]
        field = field[:half] + lax.ppermute(field[half:], "visit", perm=pairs)
    return field[0]


def shards(tile_image, tile_variance, match_coeffs, tile_patch, tile_offset, row_taps, col_taps):
    n_sky = lax.axis_size("sky")
    n_visit = lax.axis_size("visit")
    images = tile_image[0]
    variance = tile_variance[0]
    coeffs = match_coeffs[0]
    count = images.shape[0]
    tile = images.shape[1]
    held_most = max(2, 2 * count // n_sky)
    positions = GRID * GRID
    per_dev = GRID // n_visit
    dest = tile_patch[0, :, 0]
    offsets = tile_offset[0]
    band_row = band_table(row_taps, tile)
    band_col = band_table(col_taps, tile)
    row_side = band_row.transpose(1, 0, 2).reshape(tile, BASIS * tile)
    col_side = band_col.transpose(2, 0, 1).reshape(tile, BASIS * tile)
    order = jnp.arange(count)
    earlier = (dest[:, None] == dest[None, :]) & (order[None, :] < order[:, None])
    rank = jnp.sum(earlier.astype(jnp.int32), axis=1)
    slot = dest * held_most + rank
    slots_all = n_sky * held_most
    pick = (jnp.arange(slots_all)[:, None] == slot[None, :]).astype(jnp.bfloat16)
    me = lax.axis_index("sky")
    shift = (dest - me) % n_sky
    pick_shift = (jnp.arange(slots_all)[:, None] == (shift * held_most + rank)[None, :])
    weight_src = 1.0 / jnp.mean(variance.astype(jnp.float32), axis=(1, 2))
    w_parts = split_exact(weight_src)
    meta_row = jnp.concatenate(
        [coeffs, (offsets + 1).astype(jnp.bfloat16)[:, None]]
        + [part[:, None] for part in w_parts]
        + [jnp.zeros((count, tile - BASIS - 4), jnp.bfloat16)],
        axis=1,
    )
    meta = jnp.concatenate(
        [meta_row[:, None, :], jnp.zeros((count, META - 1, tile), jnp.bfloat16)], axis=1
    )
    var_meta = jnp.concatenate([variance, meta], axis=1)
    send_vm = jnp.dot(
        pick_shift.astype(jnp.bfloat16), var_meta.reshape(count, (tile + META) * tile),
        preferred_element_type=jnp.float32,
    )
    send_vm = send_vm.astype(jnp.bfloat16).reshape(n_sky, held_most, tile + META, tile)
    send_im = jnp.dot(
        pick, images.reshape(count, tile * tile), preferred_element_type=jnp.float32
    )
    send_im = send_im.astype(jnp.bfloat16).reshape(n_sky, held_most, tile, tile)

    got_vm = [send_vm[0]]
    for step in range(1, n_sky):
        pairs = [(src, (src + step) % n_sky) for src in range(n_sky)]
        got_vm.append(lax.ppermute(send_vm[step], "sky", perm=pairs))
    got_vm, send_im = lax.optimization_barrier((got_vm, send_im))
    got_meta = jnp.concatenate([chunk[:, tile, :] for chunk in got_vm]).astype(jnp.float32)
    got_coef = got_meta[:, :BASIS]
    place = got_meta[:, BASIS].astype(jnp.int32) - 1
    valid = place >= 0
    weight = (got_meta[:, BASIS + 1] + got_meta[:, BASIS + 2]) + got_meta[:, BASIS + 3]
    weight = jnp.where(valid, weight, 0.0)
    tile_row = jnp.where(valid, place // GRID, -1)
    tile_col = place % GRID
    bits = n_visit.bit_length() - 1
    me_visit = lax.axis_index("visit")
    where = (tile_row, bit_reverse((tile_col // per_dev) ^ me_visit, bits), tile_col % per_dev)
    psf_part = jnp.sum(weight[:, None] * got_coef, axis=0)
    weight_part = jnp.sum(weight)
    weight_pos = jnp.sum(
        jnp.where(jnp.arange(positions)[:, None] == place[None, :], weight[None, :], 0.0), axis=1
    )
    pos_lanes = weight_pos.reshape(GRID, n_visit, per_dev).transpose(1, 2, 0)
    pos_lanes = jnp.take(pos_lanes, bit_reverse(jnp.arange(n_visit), bits) ^ me_visit, axis=0)
    pos_lanes = jnp.concatenate(
        [pos_lanes, jnp.zeros((n_visit, per_dev, tile - GRID), jnp.float32)], axis=2
    ).reshape(n_visit, 1, per_dev * tile)
    psf_row = jnp.concatenate(
        [psf_part, weight_part[None], jnp.zeros((per_dev * tile - BASIS - 1,), jnp.float32)]
    )
    extra = jnp.concatenate(
        [
            pos_lanes,
            jnp.broadcast_to(psf_row[None, None, :], (n_visit, 1, per_dev * tile)),
            jnp.zeros((n_visit, EXTRA - 2, per_dev * tile), jnp.float32),
        ],
        axis=1,
    )
    var_pos = variance_field(
        where, weight * weight, got_vm, extra, (n_visit, GRID * tile + EXTRA, per_dev * tile)
    )
    var_share = reduce_scatter_visit(var_pos, n_visit)

    part_im = lax.all_to_all(send_im, "sky", split_axis=0, concat_axis=0, tiled=True)
    var_share, part_im = lax.optimization_barrier((var_share, part_im))
    part_im = part_im.reshape(slots_all, tile, tile)
    source = (me - jnp.arange(n_sky)) % n_sky

    def by_source(values):
        return jnp.take(values.reshape(n_sky, held_most, -1), source, axis=0).reshape(slots_all, -1)

    im_where = tuple(by_source(values)[:, 0] for values in where)
    band = GRID // 2
    im_w = by_source(weight)[:, 0]
    im_coef = by_source(got_coef).reshape(slots_all * BASIS)
    shares = []
    for lower in (0, band):
        rows = im_where[0] - lower
        rows = jnp.where((rows >= 0) & (rows < band), rows, -1)
        band_pos = image_field(
            (rows,) + im_where[1:], im_w, im_coef, part_im, row_side, col_side,
            (n_visit, band * tile, per_dev * tile),
        )
        shares.append(reduce_scatter_visit(band_pos, n_visit))
    image_share = jnp.concatenate(shares, axis=0)

    body_rows = GRID * tile
    pos_weight = var_share[body_rows, :].reshape(per_dev, tile)[:, :GRID]
    denom = jnp.maximum(pos_weight, weight_floor).T
    denom = jnp.broadcast_to(denom[:, None, :, None], (GRID, tile, per_dev, tile))
    denom = denom.reshape(body_rows, per_dev * tile)
    coadd_image = image_share / denom
    coadd_variance = var_share[:body_rows, :] / (denom * denom)

    psf_total = var_share[body_rows + 1, :BASIS]
    weight_total = var_share[body_rows + 1, BASIS]
    share = psf_total / weight_total
    high = lax.Precision.HIGHEST
    coadd_psf = jnp.einsum(
        "k,ka,kb->ab",
        share,
        col_taps.astype(jnp.float32),
        row_taps.astype(jnp.float32),
        precision=high,
    )[None]
    return (coadd_image, coadd_variance, coadd_psf)


def solution(mesh):
    return jax.shard_map(
        shards,
        mesh=mesh,
        in_specs=(
            P("visit", "sky", None, None),
            P("visit", "sky", None, None),
            P("visit", "sky", None),
            P("visit", "sky", None),
            P("visit", "sky"),
            P(),
            P(),
        ),
        out_specs=(P("sky", "visit"), P("sky", "visit"), P("sky", None, None)),
        check_vma=False,
    )
```

```python
import jax
import jax.numpy as jnp
from jax import lax
from jax.experimental import pallas as pl
from jax.experimental.pallas import tpu as pltpu
from jax.sharding import PartitionSpec as P

GRID = 8
BASIS = 9
META = 16
EXTRA = 8


weight_floor = 0.5


def band_table(taps, tile):
    span = taps.shape[1]
    offset = jnp.arange(tile)[:, None] - jnp.arange(tile)[None, :] + (span - 1) // 2
    select = (offset[None, :, :] == jnp.arange(span)[:, None, None]).astype(jnp.float32)
    return jnp.einsum("kt,tij->kij", taps.astype(jnp.float32), select).astype(jnp.bfloat16)


def place_tile(out_ref, row, group, sub, contrib):
    tile = contrib.shape[0]
    per_dev = out_ref.shape[2] // tile
    start = pl.multiple_of(row * tile, tile)
    for c in range(per_dev):

        @pl.when(sub == c)
        def _():
            out_ref[group, pl.ds(start, tile), c * tile:(c + 1) * tile] += contrib


def variance_kernel(place_ref, w2_ref, *refs):
    chunks, extra_ref, out_ref = refs[:-2], refs[-2], refs[-1]
    held = chunks[0].shape[0]
    tile = chunks[0].shape[2]
    out_ref[:, :tile, :] = jnp.zeros((out_ref.shape[0], tile, tile), jnp.float32)
    out_ref[:, tile:, :] = extra_ref[...]
    for d, chunk in enumerate(chunks):

        def body(r, carry):
            t = d * held + r
            q = place_ref[t]

            @pl.when(q >= 0)
            def _():
                out_ref[q, :tile, :] += w2_ref[t] * chunk[r, :tile, :].astype(jnp.float32)

            return carry

        lax.fori_loop(0, held, body, 0)


def image_kernel(order_ref, count_ref, row_ref, group_ref, sub_ref, w_ref, coef_ref, img_ref,
                 row_side_ref, col_side_ref, out_ref):
    tile = img_ref.shape[2]
    out_ref[...] = jnp.zeros(out_ref.shape, jnp.float32)

    def body(p, carry):
        pair = (order_ref[2 * p], order_ref[2 * p + 1])
        both = jnp.concatenate([img_ref[pair[0]], img_ref[pair[1]]], axis=0)
        first = jnp.dot(both, row_side_ref[...], preferred_element_type=jnp.float32)
        blocks = []
        for k in range(BASIS):
            halves = [
                (first[h * tile:(h + 1) * tile, k * tile:(k + 1) * tile]
                 * coef_ref[pair[h] * BASIS + k]).astype(jnp.bfloat16)
                for h in range(2)
            ]
            blocks.append(jnp.concatenate(halves, axis=1))
        scaled = jnp.concatenate(blocks, axis=0)
        matched = jnp.dot(col_side_ref[...], scaled, preferred_element_type=jnp.float32)
        for h in range(2):
            t = pair[h]
            row = row_ref[t]

            @pl.when(row >= 0)
            def _():
                place_tile(out_ref, row, group_ref[t], sub_ref[t],
                           w_ref[t] * matched[:, h * tile:(h + 1) * tile])

        return carry

    lax.fori_loop(0, (count_ref[0] + 1) // 2, body, 0)


def smem():
    return pl.BlockSpec(memory_space=pltpu.SMEM)


def vmem():
    return pl.BlockSpec(memory_space=pltpu.VMEM)


def variance_field(where, w2, chunks, extra, field_shape):
    return pl.pallas_call(
        variance_kernel,
        out_shape=jax.ShapeDtypeStruct(field_shape, jnp.float32),
        in_specs=[smem()] * 2 + [vmem()] * (len(chunks) + 1),
        out_specs=vmem(),
    )(where, w2, *chunks, extra)


def image_field(where, w, coef, images, row_side, col_side, field_shape):
    filled = where[0] >= 0
    order = jnp.argsort(jnp.logical_not(filled), stable=True).astype(jnp.int32)
    count = jnp.sum(filled.astype(jnp.int32))[None]
    return pl.pallas_call(
        image_kernel,
        out_shape=jax.ShapeDtypeStruct(field_shape, jnp.float32),
        in_specs=[smem()] * 7 + [vmem()] * 3,
        out_specs=vmem(),
        cost_estimate=pl.CostEstimate(
            flops=4 * images.shape[0] * images.shape[2] ** 3 * BASIS,
            transcendentals=0,
            bytes_accessed=images.size * 2 + 4 * (field_shape[0] * field_shape[1] * field_shape[2]),
        ),
    )(order, count, *where, w, coef, images, row_side, col_side)


def split_exact(value):
    high = lax.reduce_precision(value, exponent_bits=8, mantissa_bits=7)
    rest = value - high
    middle = lax.reduce_precision(rest, exponent_bits=8, mantissa_bits=7)
    low = rest - middle
    return tuple(part.astype(jnp.bfloat16) for part in (high, middle, low))


def bit_reverse(values, bits):
    out = jnp.zeros_like(values)
    for b in range(bits):
        out = out | (((values >> b) & 1) << (bits - 1 - b))
    return out


def reduce_scatter_visit(field, n_visit):
    bits = n_visit.bit_length() - 1
    for b in range(bits):
        half = field.shape[0] // 2
        pairs = [(i, i ^ (1 << b)) for i in range(n_visit)]
        field = field[:half] + lax.ppermute(field[half:], "visit", perm=pairs)
    return field[0]


def shards(tile_image, tile_variance, match_coeffs, tile_patch, tile_offset, row_taps, col_taps):
    n_sky = lax.axis_size("sky")
    n_visit = lax.axis_size("visit")
    images = tile_image[0]
    variance = tile_variance[0]
    coeffs = match_coeffs[0]
    count = images.shape[0]
    tile = images.shape[1]
    held_most = max(2, 2 * count // n_sky)
    positions = GRID * GRID
    per_dev = GRID // n_visit
    dest = tile_patch[0, :, 0]
    offsets = tile_offset[0]
    band_row = band_table(row_taps, tile)
    band_col = band_table(col_taps, tile)
    row_side = band_row.transpose(1, 0, 2).reshape(tile, BASIS * tile)
    col_side = band_col.transpose(2, 0, 1).reshape(tile, BASIS * tile)
    order = jnp.arange(count)
    earlier = (dest[:, None] == dest[None, :]) & (order[None, :] < order[:, None])
    rank = jnp.sum(earlier.astype(jnp.int32), axis=1)
    slot = dest * held_most + rank
    slots_all = n_sky * held_most
    pick = (jnp.arange(slots_all)[:, None] == slot[None, :]).astype(jnp.bfloat16)
    me = lax.axis_index("sky")
    shift = (dest - me) % n_sky
    pick_shift = (jnp.arange(slots_all)[:, None] == (shift * held_most + rank)[None, :])
    weight_src = 1.0 / jnp.mean(variance.astype(jnp.float32), axis=(1, 2))
    w_parts = split_exact(weight_src)
    meta_row = jnp.concatenate(
        [coeffs, (offsets + 1).astype(jnp.bfloat16)[:, None]]
        + [part[:, None] for part in w_parts]
        + [jnp.zeros((count, tile - BASIS - 4), jnp.bfloat16)],
        axis=1,
    )
    meta = jnp.concatenate(
        [meta_row[:, None, :], jnp.zeros((count, META - 1, tile), jnp.bfloat16)], axis=1
    )
    var_meta = jnp.concatenate([variance, meta], axis=1)
    send_vm = jnp.dot(
        pick_shift.astype(jnp.bfloat16), var_meta.reshape(count, (tile + META) * tile),
        preferred_element_type=jnp.float32,
    )
    send_vm = send_vm.astype(jnp.bfloat16).reshape(n_sky, held_most, tile + META, tile)
    send_im = jnp.dot(
        pick, images.reshape(count, tile * tile), preferred_element_type=jnp.float32
    )
    send_im = send_im.astype(jnp.bfloat16).reshape(n_sky, held_most, tile, tile)

    got_vm = [send_vm[0]]
    for step in range(1, n_sky):
        pairs = [(src, (src + step) % n_sky) for src in range(n_sky)]
        got_vm.append(lax.ppermute(send_vm[step], "sky", perm=pairs))
    got_vm, send_im = lax.optimization_barrier((got_vm, send_im))
    got_meta = jnp.concatenate([chunk[:, tile, :] for chunk in got_vm]).astype(jnp.float32)
    got_coef = got_meta[:, :BASIS]
    place = got_meta[:, BASIS].astype(jnp.int32) - 1
    valid = place >= 0
    weight = (got_meta[:, BASIS + 1] + got_meta[:, BASIS + 2]) + got_meta[:, BASIS + 3]
    weight = jnp.where(valid, weight, 0.0)
    tile_row = jnp.where(valid, place // GRID, -1)
    tile_col = place % GRID
    bits = n_visit.bit_length() - 1
    me_visit = lax.axis_index("visit")
    where = (tile_row, bit_reverse((tile_col // per_dev) ^ me_visit, bits), tile_col % per_dev)
    psf_part = jnp.sum(weight[:, None] * got_coef, axis=0)
    weight_part = jnp.sum(weight)
    weight_pos = jnp.sum(
        jnp.where(jnp.arange(positions)[:, None] == place[None, :], weight[None, :], 0.0), axis=1
    )
    psf_row = jnp.concatenate(
        [psf_part, weight_part[None], jnp.zeros((tile - BASIS - 1,), jnp.float32)]
    )
    pos_weight = weight_pos.reshape(GRID, GRID).T.reshape(positions)
    extra = jnp.concatenate(
        [
            jnp.broadcast_to(pos_weight[:, None, None], (positions, 1, tile)),
            jnp.broadcast_to(psf_row[None, None, :], (positions, 1, tile)),
            jnp.zeros((positions, EXTRA - 2, tile), jnp.float32),
        ],
        axis=1,
    )
    var_place = jnp.where(valid, tile_col * GRID + jnp.maximum(tile_row, 0), -1)
    var_pos = variance_field(
        var_place, weight * weight, got_vm, extra, (positions, tile + EXTRA, tile)
    )
    var_share = lax.psum_scatter(
        var_pos.reshape(GRID, GRID, tile + EXTRA, tile), "visit", scatter_dimension=0, tiled=True
    )

    part_im = lax.all_to_all(send_im, "sky", split_axis=0, concat_axis=0, tiled=True)
    var_share, part_im = lax.optimization_barrier((var_share, part_im))
    part_im = part_im.reshape(slots_all, tile, tile)
    source = (me - jnp.arange(n_sky)) % n_sky

    def by_source(values):
        return jnp.take(values.reshape(n_sky, held_most, -1), source, axis=0).reshape(slots_all, -1)

    im_where = tuple(by_source(values)[:, 0] for values in where)
    band = GRID // 2
    im_w = by_source(weight)[:, 0]
    im_coef = by_source(got_coef).reshape(slots_all * BASIS)
    shares = []
    for lower in (0, band):
        rows = im_where[0] - lower
        rows = jnp.where((rows >= 0) & (rows < band), rows, -1)
        band_pos = image_field(
            (rows,) + im_where[1:], im_w, im_coef, part_im, row_side, col_side,
            (n_visit, band * tile, per_dev * tile),
        )
        shares.append(reduce_scatter_visit(band_pos, n_visit))
    image_share = jnp.concatenate(shares, axis=0)

    body_rows = GRID * tile
    denom = jnp.maximum(var_share[:, :, tile, 0], weight_floor).T
    denom = jnp.broadcast_to(denom[:, None, :, None], (GRID, tile, per_dev, tile))
    denom = denom.reshape(body_rows, per_dev * tile)
    coadd_image = image_share / denom
    var_body = var_share[:, :, :tile, :].transpose(1, 2, 0, 3).reshape(body_rows, per_dev * tile)
    coadd_variance = var_body / (denom * denom)

    psf_total = var_share[0, 0, tile + 1, :BASIS]
    weight_total = var_share[0, 0, tile + 1, BASIS]
    share = psf_total / weight_total
    high = lax.Precision.HIGHEST
    coadd_psf = jnp.einsum(
        "k,ka,kb->ab",
        share,
        col_taps.astype(jnp.float32),
        row_taps.astype(jnp.float32),
        precision=high,
    )[None]
    return (coadd_image, coadd_variance, coadd_psf)


def solution(mesh):
    return jax.shard_map(
        shards,
        mesh=mesh,
        in_specs=(
            P("visit", "sky", None, None),
            P("visit", "sky", None, None),
            P("visit", "sky", None),
            P("visit", "sky", None),
            P("visit", "sky"),
            P(),
            P(),
        ),
        out_specs=(P("sky", "visit"), P("sky", "visit"), P("sky", None, None)),
        check_vma=False,
    )
```

```python
import functools

import jax
import jax.numpy as jnp
from jax import lax
from jax.experimental import pallas as pl
from jax.experimental.pallas import tpu as pltpu
from jax.sharding import PartitionSpec as P

GRID = 8
BASIS = 9
META = 16
EXTRA = 8


weight_floor = 0.5


def band_table(taps, tile):
    span = taps.shape[1]
    offset = jnp.arange(tile)[:, None] - jnp.arange(tile)[None, :] + (span - 1) // 2
    select = (offset[None, :, :] == jnp.arange(span)[:, None, None]).astype(jnp.float32)
    return jnp.einsum("kt,tij->kij", taps.astype(jnp.float32), select).astype(jnp.bfloat16)


def place_tile(out_ref, row, group, sub, contrib):
    tile = contrib.shape[0]
    per_dev = out_ref.shape[2] // tile
    start = pl.multiple_of(row * tile, tile)
    for c in range(per_dev):

        @pl.when(sub == c)
        def _():
            out_ref[group, pl.ds(start, tile), c * tile:(c + 1) * tile] += contrib


def variance_kernel(row_ref, group_ref, sub_ref, w2_ref, *refs):
    chunks, extra_ref, out_ref = refs[:-2], refs[-2], refs[-1]
    held = chunks[0].shape[0]
    tile = chunks[0].shape[2]
    body_rows = out_ref.shape[1] - extra_ref.shape[1]
    out_ref[:, :body_rows, :] = jnp.zeros((out_ref.shape[0], body_rows, out_ref.shape[2]), jnp.float32)
    out_ref[:, body_rows:, :] = extra_ref[...]
    for d, chunk in enumerate(chunks):

        def body(r, carry):
            t = d * held + r
            row = row_ref[t]

            @pl.when(row >= 0)
            def _():
                contrib = w2_ref[t] * chunk[r, :tile, :].astype(jnp.float32)
                place_tile(out_ref, row, group_ref[t], sub_ref[t], contrib)

            return carry

        lax.fori_loop(0, held, body, 0)


def image_kernel(base, accumulate, order_ref, count_ref, row_ref, group_ref, sub_ref, w_ref, coef_ref,
                 *refs):
    if accumulate:
        chunks, (row_side_ref, col_side_ref, field_ref, out_ref) = refs[:-4], refs[-4:]
        out_ref[...] = field_ref[...]
    else:
        chunks, (row_side_ref, col_side_ref, out_ref) = refs[:-3], refs[-3:]
        out_ref[...] = jnp.zeros(out_ref.shape, jnp.float32)
    held = chunks[0].shape[0]
    tile = chunks[0].shape[2]
    for c, chunk in enumerate(chunks):
        first_slot = (base + c) * held

        def body(p, carry):
            local = (order_ref[c * held + 2 * p], order_ref[c * held + 2 * p + 1])
            pair = (first_slot + local[0], first_slot + local[1])
            both = jnp.concatenate([chunk[local[0]], chunk[local[1]]], axis=0)
            first = jnp.dot(both, row_side_ref[...], preferred_element_type=jnp.float32)
            blocks = []
            for k in range(BASIS):
                halves = [
                    (first[h * tile:(h + 1) * tile, k * tile:(k + 1) * tile]
                     * coef_ref[pair[h] * BASIS + k]).astype(jnp.bfloat16)
                    for h in range(2)
                ]
                blocks.append(jnp.concatenate(halves, axis=1))
            scaled = jnp.concatenate(blocks, axis=0)
            matched = jnp.dot(col_side_ref[...], scaled, preferred_element_type=jnp.float32)
            for h in range(2):
                t = pair[h]
                row = row_ref[t]

                @pl.when(row >= 0)
                def _():
                    place_tile(out_ref, row, group_ref[t], sub_ref[t],
                               w_ref[t] * matched[:, h * tile:(h + 1) * tile])

            return carry

        lax.fori_loop(0, (count_ref[c] + 1) // 2, body, 0)


def smem():
    return pl.BlockSpec(memory_space=pltpu.SMEM)


def vmem():
    return pl.BlockSpec(memory_space=pltpu.VMEM)


def variance_field(where, w2, chunks, extra, field_shape):
    return pl.pallas_call(
        variance_kernel,
        out_shape=jax.ShapeDtypeStruct(field_shape, jnp.float32),
        in_specs=[smem()] * 4 + [vmem()] * (len(chunks) + 1),
        out_specs=vmem(),
    )(*where, w2, *chunks, extra)


def image_field(where, w, coef, chunks, base, row_side, col_side, field_shape, field=None):
    held = chunks[0].shape[0]
    n = len(chunks)
    filled = where[0][base * held:(base + n) * held].reshape(n, held) >= 0
    order = jnp.argsort(jnp.logical_not(filled), axis=1, stable=True).astype(jnp.int32)
    count = jnp.sum(filled.astype(jnp.int32), axis=1)
    args = [order.reshape(n * held), count, *where, w, coef, *chunks, row_side, col_side]
    if field is not None:
        args.append(field)
    tile = chunks[0].shape[2]
    return pl.pallas_call(
        functools.partial(image_kernel, base, field is not None),
        out_shape=jax.ShapeDtypeStruct(field_shape, jnp.float32),
        in_specs=[smem()] * 7 + [vmem()] * (len(args) - 7),
        out_specs=vmem(),
        input_output_aliases={} if field is None else {len(args) - 1: 0},
        cost_estimate=pl.CostEstimate(
            flops=4 * n * held * tile ** 3 * BASIS,
            transcendentals=0,
            bytes_accessed=n * held * tile * tile * 2 + 8 * (field_shape[0] * field_shape[1] * field_shape[2]),
        ),
    )(*args)


def split_exact(value):
    high = lax.reduce_precision(value, exponent_bits=8, mantissa_bits=7)
    rest = value - high
    middle = lax.reduce_precision(rest, exponent_bits=8, mantissa_bits=7)
    low = rest - middle
    return tuple(part.astype(jnp.bfloat16) for part in (high, middle, low))


def bit_reverse(values, bits):
    out = jnp.zeros_like(values)
    for b in range(bits):
        out = out | (((values >> b) & 1) << (bits - 1 - b))
    return out


def reduce_scatter_visit(field, n_visit):
    bits = n_visit.bit_length() - 1
    for b in range(bits):
        half = field.shape[0] // 2
        pairs = [(i, i ^ (1 << b)) for i in range(n_visit)]
        field = field[:half] + lax.ppermute(field[half:], "visit", perm=pairs)
    return field[0]


def shards(tile_image, tile_variance, match_coeffs, tile_patch, tile_offset, row_taps, col_taps):
    n_sky = lax.axis_size("sky")
    n_visit = lax.axis_size("visit")
    images = tile_image[0]
    variance = tile_variance[0]
    coeffs = match_coeffs[0]
    count = images.shape[0]
    tile = images.shape[1]
    held_most = max(2, 2 * count // n_sky)
    positions = GRID * GRID
    per_dev = GRID // n_visit
    dest = tile_patch[0, :, 0]
    offsets = tile_offset[0]
    band_row = band_table(row_taps, tile)
    band_col = band_table(col_taps, tile)
    row_side = band_row.transpose(1, 0, 2).reshape(tile, BASIS * tile)
    col_side = band_col.transpose(2, 0, 1).reshape(tile, BASIS * tile)
    order = jnp.arange(count)
    earlier = (dest[:, None] == dest[None, :]) & (order[None, :] < order[:, None])
    rank = jnp.sum(earlier.astype(jnp.int32), axis=1)
    slot = dest * held_most + rank
    slots_all = n_sky * held_most
    pick = (jnp.arange(slots_all)[:, None] == slot[None, :]).astype(jnp.bfloat16)
    me = lax.axis_index("sky")
    shift = (dest - me) % n_sky
    pick_shift = (jnp.arange(slots_all)[:, None] == (shift * held_most + rank)[None, :])
    weight_src = 1.0 / jnp.mean(variance.astype(jnp.float32), axis=(1, 2))
    w_parts = split_exact(weight_src)
    meta_row = jnp.concatenate(
        [coeffs, (offsets + 1).astype(jnp.bfloat16)[:, None]]
        + [part[:, None] for part in w_parts]
        + [jnp.zeros((count, tile - BASIS - 4), jnp.bfloat16)],
        axis=1,
    )
    meta = jnp.concatenate(
        [meta_row[:, None, :], jnp.zeros((count, META - 1, tile), jnp.bfloat16)], axis=1
    )
    var_meta = jnp.concatenate([variance, meta], axis=1)
    send_vm = jnp.dot(
        pick_shift.astype(jnp.bfloat16), var_meta.reshape(count, (tile + META) * tile),
        preferred_element_type=jnp.float32,
    )
    send_vm = send_vm.astype(jnp.bfloat16).reshape(n_sky, held_most, tile + META, tile)
    send_im = jnp.dot(
        pick_shift.astype(jnp.bfloat16), images.reshape(count, tile * tile),
        preferred_element_type=jnp.float32,
    )
    send_im = send_im.astype(jnp.bfloat16).reshape(n_sky, held_most, tile, tile)

    got_vm = [send_vm[0]]
    for step in range(1, n_sky):
        pairs = [(src, (src + step) % n_sky) for src in range(n_sky)]
        got_vm.append(lax.ppermute(send_vm[step], "sky", perm=pairs))
    got_vm, send_im = lax.optimization_barrier((got_vm, send_im))
    got_meta = jnp.concatenate([chunk[:, tile, :] for chunk in got_vm]).astype(jnp.float32)
    got_coef = got_meta[:, :BASIS]
    place = got_meta[:, BASIS].astype(jnp.int32) - 1
    valid = place >= 0
    weight = (got_meta[:, BASIS + 1] + got_meta[:, BASIS + 2]) + got_meta[:, BASIS + 3]
    weight = jnp.where(valid, weight, 0.0)
    tile_row = jnp.where(valid, place // GRID, -1)
    tile_col = place % GRID
    bits = n_visit.bit_length() - 1
    me_visit = lax.axis_index("visit")
    where = (tile_row, bit_reverse((tile_col // per_dev) ^ me_visit, bits), tile_col % per_dev)
    psf_part = jnp.sum(weight[:, None] * got_coef, axis=0)
    weight_part = jnp.sum(weight)
    weight_pos = jnp.sum(
        jnp.where(jnp.arange(positions)[:, None] == place[None, :], weight[None, :], 0.0), axis=1
    )
    pos_lanes = weight_pos.reshape(GRID, n_visit, per_dev).transpose(1, 2, 0)
    pos_lanes = jnp.take(pos_lanes, bit_reverse(jnp.arange(n_visit), bits) ^ me_visit, axis=0)
    pos_lanes = jnp.concatenate(
        [pos_lanes, jnp.zeros((n_visit, per_dev, tile - GRID), jnp.float32)], axis=2
    ).reshape(n_visit, 1, per_dev * tile)
    psf_row = jnp.concatenate(
        [psf_part, weight_part[None], jnp.zeros((per_dev * tile - BASIS - 1,), jnp.float32)]
    )
    extra = jnp.concatenate(
        [
            pos_lanes,
            jnp.broadcast_to(psf_row[None, None, :], (n_visit, 1, per_dev * tile)),
            jnp.zeros((n_visit, EXTRA - 2, per_dev * tile), jnp.float32),
        ],
        axis=1,
    )
    var_pos = variance_field(
        where, weight * weight, got_vm, extra, (n_visit, GRID * tile + EXTRA, per_dev * tile)
    )
    var_share = reduce_scatter_visit(var_pos, n_visit)

    half = n_sky // 2
    group_a = [send_im[0]]
    for step in range(1, half):
        pairs = [(src, (src + step) % n_sky) for src in range(n_sky)]
        group_a.append(lax.ppermute(send_im[step], "sky", perm=pairs))
    group_a, later, var_share = lax.optimization_barrier((group_a, send_im[half:], var_share))
    group_b = []
    for step in range(half, n_sky):
        pairs = [(src, (src + step) % n_sky) for src in range(n_sky)]
        group_b.append(lax.ppermute(later[step - half], "sky", perm=pairs))
    im_coef = got_coef.reshape(slots_all * BASIS)
    field_shape = (n_visit, GRID * tile, per_dev * tile)
    image_pos = image_field(where, weight, im_coef, group_a, 0, row_side, col_side, field_shape)
    image_pos = image_field(
        where, weight, im_coef, group_b, half, row_side, col_side, field_shape, image_pos
    )
    image_share = reduce_scatter_visit(image_pos, n_visit)

    body_rows = GRID * tile
    pos_weight = var_share[body_rows, :].reshape(per_dev, tile)[:, :GRID]
    denom = jnp.maximum(pos_weight, weight_floor).T
    denom = jnp.broadcast_to(denom[:, None, :, None], (GRID, tile, per_dev, tile))
    denom = denom.reshape(body_rows, per_dev * tile)
    coadd_image = image_share / denom
    coadd_variance = var_share[:body_rows, :] / (denom * denom)

    psf_total = var_share[body_rows + 1, :BASIS]
    weight_total = var_share[body_rows + 1, BASIS]
    share = psf_total / weight_total
    high = lax.Precision.HIGHEST
    coadd_psf = jnp.einsum(
        "k,ka,kb->ab",
        share,
        col_taps.astype(jnp.float32),
        row_taps.astype(jnp.float32),
        precision=high,
    )[None]
    return (coadd_image, coadd_variance, coadd_psf)


def solution(mesh):
    return jax.shard_map(
        shards,
        mesh=mesh,
        in_specs=(
            P("visit", "sky", None, None),
            P("visit", "sky", None, None),
            P("visit", "sky", None),
            P("visit", "sky", None),
            P("visit", "sky"),
            P(),
            P(),
        ),
        out_specs=(P("sky", "visit"), P("sky", "visit"), P("sky", None, None)),
        check_vma=False,
    )
```

```python
import jax
import jax.numpy as jnp
from jax import lax
from jax.experimental import pallas as pl
from jax.experimental.pallas import tpu as pltpu
from jax.sharding import PartitionSpec as P

GRID = 8
BASIS = 9
META = 16
EXTRA = 8


weight_floor = 0.5


def band_table(taps, tile):
    span = taps.shape[1]
    offset = jnp.arange(tile)[:, None] - jnp.arange(tile)[None, :] + (span - 1) // 2
    select = (offset[None, :, :] == jnp.arange(span)[:, None, None]).astype(jnp.float32)
    return jnp.einsum("kt,tij->kij", taps.astype(jnp.float32), select).astype(jnp.bfloat16)


def place_tile(out_ref, row, group, sub, contrib):
    tile = contrib.shape[0]
    per_dev = out_ref.shape[2] // tile
    start = pl.multiple_of(row * tile, tile)
    for c in range(per_dev):

        @pl.when(sub == c)
        def _():
            out_ref[group, pl.ds(start, tile), c * tile:(c + 1) * tile] += contrib


def variance_kernel(row_ref, group_ref, sub_ref, w2_ref, *refs):
    chunks, extra_ref, out_ref = refs[:-2], refs[-2], refs[-1]
    held = chunks[0].shape[0]
    tile = chunks[0].shape[2]
    body_rows = out_ref.shape[1] - extra_ref.shape[1]
    out_ref[:, :body_rows, :] = jnp.zeros((out_ref.shape[0], body_rows, out_ref.shape[2]), jnp.float32)
    out_ref[:, body_rows:, :] = extra_ref[...]
    for d, chunk in enumerate(chunks):

        def body(r, carry):
            t = d * held + r
            row = row_ref[t]

            @pl.when(row >= 0)
            def _():
                contrib = w2_ref[t] * chunk[r, :tile, :].astype(jnp.float32)
                place_tile(out_ref, row, group_ref[t], sub_ref[t], contrib)

            return carry

        lax.fori_loop(0, held, body, 0)


def image_kernel(order_ref, count_ref, row_ref, group_ref, sub_ref, w_ref, coef_ref, img_ref,
                 row_side_ref, col_side_ref, out_ref):
    tile = img_ref.shape[2]
    out_ref[...] = jnp.zeros(out_ref.shape, jnp.float32)

    def body(p, carry):
        pair = (order_ref[2 * p], order_ref[2 * p + 1])
        both = jnp.concatenate([img_ref[pair[0]], img_ref[pair[1]]], axis=0)
        first = jnp.dot(both, row_side_ref[...], preferred_element_type=jnp.float32)
        blocks = []
        for k in range(BASIS):
            halves = [
                (first[h * tile:(h + 1) * tile, k * tile:(k + 1) * tile]
                 * coef_ref[pair[h] * BASIS + k]).astype(jnp.bfloat16)
                for h in range(2)
            ]
            blocks.append(jnp.concatenate(halves, axis=1))
        scaled = jnp.concatenate(blocks, axis=0)
        matched = jnp.dot(col_side_ref[...], scaled, preferred_element_type=jnp.float32)
        for h in range(2):
            t = pair[h]
            row = row_ref[t]

            @pl.when(row >= 0)
            def _():
                place_tile(out_ref, row, group_ref[t], sub_ref[t],
                           w_ref[t] * matched[:, h * tile:(h + 1) * tile])

        return carry

    lax.fori_loop(0, (count_ref[0] + 1) // 2, body, 0)


def smem():
    return pl.BlockSpec(memory_space=pltpu.SMEM)


def vmem():
    return pl.BlockSpec(memory_space=pltpu.VMEM)


def variance_field(where, w2, chunks, extra, field_shape):
    return pl.pallas_call(
        variance_kernel,
        out_shape=jax.ShapeDtypeStruct(field_shape, jnp.float32),
        in_specs=[smem()] * 4 + [vmem()] * (len(chunks) + 1),
        out_specs=vmem(),
    )(*where, w2, *chunks, extra)


def image_field(where, w, coef, images, row_side, col_side, field_shape):
    filled = where[0] >= 0
    order = jnp.argsort(jnp.logical_not(filled), stable=True).astype(jnp.int32)
    count = jnp.sum(filled.astype(jnp.int32))[None]
    return pl.pallas_call(
        image_kernel,
        out_shape=jax.ShapeDtypeStruct(field_shape, jnp.float32),
        in_specs=[smem()] * 7 + [vmem()] * 3,
        out_specs=vmem(),
        cost_estimate=pl.CostEstimate(
            flops=4 * images.shape[0] * images.shape[2] ** 3 * BASIS,
            transcendentals=0,
            bytes_accessed=images.size * 2 + 4 * (field_shape[0] * field_shape[1] * field_shape[2]),
        ),
    )(order, count, *where, w, coef, images, row_side, col_side)


def split_exact(value):
    high = lax.reduce_precision(value, exponent_bits=8, mantissa_bits=7)
    rest = value - high
    middle = lax.reduce_precision(rest, exponent_bits=8, mantissa_bits=7)
    low = rest - middle
    return tuple(part.astype(jnp.bfloat16) for part in (high, middle, low))


def bit_reverse(values, bits):
    out = jnp.zeros_like(values)
    for b in range(bits):
        out = out | (((values >> b) & 1) << (bits - 1 - b))
    return out


def reduce_scatter_visit(field, n_visit):
    bits = n_visit.bit_length() - 1
    for b in range(bits):
        half = field.shape[0] // 2
        pairs = [(i, i ^ (1 << b)) for i in range(n_visit)]
        pieces = 1 if b == 0 else 2
        rows = field.shape[1] // pieces
        got = [
            lax.ppermute(field[half:, j * rows:(j + 1) * rows], "visit", perm=pairs)
            for j in range(pieces)
        ]
        field = field[:half] + jnp.concatenate(got, axis=1)
    return field[0]


def shards(tile_image, tile_variance, match_coeffs, tile_patch, tile_offset, row_taps, col_taps):
    n_sky = lax.axis_size("sky")
    n_visit = lax.axis_size("visit")
    images = tile_image[0]
    variance = tile_variance[0]
    coeffs = match_coeffs[0]
    count = images.shape[0]
    tile = images.shape[1]
    held_most = max(2, 2 * count // n_sky)
    positions = GRID * GRID
    per_dev = GRID // n_visit
    dest = tile_patch[0, :, 0]
    offsets = tile_offset[0]
    band_row = band_table(row_taps, tile)
    band_col = band_table(col_taps, tile)
    row_side = band_row.transpose(1, 0, 2).reshape(tile, BASIS * tile)
    col_side = band_col.transpose(2, 0, 1).reshape(tile, BASIS * tile)
    order = jnp.arange(count)
    earlier = (dest[:, None] == dest[None, :]) & (order[None, :] < order[:, None])
    rank = jnp.sum(earlier.astype(jnp.int32), axis=1)
    slot = dest * held_most + rank
    slots_all = n_sky * held_most
    pick = (jnp.arange(slots_all)[:, None] == slot[None, :]).astype(jnp.bfloat16)
    me = lax.axis_index("sky")
    shift = (dest - me) % n_sky
    pick_shift = (jnp.arange(slots_all)[:, None] == (shift * held_most + rank)[None, :])
    weight_src = 1.0 / jnp.mean(variance.astype(jnp.float32), axis=(1, 2))
    w_parts = split_exact(weight_src)
    meta_row = jnp.concatenate(
        [coeffs, (offsets + 1).astype(jnp.bfloat16)[:, None]]
        + [part[:, None] for part in w_parts]
        + [jnp.zeros((count, tile - BASIS - 4), jnp.bfloat16)],
        axis=1,
    )
    meta = jnp.concatenate(
        [meta_row[:, None, :], jnp.zeros((count, META - 1, tile), jnp.bfloat16)], axis=1
    )
    var_meta = jnp.concatenate([variance, meta], axis=1)
    send_vm = jnp.dot(
        pick_shift.astype(jnp.bfloat16), var_meta.reshape(count, (tile + META) * tile),
        preferred_element_type=jnp.float32,
    )
    send_vm = send_vm.astype(jnp.bfloat16).reshape(n_sky, held_most, tile + META, tile)
    send_im = jnp.dot(
        pick, images.reshape(count, tile * tile), preferred_element_type=jnp.float32
    )
    send_im = send_im.astype(jnp.bfloat16).reshape(n_sky, held_most, tile, tile)

    got_vm = [send_vm[0]]
    for step in range(1, n_sky):
        pairs = [(src, (src + step) % n_sky) for src in range(n_sky)]
        got_vm.append(lax.ppermute(send_vm[step], "sky", perm=pairs))
    got_vm, send_im = lax.optimization_barrier((got_vm, send_im))
    got_meta = jnp.concatenate([chunk[:, tile, :] for chunk in got_vm]).astype(jnp.float32)
    got_coef = got_meta[:, :BASIS]
    place = got_meta[:, BASIS].astype(jnp.int32) - 1
    valid = place >= 0
    weight = (got_meta[:, BASIS + 1] + got_meta[:, BASIS + 2]) + got_meta[:, BASIS + 3]
    weight = jnp.where(valid, weight, 0.0)
    tile_row = jnp.where(valid, place // GRID, -1)
    tile_col = place % GRID
    bits = n_visit.bit_length() - 1
    me_visit = lax.axis_index("visit")
    where = (tile_row, bit_reverse((tile_col // per_dev) ^ me_visit, bits), tile_col % per_dev)
    psf_part = jnp.sum(weight[:, None] * got_coef, axis=0)
    weight_part = jnp.sum(weight)
    weight_pos = jnp.sum(
        jnp.where(jnp.arange(positions)[:, None] == place[None, :], weight[None, :], 0.0), axis=1
    )
    pos_lanes = weight_pos.reshape(GRID, n_visit, per_dev).transpose(1, 2, 0)
    pos_lanes = jnp.take(pos_lanes, bit_reverse(jnp.arange(n_visit), bits) ^ me_visit, axis=0)
    pos_lanes = jnp.concatenate(
        [pos_lanes, jnp.zeros((n_visit, per_dev, tile - GRID), jnp.float32)], axis=2
    ).reshape(n_visit, 1, per_dev * tile)
    psf_row = jnp.concatenate(
        [psf_part, weight_part[None], jnp.zeros((per_dev * tile - BASIS - 1,), jnp.float32)]
    )
    extra = jnp.concatenate(
        [
            pos_lanes,
            jnp.broadcast_to(psf_row[None, None, :], (n_visit, 1, per_dev * tile)),
            jnp.zeros((n_visit, EXTRA - 2, per_dev * tile), jnp.float32),
        ],
        axis=1,
    )
    var_pos = variance_field(
        where, weight * weight, got_vm, extra, (n_visit, GRID * tile + EXTRA, per_dev * tile)
    )
    var_share = reduce_scatter_visit(var_pos, n_visit)

    part_im = lax.all_to_all(send_im, "sky", split_axis=0, concat_axis=0, tiled=True)
    var_share, part_im = lax.optimization_barrier((var_share, part_im))
    part_im = part_im.reshape(slots_all, tile, tile)
    source = (me - jnp.arange(n_sky)) % n_sky

    def by_source(values):
        return jnp.take(values.reshape(n_sky, held_most, -1), source, axis=0).reshape(slots_all, -1)

    im_where = tuple(by_source(values)[:, 0] for values in where)
    band = GRID // 2
    im_w = by_source(weight)[:, 0]
    im_coef = by_source(got_coef).reshape(slots_all * BASIS)
    shares = []
    for lower in (0, band):
        rows = im_where[0] - lower
        rows = jnp.where((rows >= 0) & (rows < band), rows, -1)
        band_pos = image_field(
            (rows,) + im_where[1:], im_w, im_coef, part_im, row_side, col_side,
            (n_visit, band * tile, per_dev * tile),
        )
        shares.append(reduce_scatter_visit(band_pos, n_visit))
    image_share = jnp.concatenate(shares, axis=0)

    body_rows = GRID * tile
    pos_weight = var_share[body_rows, :].reshape(per_dev, tile)[:, :GRID]
    denom = jnp.maximum(pos_weight, weight_floor).T
    denom = jnp.broadcast_to(denom[:, None, :, None], (GRID, tile, per_dev, tile))
    denom = denom.reshape(body_rows, per_dev * tile)
    coadd_image = image_share / denom
    coadd_variance = var_share[:body_rows, :] / (denom * denom)

    psf_total = var_share[body_rows + 1, :BASIS]
    weight_total = var_share[body_rows + 1, BASIS]
    share = psf_total / weight_total
    high = lax.Precision.HIGHEST
    coadd_psf = jnp.einsum(
        "k,ka,kb->ab",
        share,
        col_taps.astype(jnp.float32),
        row_taps.astype(jnp.float32),
        precision=high,
    )[None]
    return (coadd_image, coadd_variance, coadd_psf)


def solution(mesh):
    return jax.shard_map(
        shards,
        mesh=mesh,
        in_specs=(
            P("visit", "sky", None, None),
            P("visit", "sky", None, None),
            P("visit", "sky", None),
            P("visit", "sky", None),
            P("visit", "sky"),
            P(),
            P(),
        ),
        out_specs=(P("sky", "visit"), P("sky", "visit"), P("sky", None, None)),
        check_vma=False,
    )
```

```python
import functools

import jax
import jax.numpy as jnp
from jax import lax
from jax.experimental import pallas as pl
from jax.experimental.pallas import tpu as pltpu
from jax.sharding import PartitionSpec as P

GRID = 8
BASIS = 9
META = 16
EXTRA = 8


weight_floor = 0.5


def band_table(taps, tile):
    span = taps.shape[1]
    offset = jnp.arange(tile)[:, None] - jnp.arange(tile)[None, :] + (span - 1) // 2
    select = (offset[None, :, :] == jnp.arange(span)[:, None, None]).astype(jnp.float32)
    return jnp.einsum("kt,tij->kij", taps.astype(jnp.float32), select).astype(jnp.bfloat16)


def place_tile(out_ref, row, group, sub, contrib):
    tile = contrib.shape[0]
    per_dev = out_ref.shape[2] // tile
    start = pl.multiple_of(row * tile, tile)
    for c in range(per_dev):

        @pl.when(sub == c)
        def _():
            out_ref[group, pl.ds(start, tile), c * tile:(c + 1) * tile] += contrib


def variance_kernel(row_ref, group_ref, sub_ref, w2_ref, *refs):
    chunks, extra_ref, out_ref = refs[:-2], refs[-2], refs[-1]
    held = chunks[0].shape[0]
    tile = chunks[0].shape[2]
    body_rows = out_ref.shape[1] - extra_ref.shape[1]
    out_ref[:, :body_rows, :] = jnp.zeros((out_ref.shape[0], body_rows, out_ref.shape[2]), jnp.float32)
    out_ref[:, body_rows:, :] = extra_ref[...]
    for d, chunk in enumerate(chunks):

        def body(r, carry):
            t = d * held + r
            row = row_ref[t]

            @pl.when(row >= 0)
            def _():
                contrib = w2_ref[t] * chunk[r, :tile, :].astype(jnp.float32)
                place_tile(out_ref, row, group_ref[t], sub_ref[t], contrib)

            return carry

        lax.fori_loop(0, held, body, 0)


def image_kernel(accumulate, order_ref, count_ref, row_ref, group_ref, sub_ref, w_ref, coef_ref,
                 img_ref, row_side_ref, col_side_ref, *refs):
    tile = img_ref.shape[2]
    out_ref = refs[-1]
    if accumulate:
        out_ref[...] = refs[0][...]
    else:
        out_ref[...] = jnp.zeros(out_ref.shape, jnp.float32)

    def body(p, carry):
        pair = (order_ref[2 * p], order_ref[2 * p + 1])
        both = jnp.concatenate([img_ref[pair[0]], img_ref[pair[1]]], axis=0)
        first = jnp.dot(both, row_side_ref[...], preferred_element_type=jnp.float32)
        blocks = []
        for k in range(BASIS):
            halves = [
                (first[h * tile:(h + 1) * tile, k * tile:(k + 1) * tile]
                 * coef_ref[pair[h] * BASIS + k]).astype(jnp.bfloat16)
                for h in range(2)
            ]
            blocks.append(jnp.concatenate(halves, axis=1))
        scaled = jnp.concatenate(blocks, axis=0)
        matched = jnp.dot(col_side_ref[...], scaled, preferred_element_type=jnp.float32)
        for h in range(2):
            t = pair[h]
            row = row_ref[t]

            @pl.when(row >= 0)
            def _():
                place_tile(out_ref, row, group_ref[t], sub_ref[t],
                           w_ref[t] * matched[:, h * tile:(h + 1) * tile])

        return carry

    lax.fori_loop(0, (count_ref[0] + 1) // 2, body, 0)


def smem():
    return pl.BlockSpec(memory_space=pltpu.SMEM)


def vmem():
    return pl.BlockSpec(memory_space=pltpu.VMEM)


def variance_field(where, w2, chunks, extra, field_shape):
    return pl.pallas_call(
        variance_kernel,
        out_shape=jax.ShapeDtypeStruct(field_shape, jnp.float32),
        in_specs=[smem()] * 4 + [vmem()] * (len(chunks) + 1),
        out_specs=vmem(),
    )(*where, w2, *chunks, extra)


def image_field(where, w, coef, images, row_side, col_side, field_shape, field=None):
    filled = where[0] >= 0
    order = jnp.argsort(jnp.logical_not(filled), stable=True).astype(jnp.int32)
    count = jnp.sum(filled.astype(jnp.int32))[None]
    args = [order, count, *where, w, coef, images, row_side, col_side]
    if field is not None:
        args.append(field)
    return pl.pallas_call(
        functools.partial(image_kernel, field is not None),
        out_shape=jax.ShapeDtypeStruct(field_shape, jnp.float32),
        in_specs=[smem()] * 7 + [vmem()] * (len(args) - 7),
        out_specs=vmem(),
        input_output_aliases={} if field is None else {len(args) - 1: 0},
        cost_estimate=pl.CostEstimate(
            flops=4 * images.shape[0] * images.shape[2] ** 3 * BASIS,
            transcendentals=0,
            bytes_accessed=images.size * 2 + 8 * (field_shape[0] * field_shape[1] * field_shape[2]),
        ),
    )(*args)


def split_exact(value):
    high = lax.reduce_precision(value, exponent_bits=8, mantissa_bits=7)
    rest = value - high
    middle = lax.reduce_precision(rest, exponent_bits=8, mantissa_bits=7)
    low = rest - middle
    return tuple(part.astype(jnp.bfloat16) for part in (high, middle, low))


def bit_reverse(values, bits):
    out = jnp.zeros_like(values)
    for b in range(bits):
        out = out | (((values >> b) & 1) << (bits - 1 - b))
    return out


def reduce_scatter_visit(field, n_visit):
    bits = n_visit.bit_length() - 1
    for b in range(bits):
        half = field.shape[0] // 2
        pairs = [(i, i ^ (1 << b)) for i in range(n_visit)]
        field = field[:half] + lax.ppermute(field[half:], "visit", perm=pairs)
    return field[0]


def shards(tile_image, tile_variance, match_coeffs, tile_patch, tile_offset, row_taps, col_taps):
    n_sky = lax.axis_size("sky")
    n_visit = lax.axis_size("visit")
    images = tile_image[0]
    variance = tile_variance[0]
    coeffs = match_coeffs[0]
    count = images.shape[0]
    tile = images.shape[1]
    held_most = max(2, 2 * count // n_sky)
    positions = GRID * GRID
    per_dev = GRID // n_visit
    dest = tile_patch[0, :, 0]
    offsets = tile_offset[0]
    band_row = band_table(row_taps, tile)
    band_col = band_table(col_taps, tile)
    row_side = band_row.transpose(1, 0, 2).reshape(tile, BASIS * tile)
    col_side = band_col.transpose(2, 0, 1).reshape(tile, BASIS * tile)
    order = jnp.arange(count)
    earlier = (dest[:, None] == dest[None, :]) & (order[None, :] < order[:, None])
    rank = jnp.sum(earlier.astype(jnp.int32), axis=1)
    slot = dest * held_most + rank
    slots_all = n_sky * held_most
    pick = (jnp.arange(slots_all)[:, None] == slot[None, :]).astype(jnp.bfloat16)
    me = lax.axis_index("sky")
    shift = (dest - me) % n_sky
    pick_shift = (jnp.arange(slots_all)[:, None] == (shift * held_most + rank)[None, :])
    weight_src = 1.0 / jnp.mean(variance.astype(jnp.float32), axis=(1, 2))
    w_parts = split_exact(weight_src)
    meta_row = jnp.concatenate(
        [coeffs, (offsets + 1).astype(jnp.bfloat16)[:, None]]
        + [part[:, None] for part in w_parts]
        + [jnp.zeros((count, tile - BASIS - 4), jnp.bfloat16)],
        axis=1,
    )
    meta = jnp.concatenate(
        [meta_row[:, None, :], jnp.zeros((count, META - 1, tile), jnp.bfloat16)], axis=1
    )
    var_meta = jnp.concatenate([variance, meta], axis=1)
    send_vm = jnp.dot(
        pick_shift.astype(jnp.bfloat16), var_meta.reshape(count, (tile + META) * tile),
        preferred_element_type=jnp.float32,
    )
    send_vm = send_vm.astype(jnp.bfloat16).reshape(n_sky, held_most, tile + META, tile)
    send_im = jnp.dot(
        pick, images.reshape(count, tile * tile), preferred_element_type=jnp.float32
    )
    send_im = send_im.astype(jnp.bfloat16).reshape(n_sky, held_most, tile, tile)

    got_vm = [send_vm[0]]
    for step in range(1, n_sky):
        pairs = [(src, (src + step) % n_sky) for src in range(n_sky)]
        got_vm.append(lax.ppermute(send_vm[step], "sky", perm=pairs))
    got_vm, send_im = lax.optimization_barrier((got_vm, send_im))
    got_meta = jnp.concatenate([chunk[:, tile, :] for chunk in got_vm]).astype(jnp.float32)
    got_coef = got_meta[:, :BASIS]
    place = got_meta[:, BASIS].astype(jnp.int32) - 1
    valid = place >= 0
    weight = (got_meta[:, BASIS + 1] + got_meta[:, BASIS + 2]) + got_meta[:, BASIS + 3]
    weight = jnp.where(valid, weight, 0.0)
    tile_row = jnp.where(valid, place // GRID, -1)
    tile_col = place % GRID
    bits = n_visit.bit_length() - 1
    me_visit = lax.axis_index("visit")
    where = (tile_row, bit_reverse((tile_col // per_dev) ^ me_visit, bits), tile_col % per_dev)
    psf_part = jnp.sum(weight[:, None] * got_coef, axis=0)
    weight_part = jnp.sum(weight)
    weight_pos = jnp.sum(
        jnp.where(jnp.arange(positions)[:, None] == place[None, :], weight[None, :], 0.0), axis=1
    )
    pos_lanes = weight_pos.reshape(GRID, n_visit, per_dev).transpose(1, 2, 0)
    pos_lanes = jnp.take(pos_lanes, bit_reverse(jnp.arange(n_visit), bits) ^ me_visit, axis=0)
    pos_lanes = jnp.concatenate(
        [pos_lanes, jnp.zeros((n_visit, per_dev, tile - GRID), jnp.float32)], axis=2
    ).reshape(n_visit, 1, per_dev * tile)
    psf_row = jnp.concatenate(
        [psf_part, weight_part[None], jnp.zeros((per_dev * tile - BASIS - 1,), jnp.float32)]
    )
    extra = jnp.concatenate(
        [
            pos_lanes,
            jnp.broadcast_to(psf_row[None, None, :], (n_visit, 1, per_dev * tile)),
            jnp.zeros((n_visit, EXTRA - 2, per_dev * tile), jnp.float32),
        ],
        axis=1,
    )
    var_pos = variance_field(
        where, weight * weight, got_vm, extra, (n_visit, GRID * tile + EXTRA, per_dev * tile)
    )
    var_share = reduce_scatter_visit(var_pos, n_visit)

    low = held_most // 2
    part_a = lax.all_to_all(send_im[:, :low], "sky", split_axis=0, concat_axis=0, tiled=True)
    var_share, part_a, send_b = lax.optimization_barrier((var_share, part_a, send_im[:, low:]))
    part_b = lax.all_to_all(send_b, "sky", split_axis=0, concat_axis=0, tiled=True)
    source = (me - jnp.arange(n_sky)) % n_sky

    def by_source(values, lower, upper):
        values = jnp.take(values.reshape(n_sky, held_most, -1), source, axis=0)
        return values[:, lower:upper].reshape(n_sky * (upper - lower), -1)

    field_shape = (n_visit, GRID * tile, per_dev * tile)
    image_pos = None
    for lower, upper, part in ((0, low, part_a), (low, held_most, part_b)):
        image_pos = image_field(
            tuple(by_source(values, lower, upper)[:, 0] for values in where),
            by_source(weight, lower, upper)[:, 0],
            by_source(got_coef, lower, upper).reshape(-1),
            part.reshape(n_sky * (upper - lower), tile, tile),
            row_side, col_side, field_shape, image_pos,
        )
    image_share = reduce_scatter_visit(image_pos, n_visit)

    body_rows = GRID * tile
    pos_weight = var_share[body_rows, :].reshape(per_dev, tile)[:, :GRID]
    denom = jnp.maximum(pos_weight, weight_floor).T
    denom = jnp.broadcast_to(denom[:, None, :, None], (GRID, tile, per_dev, tile))
    denom = denom.reshape(body_rows, per_dev * tile)
    coadd_image = image_share / denom
    coadd_variance = var_share[:body_rows, :] / (denom * denom)

    psf_total = var_share[body_rows + 1, :BASIS]
    weight_total = var_share[body_rows + 1, BASIS]
    share = psf_total / weight_total
    high = lax.Precision.HIGHEST
    coadd_psf = jnp.einsum(
        "k,ka,kb->ab",
        share,
        col_taps.astype(jnp.float32),
        row_taps.astype(jnp.float32),
        precision=high,
    )[None]
    return (coadd_image, coadd_variance, coadd_psf)


def solution(mesh):
    return jax.shard_map(
        shards,
        mesh=mesh,
        in_specs=(
            P("visit", "sky", None, None),
            P("visit", "sky", None, None),
            P("visit", "sky", None),
            P("visit", "sky", None),
            P("visit", "sky"),
            P(),
            P(),
        ),
        out_specs=(P("sky", "visit"), P("sky", "visit"), P("sky", None, None)),
        check_vma=False,
    )
```

```python
import functools

import jax
import jax.numpy as jnp
from jax import lax
from jax.experimental import pallas as pl
from jax.experimental.pallas import tpu as pltpu
from jax.sharding import PartitionSpec as P

GRID = 8
BASIS = 9
META = 16
EXTRA = 8


weight_floor = 0.5


def band_table(taps, tile):
    span = taps.shape[1]
    offset = jnp.arange(tile)[:, None] - jnp.arange(tile)[None, :] + (span - 1) // 2
    select = (offset[None, :, :] == jnp.arange(span)[:, None, None]).astype(jnp.float32)
    return jnp.einsum("kt,tij->kij", taps.astype(jnp.float32), select).astype(jnp.bfloat16)


def place_tile(out_ref, row, group, sub, contrib):
    tile = contrib.shape[0]
    per_dev = out_ref.shape[2] // tile
    start = pl.multiple_of(row * tile, tile)
    for c in range(per_dev):

        @pl.when(sub == c)
        def _():
            out_ref[group, pl.ds(start, tile), c * tile:(c + 1) * tile] += contrib


def variance_kernel(row_ref, group_ref, sub_ref, w2_ref, *refs):
    chunks, extra_ref, out_ref = refs[:-2], refs[-2], refs[-1]
    held = chunks[0].shape[0]
    tile = chunks[0].shape[2]
    body_rows = out_ref.shape[1] - extra_ref.shape[1]
    out_ref[:, :body_rows, :] = jnp.zeros((out_ref.shape[0], body_rows, out_ref.shape[2]), jnp.float32)
    out_ref[:, body_rows:, :] = extra_ref[...]
    for d, chunk in enumerate(chunks):

        def body(r, carry):
            t = d * held + r
            row = row_ref[t]

            @pl.when(row >= 0)
            def _():
                contrib = w2_ref[t] * chunk[r, :tile, :].astype(jnp.float32)
                place_tile(out_ref, row, group_ref[t], sub_ref[t], contrib)

            return carry

        lax.fori_loop(0, held, body, 0)


def image_kernel(accumulate, order_ref, count_ref, row_ref, group_ref, sub_ref, w_ref, coef_ref,
                 img_ref, row_side_ref, col_side_ref, *refs):
    tile = img_ref.shape[2]
    out_ref = refs[-1]
    if accumulate:
        out_ref[...] = refs[0][...]
    else:
        out_ref[...] = jnp.zeros(out_ref.shape, jnp.float32)

    def body(p, carry):
        pair = (order_ref[2 * p], order_ref[2 * p + 1])
        both = jnp.concatenate([img_ref[pair[0]], img_ref[pair[1]]], axis=0)
        first = jnp.dot(both, row_side_ref[...], preferred_element_type=jnp.float32)
        blocks = []
        for k in range(BASIS):
            halves = [
                (first[h * tile:(h + 1) * tile, k * tile:(k + 1) * tile]
                 * coef_ref[pair[h] * BASIS + k]).astype(jnp.bfloat16)
                for h in range(2)
            ]
            blocks.append(jnp.concatenate(halves, axis=1))
        scaled = jnp.concatenate(blocks, axis=0)
        matched = jnp.dot(col_side_ref[...], scaled, preferred_element_type=jnp.float32)
        for h in range(2):
            t = pair[h]
            row = row_ref[t]

            @pl.when(row >= 0)
            def _():
                place_tile(out_ref, row, group_ref[t], sub_ref[t],
                           w_ref[t] * matched[:, h * tile:(h + 1) * tile])

        return carry

    lax.fori_loop(0, (count_ref[0] + 1) // 2, body, 0)


def smem():
    return pl.BlockSpec(memory_space=pltpu.SMEM)


def vmem():
    return pl.BlockSpec(memory_space=pltpu.VMEM)


def variance_field(where, w2, chunks, extra, field_shape):
    return pl.pallas_call(
        variance_kernel,
        out_shape=jax.ShapeDtypeStruct(field_shape, jnp.float32),
        in_specs=[smem()] * 4 + [vmem()] * (len(chunks) + 1),
        out_specs=vmem(),
    )(*where, w2, *chunks, extra)


def image_field(where, w, coef, images, row_side, col_side, field_shape, field=None):
    filled = where[0] >= 0
    order = jnp.argsort(jnp.logical_not(filled), stable=True).astype(jnp.int32)
    count = jnp.sum(filled.astype(jnp.int32))[None]
    args = [order, count, *where, w, coef, images, row_side, col_side]
    if field is not None:
        args.append(field)
    return pl.pallas_call(
        functools.partial(image_kernel, field is not None),
        out_shape=jax.ShapeDtypeStruct(field_shape, jnp.float32),
        in_specs=[smem()] * 7 + [vmem()] * (len(args) - 7),
        out_specs=vmem(),
        input_output_aliases={} if field is None else {len(args) - 1: 0},
        cost_estimate=pl.CostEstimate(
            flops=4 * images.shape[0] * images.shape[2] ** 3 * BASIS,
            transcendentals=0,
            bytes_accessed=images.size * 2 + 8 * (field_shape[0] * field_shape[1] * field_shape[2]),
        ),
    )(*args)


def split_exact(value):
    high = lax.reduce_precision(value, exponent_bits=8, mantissa_bits=7)
    rest = value - high
    middle = lax.reduce_precision(rest, exponent_bits=8, mantissa_bits=7)
    low = rest - middle
    return tuple(part.astype(jnp.bfloat16) for part in (high, middle, low))


def bit_reverse(values, bits):
    out = jnp.zeros_like(values)
    for b in range(bits):
        out = out | (((values >> b) & 1) << (bits - 1 - b))
    return out


def reduce_scatter_visit(field, n_visit):
    bits = n_visit.bit_length() - 1
    for b in range(bits):
        half = field.shape[0] // 2
        pairs = [(i, i ^ (1 << b)) for i in range(n_visit)]
        field = field[:half] + lax.ppermute(field[half:], "visit", perm=pairs)
    return field[0]


def shards(tile_image, tile_variance, match_coeffs, tile_patch, tile_offset, row_taps, col_taps):
    n_sky = lax.axis_size("sky")
    n_visit = lax.axis_size("visit")
    images = tile_image[0]
    variance = tile_variance[0]
    coeffs = match_coeffs[0]
    count = images.shape[0]
    tile = images.shape[1]
    held_most = max(2, 2 * count // n_sky)
    positions = GRID * GRID
    per_dev = GRID // n_visit
    dest = tile_patch[0, :, 0]
    offsets = tile_offset[0]
    band_row = band_table(row_taps, tile)
    band_col = band_table(col_taps, tile)
    row_side = band_row.transpose(1, 0, 2).reshape(tile, BASIS * tile)
    col_side = band_col.transpose(2, 0, 1).reshape(tile, BASIS * tile)
    order = jnp.arange(count)
    earlier = (dest[:, None] == dest[None, :]) & (order[None, :] < order[:, None])
    rank = jnp.sum(earlier.astype(jnp.int32), axis=1)
    slot = dest * held_most + rank
    slots_all = n_sky * held_most
    pick = (jnp.arange(slots_all)[:, None] == slot[None, :]).astype(jnp.bfloat16)
    me = lax.axis_index("sky")
    shift = (dest - me) % n_sky
    pick_shift = (jnp.arange(slots_all)[:, None] == (shift * held_most + rank)[None, :])
    weight_src = 1.0 / jnp.mean(variance.astype(jnp.float32), axis=(1, 2))
    w_parts = split_exact(weight_src)
    meta_row = jnp.concatenate(
        [coeffs, (offsets + 1).astype(jnp.bfloat16)[:, None]]
        + [part[:, None] for part in w_parts]
        + [jnp.zeros((count, tile - BASIS - 4), jnp.bfloat16)],
        axis=1,
    )
    meta = jnp.concatenate(
        [meta_row[:, None, :], jnp.zeros((count, META - 1, tile), jnp.bfloat16)], axis=1
    )
    var_meta = jnp.concatenate([variance, meta], axis=1)
    send_vm = jnp.dot(
        pick_shift.astype(jnp.bfloat16), var_meta.reshape(count, (tile + META) * tile),
        preferred_element_type=jnp.float32,
    )
    send_vm = send_vm.astype(jnp.bfloat16).reshape(n_sky, held_most, tile + META, tile)
    send_im = jnp.dot(
        pick, images.reshape(count, tile * tile), preferred_element_type=jnp.float32
    )
    send_im = send_im.astype(jnp.bfloat16).reshape(n_sky, held_most, tile, tile)

    got_vm = [send_vm[0]]
    for step in range(1, n_sky):
        pairs = [(src, (src + step) % n_sky) for src in range(n_sky)]
        got_vm.append(lax.ppermute(send_vm[step], "sky", perm=pairs))
    got_vm, send_im = lax.optimization_barrier((got_vm, send_im))
    got_meta = jnp.concatenate([chunk[:, tile, :] for chunk in got_vm]).astype(jnp.float32)
    got_coef = got_meta[:, :BASIS]
    place = got_meta[:, BASIS].astype(jnp.int32) - 1
    valid = place >= 0
    weight = (got_meta[:, BASIS + 1] + got_meta[:, BASIS + 2]) + got_meta[:, BASIS + 3]
    weight = jnp.where(valid, weight, 0.0)
    tile_row = jnp.where(valid, place // GRID, -1)
    tile_col = place % GRID
    bits = n_visit.bit_length() - 1
    me_visit = lax.axis_index("visit")
    where = (tile_row, bit_reverse((tile_col // per_dev) ^ me_visit, bits), tile_col % per_dev)
    psf_part = jnp.sum(weight[:, None] * got_coef, axis=0)
    weight_part = jnp.sum(weight)
    weight_pos = jnp.sum(
        jnp.where(jnp.arange(positions)[:, None] == place[None, :], weight[None, :], 0.0), axis=1
    )
    pos_lanes = weight_pos.reshape(GRID, n_visit, per_dev).transpose(1, 2, 0)
    pos_lanes = jnp.take(pos_lanes, bit_reverse(jnp.arange(n_visit), bits) ^ me_visit, axis=0)
    pos_lanes = jnp.concatenate(
        [pos_lanes, jnp.zeros((n_visit, per_dev, tile - GRID), jnp.float32)], axis=2
    ).reshape(n_visit, 1, per_dev * tile)
    psf_row = jnp.concatenate(
        [psf_part, weight_part[None], jnp.zeros((per_dev * tile - BASIS - 1,), jnp.float32)]
    )
    extra = jnp.concatenate(
        [
            pos_lanes,
            jnp.broadcast_to(psf_row[None, None, :], (n_visit, 1, per_dev * tile)),
            jnp.zeros((n_visit, EXTRA - 2, per_dev * tile), jnp.float32),
        ],
        axis=1,
    )
    var_pos = variance_field(
        where, weight * weight, got_vm, extra, (n_visit, GRID * tile + EXTRA, per_dev * tile)
    )
    var_share = reduce_scatter_visit(var_pos, n_visit)

    low = held_most // 2
    part_a = lax.all_to_all(send_im[:, :low], "sky", split_axis=0, concat_axis=0, tiled=True)
    part_a, send_b = lax.optimization_barrier((part_a, send_im[:, low:]))
    part_b = lax.all_to_all(send_b, "sky", split_axis=0, concat_axis=0, tiled=True)
    var_share, part_b = lax.optimization_barrier((var_share, part_b))
    source = (me - jnp.arange(n_sky)) % n_sky

    def by_source(values, lower, upper):
        values = jnp.take(values.reshape(n_sky, held_most, -1), source, axis=0)
        return values[:, lower:upper].reshape(n_sky * (upper - lower), -1)

    field_shape = (n_visit, GRID * tile, per_dev * tile)
    image_pos = None
    for lower, upper, part in ((0, low, part_a), (low, held_most, part_b)):
        image_pos = image_field(
            tuple(by_source(values, lower, upper)[:, 0] for values in where),
            by_source(weight, lower, upper)[:, 0],
            by_source(got_coef, lower, upper).reshape(-1),
            part.reshape(n_sky * (upper - lower), tile, tile),
            row_side, col_side, field_shape, image_pos,
        )
    image_share = reduce_scatter_visit(image_pos, n_visit)

    body_rows = GRID * tile
    pos_weight = var_share[body_rows, :].reshape(per_dev, tile)[:, :GRID]
    denom = jnp.maximum(pos_weight, weight_floor).T
    denom = jnp.broadcast_to(denom[:, None, :, None], (GRID, tile, per_dev, tile))
    denom = denom.reshape(body_rows, per_dev * tile)
    coadd_image = image_share / denom
    coadd_variance = var_share[:body_rows, :] / (denom * denom)

    psf_total = var_share[body_rows + 1, :BASIS]
    weight_total = var_share[body_rows + 1, BASIS]
    share = psf_total / weight_total
    high = lax.Precision.HIGHEST
    coadd_psf = jnp.einsum(
        "k,ka,kb->ab",
        share,
        col_taps.astype(jnp.float32),
        row_taps.astype(jnp.float32),
        precision=high,
    )[None]
    return (coadd_image, coadd_variance, coadd_psf)


def solution(mesh):
    return jax.shard_map(
        shards,
        mesh=mesh,
        in_specs=(
            P("visit", "sky", None, None),
            P("visit", "sky", None, None),
            P("visit", "sky", None),
            P("visit", "sky", None),
            P("visit", "sky"),
            P(),
            P(),
        ),
        out_specs=(P("sky", "visit"), P("sky", "visit"), P("sky", None, None)),
        check_vma=False,
    )
```

```python
import jax
import jax.numpy as jnp
from jax import lax
from jax.experimental import pallas as pl
from jax.experimental.pallas import tpu as pltpu
from jax.sharding import PartitionSpec as P

GRID = 8
BASIS = 9
META = 16
EXTRA = 8


weight_floor = 0.5


def band_table(taps, tile):
    span = taps.shape[1]
    offset = jnp.arange(tile)[:, None] - jnp.arange(tile)[None, :] + (span - 1) // 2
    select = (offset[None, :, :] == jnp.arange(span)[:, None, None]).astype(jnp.float32)
    return jnp.einsum("kt,tij->kij", taps.astype(jnp.float32), select).astype(jnp.bfloat16)


def place_tile(out_refs, row, group, sub, contrib):
    tile = contrib.shape[0]
    half = out_refs[0].shape[0]
    per_dev = out_refs[0].shape[2] // tile
    start = pl.multiple_of(row * tile, tile)
    for which, out_ref in enumerate(out_refs):
        for c in range(per_dev):

            @pl.when((sub == c) & (group >= which * half) & (group < (which + 1) * half))
            def _():
                out_ref[group - which * half, pl.ds(start, tile), c * tile:(c + 1) * tile] += contrib


def variance_kernel(row_ref, group_ref, sub_ref, w2_ref, *refs):
    chunks, extra_ref, out_refs = refs[:-3], refs[-3], refs[-2:]
    held = chunks[0].shape[0]
    tile = chunks[0].shape[2]
    half, height, width = out_refs[0].shape
    body_rows = height - extra_ref.shape[1]
    for which, out_ref in enumerate(out_refs):
        out_ref[:, :body_rows, :] = jnp.zeros((half, body_rows, width), jnp.float32)
        out_ref[:, body_rows:, :] = extra_ref[which * half:(which + 1) * half]
    for d, chunk in enumerate(chunks):

        def body(r, carry):
            t = d * held + r
            row = row_ref[t]

            @pl.when(row >= 0)
            def _():
                contrib = w2_ref[t] * chunk[r, :tile, :].astype(jnp.float32)
                place_tile(out_refs, row, group_ref[t], sub_ref[t], contrib)

            return carry

        lax.fori_loop(0, held, body, 0)


def image_kernel(order_ref, count_ref, row_ref, group_ref, sub_ref, w_ref, coef_ref, img_ref,
                 row_side_ref, col_side_ref, *out_refs):
    tile = img_ref.shape[2]
    for out_ref in out_refs:
        out_ref[...] = jnp.zeros(out_ref.shape, jnp.float32)

    def body(p, carry):
        pair = (order_ref[2 * p], order_ref[2 * p + 1])
        both = jnp.concatenate([img_ref[pair[0]], img_ref[pair[1]]], axis=0)
        first = jnp.dot(both, row_side_ref[...], preferred_element_type=jnp.float32)
        blocks = []
        for k in range(BASIS):
            halves = [
                (first[h * tile:(h + 1) * tile, k * tile:(k + 1) * tile]
                 * coef_ref[pair[h] * BASIS + k]).astype(jnp.bfloat16)
                for h in range(2)
            ]
            blocks.append(jnp.concatenate(halves, axis=1))
        scaled = jnp.concatenate(blocks, axis=0)
        matched = jnp.dot(col_side_ref[...], scaled, preferred_element_type=jnp.float32)
        for h in range(2):
            t = pair[h]
            row = row_ref[t]

            @pl.when(row >= 0)
            def _():
                place_tile(out_refs, row, group_ref[t], sub_ref[t],
                           w_ref[t] * matched[:, h * tile:(h + 1) * tile])

        return carry

    lax.fori_loop(0, (count_ref[0] + 1) // 2, body, 0)


def smem():
    return pl.BlockSpec(memory_space=pltpu.SMEM)


def vmem():
    return pl.BlockSpec(memory_space=pltpu.VMEM)


def halves_of(field_shape):
    half = jax.ShapeDtypeStruct((field_shape[0] // 2,) + tuple(field_shape[1:]), jnp.float32)
    return [half, half]


def variance_field(where, w2, chunks, extra, field_shape):
    return pl.pallas_call(
        variance_kernel,
        out_shape=halves_of(field_shape),
        in_specs=[smem()] * 4 + [vmem()] * (len(chunks) + 1),
        out_specs=[vmem(), vmem()],
    )(*where, w2, *chunks, extra)


def image_field(where, w, coef, images, row_side, col_side, field_shape):
    filled = where[0] >= 0
    order = jnp.argsort(jnp.logical_not(filled), stable=True).astype(jnp.int32)
    count = jnp.sum(filled.astype(jnp.int32))[None]
    return pl.pallas_call(
        image_kernel,
        out_shape=halves_of(field_shape),
        in_specs=[smem()] * 7 + [vmem()] * 3,
        out_specs=[vmem(), vmem()],
        cost_estimate=pl.CostEstimate(
            flops=4 * images.shape[0] * images.shape[2] ** 3 * BASIS,
            transcendentals=0,
            bytes_accessed=images.size * 2 + 4 * (field_shape[0] * field_shape[1] * field_shape[2]),
        ),
    )(order, count, *where, w, coef, images, row_side, col_side)


def split_exact(value):
    high = lax.reduce_precision(value, exponent_bits=8, mantissa_bits=7)
    rest = value - high
    middle = lax.reduce_precision(rest, exponent_bits=8, mantissa_bits=7)
    low = rest - middle
    return tuple(part.astype(jnp.bfloat16) for part in (high, middle, low))


def bit_reverse(values, bits):
    out = jnp.zeros_like(values)
    for b in range(bits):
        out = out | (((values >> b) & 1) << (bits - 1 - b))
    return out


def reduce_scatter_visit(halves, n_visit):
    bits = n_visit.bit_length() - 1
    keep, send = halves
    for b in range(bits):
        pairs = [(i, i ^ (1 << b)) for i in range(n_visit)]
        field = keep + lax.ppermute(send, "visit", perm=pairs)
        half = field.shape[0] // 2
        keep, send = field[:half], field[half:]
    return field[0]


def shards(tile_image, tile_variance, match_coeffs, tile_patch, tile_offset, row_taps, col_taps):
    n_sky = lax.axis_size("sky")
    n_visit = lax.axis_size("visit")
    images = tile_image[0]
    variance = tile_variance[0]
    coeffs = match_coeffs[0]
    count = images.shape[0]
    tile = images.shape[1]
    held_most = max(2, 2 * count // n_sky)
    positions = GRID * GRID
    per_dev = GRID // n_visit
    dest = tile_patch[0, :, 0]
    offsets = tile_offset[0]
    band_row = band_table(row_taps, tile)
    band_col = band_table(col_taps, tile)
    row_side = band_row.transpose(1, 0, 2).reshape(tile, BASIS * tile)
    col_side = band_col.transpose(2, 0, 1).reshape(tile, BASIS * tile)
    order = jnp.arange(count)
    earlier = (dest[:, None] == dest[None, :]) & (order[None, :] < order[:, None])
    rank = jnp.sum(earlier.astype(jnp.int32), axis=1)
    slot = dest * held_most + rank
    slots_all = n_sky * held_most
    pick = (jnp.arange(slots_all)[:, None] == slot[None, :]).astype(jnp.bfloat16)
    me = lax.axis_index("sky")
    shift = (dest - me) % n_sky
    pick_shift = (jnp.arange(slots_all)[:, None] == (shift * held_most + rank)[None, :])
    weight_src = 1.0 / jnp.mean(variance.astype(jnp.float32), axis=(1, 2))
    w_parts = split_exact(weight_src)
    meta_row = jnp.concatenate(
        [coeffs, (offsets + 1).astype(jnp.bfloat16)[:, None]]
        + [part[:, None] for part in w_parts]
        + [jnp.zeros((count, tile - BASIS - 4), jnp.bfloat16)],
        axis=1,
    )
    meta = jnp.concatenate(
        [meta_row[:, None, :], jnp.zeros((count, META - 1, tile), jnp.bfloat16)], axis=1
    )
    var_meta = jnp.concatenate([variance, meta], axis=1)
    send_vm = jnp.dot(
        pick_shift.astype(jnp.bfloat16), var_meta.reshape(count, (tile + META) * tile),
        preferred_element_type=jnp.float32,
    )
    send_vm = send_vm.astype(jnp.bfloat16).reshape(n_sky, held_most, tile + META, tile)
    send_im = jnp.dot(
        pick, images.reshape(count, tile * tile), preferred_element_type=jnp.float32
    )
    send_im = send_im.astype(jnp.bfloat16).reshape(n_sky, held_most, tile, tile)

    got_vm = [send_vm[0]]
    for step in range(1, n_sky):
        pairs = [(src, (src + step) % n_sky) for src in range(n_sky)]
        got_vm.append(lax.ppermute(send_vm[step], "sky", perm=pairs))
    got_vm, send_im = lax.optimization_barrier((got_vm, send_im))
    got_meta = jnp.concatenate([chunk[:, tile, :] for chunk in got_vm]).astype(jnp.float32)
    got_coef = got_meta[:, :BASIS]
    place = got_meta[:, BASIS].astype(jnp.int32) - 1
    valid = place >= 0
    weight = (got_meta[:, BASIS + 1] + got_meta[:, BASIS + 2]) + got_meta[:, BASIS + 3]
    weight = jnp.where(valid, weight, 0.0)
    tile_row = jnp.where(valid, place // GRID, -1)
    tile_col = place % GRID
    bits = n_visit.bit_length() - 1
    me_visit = lax.axis_index("visit")
    where = (tile_row, bit_reverse((tile_col // per_dev) ^ me_visit, bits), tile_col % per_dev)
    psf_part = jnp.sum(weight[:, None] * got_coef, axis=0)
    weight_part = jnp.sum(weight)
    weight_pos = jnp.sum(
        jnp.where(jnp.arange(positions)[:, None] == place[None, :], weight[None, :], 0.0), axis=1
    )
    pos_lanes = weight_pos.reshape(GRID, n_visit, per_dev).transpose(1, 2, 0)
    pos_lanes = jnp.take(pos_lanes, bit_reverse(jnp.arange(n_visit), bits) ^ me_visit, axis=0)
    pos_lanes = jnp.concatenate(
        [pos_lanes, jnp.zeros((n_visit, per_dev, tile - GRID), jnp.float32)], axis=2
    ).reshape(n_visit, 1, per_dev * tile)
    psf_row = jnp.concatenate(
        [psf_part, weight_part[None], jnp.zeros((per_dev * tile - BASIS - 1,), jnp.float32)]
    )
    extra = jnp.concatenate(
        [
            pos_lanes,
            jnp.broadcast_to(psf_row[None, None, :], (n_visit, 1, per_dev * tile)),
            jnp.zeros((n_visit, EXTRA - 2, per_dev * tile), jnp.float32),
        ],
        axis=1,
    )
    var_pos = variance_field(
        where, weight * weight, got_vm, extra, (n_visit, GRID * tile + EXTRA, per_dev * tile)
    )
    var_share = reduce_scatter_visit(var_pos, n_visit)

    part_im = lax.all_to_all(send_im, "sky", split_axis=0, concat_axis=0, tiled=True)
    var_share, part_im = lax.optimization_barrier((var_share, part_im))
    part_im = part_im.reshape(slots_all, tile, tile)
    source = (me - jnp.arange(n_sky)) % n_sky

    def by_source(values):
        return jnp.take(values.reshape(n_sky, held_most, -1), source, axis=0).reshape(slots_all, -1)

    im_where = tuple(by_source(values)[:, 0] for values in where)
    image_pos = image_field(
        im_where, by_source(weight)[:, 0], by_source(got_coef).reshape(slots_all * BASIS), part_im,
        row_side, col_side, (n_visit, GRID * tile, per_dev * tile),
    )
    image_share = reduce_scatter_visit(image_pos, n_visit)

    body_rows = GRID * tile
    pos_weight = var_share[body_rows, :].reshape(per_dev, tile)[:, :GRID]
    denom = jnp.maximum(pos_weight, weight_floor).T
    denom = jnp.broadcast_to(denom[:, None, :, None], (GRID, tile, per_dev, tile))
    denom = denom.reshape(body_rows, per_dev * tile)
    coadd_image = image_share / denom
    coadd_variance = var_share[:body_rows, :] / (denom * denom)

    psf_total = var_share[body_rows + 1, :BASIS]
    weight_total = var_share[body_rows + 1, BASIS]
    share = psf_total / weight_total
    high = lax.Precision.HIGHEST
    coadd_psf = jnp.einsum(
        "k,ka,kb->ab",
        share,
        col_taps.astype(jnp.float32),
        row_taps.astype(jnp.float32),
        precision=high,
    )[None]
    return (coadd_image, coadd_variance, coadd_psf)


def solution(mesh):
    return jax.shard_map(
        shards,
        mesh=mesh,
        in_specs=(
            P("visit", "sky", None, None),
            P("visit", "sky", None, None),
            P("visit", "sky", None),
            P("visit", "sky", None),
            P("visit", "sky"),
            P(),
            P(),
        ),
        out_specs=(P("sky", "visit"), P("sky", "visit"), P("sky", None, None)),
        check_vma=False,
    )
```

```python
import jax
import jax.numpy as jnp
from jax import lax
from jax.experimental import pallas as pl
from jax.experimental.pallas import tpu as pltpu
from jax.sharding import PartitionSpec as P

GRID = 8
BASIS = 9
META = 16
EXTRA = 8


weight_floor = 0.5


def band_table(taps, tile):
    span = taps.shape[1]
    offset = jnp.arange(tile)[:, None] - jnp.arange(tile)[None, :] + (span - 1) // 2
    select = (offset[None, :, :] == jnp.arange(span)[:, None, None]).astype(jnp.float32)
    return jnp.einsum("kt,tij->kij", taps.astype(jnp.float32), select).astype(jnp.bfloat16)


def place_tile(out_refs, row, group, sub, contrib):
    tile = contrib.shape[0]
    half = out_refs[0].shape[0]
    per_dev = out_refs[0].shape[2] // tile
    start = pl.multiple_of(row * tile, tile)
    for which, out_ref in enumerate(out_refs):
        for c in range(per_dev):

            @pl.when((sub == c) & (group >= which * half) & (group < (which + 1) * half))
            def _():
                out_ref[group - which * half, pl.ds(start, tile), c * tile:(c + 1) * tile] += contrib


def variance_kernel(row_ref, group_ref, sub_ref, w2_ref, *refs):
    chunks, out_refs = refs[:-2], refs[-2:]
    held = chunks[0].shape[0]
    tile = chunks[0].shape[2]
    for out_ref in out_refs:
        out_ref[...] = jnp.zeros(out_ref.shape, jnp.float32)
    for d, chunk in enumerate(chunks):

        def body(r, carry):
            t = d * held + r
            row = row_ref[t]

            @pl.when(row >= 0)
            def _():
                contrib = w2_ref[t] * chunk[r, :tile, :].astype(jnp.float32)
                place_tile(out_refs, row, group_ref[t], sub_ref[t], contrib)

            return carry

        lax.fori_loop(0, held, body, 0)


def image_kernel(order_ref, count_ref, row_ref, group_ref, sub_ref, w_ref, coef_ref, img_ref,
                 row_side_ref, col_side_ref, extra_ref, *out_refs):
    tile = img_ref.shape[2]
    half, height, width = out_refs[0].shape
    body_rows = height - extra_ref.shape[1]
    for which, out_ref in enumerate(out_refs):
        out_ref[:, :body_rows, :] = jnp.zeros((half, body_rows, width), jnp.float32)
        out_ref[:, body_rows:, :] = extra_ref[which * half:(which + 1) * half]

    def body(p, carry):
        pair = (order_ref[2 * p], order_ref[2 * p + 1])
        both = jnp.concatenate([img_ref[pair[0]], img_ref[pair[1]]], axis=0)
        first = jnp.dot(both, row_side_ref[...], preferred_element_type=jnp.float32)
        blocks = []
        for k in range(BASIS):
            halves = [
                (first[h * tile:(h + 1) * tile, k * tile:(k + 1) * tile]
                 * coef_ref[pair[h] * BASIS + k]).astype(jnp.bfloat16)
                for h in range(2)
            ]
            blocks.append(jnp.concatenate(halves, axis=1))
        scaled = jnp.concatenate(blocks, axis=0)
        matched = jnp.dot(col_side_ref[...], scaled, preferred_element_type=jnp.float32)
        for h in range(2):
            t = pair[h]
            row = row_ref[t]

            @pl.when(row >= 0)
            def _():
                place_tile(out_refs, row, group_ref[t], sub_ref[t],
                           w_ref[t] * matched[:, h * tile:(h + 1) * tile])

        return carry

    lax.fori_loop(0, (count_ref[0] + 1) // 2, body, 0)


def smem():
    return pl.BlockSpec(memory_space=pltpu.SMEM)


def vmem():
    return pl.BlockSpec(memory_space=pltpu.VMEM)


def halves_of(field_shape):
    half = jax.ShapeDtypeStruct((field_shape[0] // 2,) + tuple(field_shape[1:]), jnp.float32)
    return [half, half]


def variance_field(where, w2, chunks, field_shape):
    return pl.pallas_call(
        variance_kernel,
        out_shape=halves_of(field_shape),
        in_specs=[smem()] * 4 + [vmem()] * len(chunks),
        out_specs=[vmem(), vmem()],
    )(*where, w2, *chunks)


def image_field(where, w, coef, images, row_side, col_side, extra, field_shape):
    filled = where[0] >= 0
    order = jnp.argsort(jnp.logical_not(filled), stable=True).astype(jnp.int32)
    count = jnp.sum(filled.astype(jnp.int32))[None]
    return pl.pallas_call(
        image_kernel,
        out_shape=halves_of(field_shape),
        in_specs=[smem()] * 7 + [vmem()] * 4,
        out_specs=[vmem(), vmem()],
        cost_estimate=pl.CostEstimate(
            flops=4 * images.shape[0] * images.shape[2] ** 3 * BASIS,
            transcendentals=0,
            bytes_accessed=images.size * 2 + 4 * (field_shape[0] * field_shape[1] * field_shape[2]),
        ),
    )(order, count, *where, w, coef, images, row_side, col_side, extra)


def split_exact(value):
    high = lax.reduce_precision(value, exponent_bits=8, mantissa_bits=7)
    rest = value - high
    middle = lax.reduce_precision(rest, exponent_bits=8, mantissa_bits=7)
    low = rest - middle
    return tuple(part.astype(jnp.bfloat16) for part in (high, middle, low))


def bit_reverse(values, bits):
    out = jnp.zeros_like(values)
    for b in range(bits):
        out = out | (((values >> b) & 1) << (bits - 1 - b))
    return out


def reduce_scatter_visit(halves, n_visit):
    bits = n_visit.bit_length() - 1
    keep, send = halves
    for b in range(bits):
        pairs = [(i, i ^ (1 << b)) for i in range(n_visit)]
        field = keep + lax.ppermute(send, "visit", perm=pairs)
        half = field.shape[0] // 2
        keep, send = field[:half], field[half:]
    return field[0]


def shards(tile_image, tile_variance, match_coeffs, tile_patch, tile_offset, row_taps, col_taps):
    n_sky = lax.axis_size("sky")
    n_visit = lax.axis_size("visit")
    images = tile_image[0]
    variance = tile_variance[0]
    coeffs = match_coeffs[0]
    count = images.shape[0]
    tile = images.shape[1]
    held_most = max(2, 2 * count // n_sky)
    positions = GRID * GRID
    per_dev = GRID // n_visit
    dest = tile_patch[0, :, 0]
    offsets = tile_offset[0]
    band_row = band_table(row_taps, tile)
    band_col = band_table(col_taps, tile)
    row_side = band_row.transpose(1, 0, 2).reshape(tile, BASIS * tile)
    col_side = band_col.transpose(2, 0, 1).reshape(tile, BASIS * tile)
    order = jnp.arange(count)
    earlier = (dest[:, None] == dest[None, :]) & (order[None, :] < order[:, None])
    rank = jnp.sum(earlier.astype(jnp.int32), axis=1)
    slot = dest * held_most + rank
    slots_all = n_sky * held_most
    pick = (jnp.arange(slots_all)[:, None] == slot[None, :]).astype(jnp.bfloat16)
    me = lax.axis_index("sky")
    shift = (dest - me) % n_sky
    pick_shift = (jnp.arange(slots_all)[:, None] == (shift * held_most + rank)[None, :])
    weight_src = 1.0 / jnp.mean(variance.astype(jnp.float32), axis=(1, 2))
    w_parts = split_exact(weight_src)
    meta_row = jnp.concatenate(
        [coeffs, (offsets + 1).astype(jnp.bfloat16)[:, None]]
        + [part[:, None] for part in w_parts]
        + [jnp.zeros((count, tile - BASIS - 4), jnp.bfloat16)],
        axis=1,
    )
    meta = jnp.concatenate(
        [meta_row[:, None, :], jnp.zeros((count, META - 1, tile), jnp.bfloat16)], axis=1
    )
    var_meta = jnp.concatenate([variance, meta], axis=1)
    send_vm = jnp.dot(
        pick_shift.astype(jnp.bfloat16), var_meta.reshape(count, (tile + META) * tile),
        preferred_element_type=jnp.float32,
    )
    send_vm = send_vm.astype(jnp.bfloat16).reshape(n_sky, held_most, tile + META, tile)
    send_im = jnp.dot(
        pick, images.reshape(count, tile * tile), preferred_element_type=jnp.float32
    )
    send_im = send_im.astype(jnp.bfloat16).reshape(n_sky, held_most, tile, tile)

    got_vm = [send_vm[0]]
    for step in range(1, n_sky):
        pairs = [(src, (src + step) % n_sky) for src in range(n_sky)]
        got_vm.append(lax.ppermute(send_vm[step], "sky", perm=pairs))
    got_vm, send_im = lax.optimization_barrier((got_vm, send_im))
    got_meta = jnp.concatenate([chunk[:, tile, :] for chunk in got_vm]).astype(jnp.float32)
    got_coef = got_meta[:, :BASIS]
    place = got_meta[:, BASIS].astype(jnp.int32) - 1
    valid = place >= 0
    weight = (got_meta[:, BASIS + 1] + got_meta[:, BASIS + 2]) + got_meta[:, BASIS + 3]
    weight = jnp.where(valid, weight, 0.0)
    tile_row = jnp.where(valid, place // GRID, -1)
    tile_col = place % GRID
    bits = n_visit.bit_length() - 1
    me_visit = lax.axis_index("visit")
    where = (tile_row, bit_reverse((tile_col // per_dev) ^ me_visit, bits), tile_col % per_dev)
    psf_part = jnp.sum(weight[:, None] * got_coef, axis=0)
    weight_part = jnp.sum(weight)
    weight_pos = jnp.sum(
        jnp.where(jnp.arange(positions)[:, None] == place[None, :], weight[None, :], 0.0), axis=1
    )
    pos_lanes = weight_pos.reshape(GRID, n_visit, per_dev).transpose(1, 2, 0)
    pos_lanes = jnp.take(pos_lanes, bit_reverse(jnp.arange(n_visit), bits) ^ me_visit, axis=0)
    pos_lanes = jnp.concatenate(
        [pos_lanes, jnp.zeros((n_visit, per_dev, tile - GRID), jnp.float32)], axis=2
    ).reshape(n_visit, 1, per_dev * tile)
    psf_row = jnp.concatenate(
        [psf_part, weight_part[None], jnp.zeros((per_dev * tile - BASIS - 1,), jnp.float32)]
    )
    extra = jnp.concatenate(
        [
            pos_lanes,
            jnp.broadcast_to(psf_row[None, None, :], (n_visit, 1, per_dev * tile)),
            jnp.zeros((n_visit, EXTRA - 2, per_dev * tile), jnp.float32),
        ],
        axis=1,
    )
    var_pos = variance_field(
        where, weight * weight, got_vm, (n_visit, GRID * tile, per_dev * tile)
    )
    var_share = reduce_scatter_visit(var_pos, n_visit)

    part_im = lax.all_to_all(send_im, "sky", split_axis=0, concat_axis=0, tiled=True)
    var_share, part_im = lax.optimization_barrier((var_share, part_im))
    part_im = part_im.reshape(slots_all, tile, tile)
    source = (me - jnp.arange(n_sky)) % n_sky

    def by_source(values):
        return jnp.take(values.reshape(n_sky, held_most, -1), source, axis=0).reshape(slots_all, -1)

    im_where = tuple(by_source(values)[:, 0] for values in where)
    image_pos = image_field(
        im_where, by_source(weight)[:, 0], by_source(got_coef).reshape(slots_all * BASIS), part_im,
        row_side, col_side, extra, (n_visit, GRID * tile + EXTRA, per_dev * tile),
    )
    image_share = reduce_scatter_visit(image_pos, n_visit)

    body_rows = GRID * tile
    pos_weight = image_share[body_rows, :].reshape(per_dev, tile)[:, :GRID]
    denom = jnp.maximum(pos_weight, weight_floor).T
    denom = jnp.broadcast_to(denom[:, None, :, None], (GRID, tile, per_dev, tile))
    denom = denom.reshape(body_rows, per_dev * tile)
    coadd_image = image_share[:body_rows, :] / denom
    coadd_variance = var_share / (denom * denom)

    psf_total = image_share[body_rows + 1, :BASIS]
    weight_total = image_share[body_rows + 1, BASIS]
    share = psf_total / weight_total
    high = lax.Precision.HIGHEST
    coadd_psf = jnp.einsum(
        "k,ka,kb->ab",
        share,
        col_taps.astype(jnp.float32),
        row_taps.astype(jnp.float32),
        precision=high,
    )[None]
    return (coadd_image, coadd_variance, coadd_psf)


def solution(mesh):
    return jax.shard_map(
        shards,
        mesh=mesh,
        in_specs=(
            P("visit", "sky", None, None),
            P("visit", "sky", None, None),
            P("visit", "sky", None),
            P("visit", "sky", None),
            P("visit", "sky"),
            P(),
            P(),
        ),
        out_specs=(P("sky", "visit"), P("sky", "visit"), P("sky", None, None)),
        check_vma=False,
    )
```

```python
import jax
import jax.numpy as jnp
from jax import lax
from jax.experimental import pallas as pl
from jax.experimental.pallas import tpu as pltpu
from jax.sharding import PartitionSpec as P

GRID = 8
BASIS = 9
META = 16
EXTRA = 8


weight_floor = 0.5


def band_table(taps, tile):
    span = taps.shape[1]
    offset = jnp.arange(tile)[:, None] - jnp.arange(tile)[None, :] + (span - 1) // 2
    select = (offset[None, :, :] == jnp.arange(span)[:, None, None]).astype(jnp.float32)
    return jnp.einsum("kt,tij->kij", taps.astype(jnp.float32), select).astype(jnp.bfloat16)


def place_tile(out_refs, row, group, sub, contrib):
    tile = contrib.shape[0]
    half = out_refs[0].shape[0]
    per_dev = out_refs[0].shape[2] // tile
    start = pl.multiple_of(row * tile, tile)
    for which, out_ref in enumerate(out_refs):
        for c in range(per_dev):

            @pl.when((sub == c) & (group >= which * half) & (group < (which + 1) * half))
            def _():
                out_ref[group - which * half, pl.ds(start, tile), c * tile:(c + 1) * tile] += contrib


def variance_kernel(row_ref, group_ref, sub_ref, w2_ref, *refs):
    chunks, out_refs = refs[:-2], refs[-2:]
    held = chunks[0].shape[0]
    tile = chunks[0].shape[2]
    for out_ref in out_refs:
        out_ref[...] = jnp.zeros(out_ref.shape, jnp.float32)
    for d, chunk in enumerate(chunks):

        def body(r, carry):
            t = d * held + r
            row = row_ref[t]

            @pl.when(row >= 0)
            def _():
                contrib = w2_ref[t] * chunk[r, :tile, :].astype(jnp.float32)
                place_tile(out_refs, row, group_ref[t], sub_ref[t], contrib)

            return carry

        lax.fori_loop(0, held, body, 0)


def image_kernel(order_ref, count_ref, row_ref, group_ref, sub_ref, w_ref, coef_ref, img_ref,
                 row_side_ref, col_side_ref, extra_ref, *out_refs):
    tile = img_ref.shape[2]
    half, height, width = out_refs[0].shape
    body_rows = height - extra_ref.shape[1]
    for which, out_ref in enumerate(out_refs):
        out_ref[:, :body_rows, :] = jnp.zeros((half, body_rows, width), jnp.float32)
        out_ref[:, body_rows:, :] = extra_ref[which * half:(which + 1) * half]

    def body(p, carry):
        pair = (order_ref[2 * p], order_ref[2 * p + 1])
        both = jnp.concatenate([img_ref[pair[0]], img_ref[pair[1]]], axis=0)
        first = jnp.dot(both, row_side_ref[...], preferred_element_type=jnp.float32)
        blocks = []
        for k in range(BASIS):
            halves = [
                (first[h * tile:(h + 1) * tile, k * tile:(k + 1) * tile]
                 * coef_ref[pair[h] * BASIS + k]).astype(jnp.bfloat16)
                for h in range(2)
            ]
            blocks.append(jnp.concatenate(halves, axis=1))
        scaled = jnp.concatenate(blocks, axis=0)
        matched = jnp.dot(col_side_ref[...], scaled, preferred_element_type=jnp.float32)
        for h in range(2):
            t = pair[h]
            row = row_ref[t]

            @pl.when(row >= 0)
            def _():
                place_tile(out_refs, row, group_ref[t], sub_ref[t],
                           w_ref[t] * matched[:, h * tile:(h + 1) * tile])

        return carry

    lax.fori_loop(0, (count_ref[0] + 1) // 2, body, 0)


def smem():
    return pl.BlockSpec(memory_space=pltpu.SMEM)


def vmem():
    return pl.BlockSpec(memory_space=pltpu.VMEM)


def halves_of(field_shape):
    half = jax.ShapeDtypeStruct((field_shape[0] // 2,) + tuple(field_shape[1:]), jnp.float32)
    return [half, half]


def variance_field(where, w2, chunks, field_shape):
    return pl.pallas_call(
        variance_kernel,
        out_shape=halves_of(field_shape),
        in_specs=[smem()] * 4 + [vmem()] * len(chunks),
        out_specs=[vmem(), vmem()],
    )(*where, w2, *chunks)


def image_field(where, w, coef, images, row_side, col_side, extra, field_shape):
    filled = where[0] >= 0
    order = jnp.argsort(jnp.logical_not(filled), stable=True).astype(jnp.int32)
    count = jnp.sum(filled.astype(jnp.int32))[None]
    return pl.pallas_call(
        image_kernel,
        out_shape=halves_of(field_shape),
        in_specs=[smem()] * 7 + [vmem()] * 4,
        out_specs=[vmem(), vmem()],
        cost_estimate=pl.CostEstimate(
            flops=4 * images.shape[0] * images.shape[2] ** 3 * BASIS,
            transcendentals=0,
            bytes_accessed=images.size * 2 + 4 * (field_shape[0] * field_shape[1] * field_shape[2]),
        ),
    )(order, count, *where, w, coef, images, row_side, col_side, extra)


def split_exact(value):
    high = lax.reduce_precision(value, exponent_bits=8, mantissa_bits=7)
    rest = value - high
    middle = lax.reduce_precision(rest, exponent_bits=8, mantissa_bits=7)
    low = rest - middle
    return tuple(part.astype(jnp.bfloat16) for part in (high, middle, low))


def bit_reverse(values, bits):
    out = jnp.zeros_like(values)
    for b in range(bits):
        out = out | (((values >> b) & 1) << (bits - 1 - b))
    return out


def reduce_scatter_visit(halves, n_visit):
    bits = n_visit.bit_length() - 1
    keep, send = halves
    for b in range(bits):
        pairs = [(i, i ^ (1 << b)) for i in range(n_visit)]
        field = keep + lax.ppermute(send, "visit", perm=pairs)
        half = field.shape[0] // 2
        keep, send = field[:half], field[half:]
    return field[0]


def shards(tile_image, tile_variance, match_coeffs, tile_patch, tile_offset, row_taps, col_taps):
    n_sky = lax.axis_size("sky")
    n_visit = lax.axis_size("visit")
    images = tile_image[0]
    variance = tile_variance[0]
    coeffs = match_coeffs[0]
    count = images.shape[0]
    tile = images.shape[1]
    held_most = max(2, 2 * count // n_sky)
    positions = GRID * GRID
    per_dev = GRID // n_visit
    dest = tile_patch[0, :, 0]
    offsets = tile_offset[0]
    band_row = band_table(row_taps, tile)
    band_col = band_table(col_taps, tile)
    row_side = band_row.transpose(1, 0, 2).reshape(tile, BASIS * tile)
    col_side = band_col.transpose(2, 0, 1).reshape(tile, BASIS * tile)
    order = jnp.arange(count)
    earlier = (dest[:, None] == dest[None, :]) & (order[None, :] < order[:, None])
    rank = jnp.sum(earlier.astype(jnp.int32), axis=1)
    slot = dest * held_most + rank
    slots_all = n_sky * held_most
    pick = (jnp.arange(slots_all)[:, None] == slot[None, :]).astype(jnp.bfloat16)
    weight_src = 1.0 / jnp.mean(variance.astype(jnp.float32), axis=(1, 2))
    w_parts = split_exact(weight_src)
    meta_row = jnp.concatenate(
        [coeffs, (offsets + 1).astype(jnp.bfloat16)[:, None]]
        + [part[:, None] for part in w_parts]
        + [jnp.zeros((count, tile - BASIS - 4), jnp.bfloat16)],
        axis=1,
    )
    meta = jnp.concatenate(
        [meta_row[:, None, :], jnp.zeros((count, META - 1, tile), jnp.bfloat16)], axis=1
    )
    var_meta = jnp.concatenate([variance, meta], axis=1)
    send_vm = jnp.dot(
        pick, var_meta.reshape(count, (tile + META) * tile),
        preferred_element_type=jnp.float32,
    )
    send_vm = send_vm.astype(jnp.bfloat16).reshape(n_sky, held_most, tile + META, tile)
    send_im = jnp.dot(
        pick, images.reshape(count, tile * tile), preferred_element_type=jnp.float32
    )
    send_im = send_im.astype(jnp.bfloat16).reshape(n_sky, held_most, tile, tile)

    part_vm = lax.all_to_all(send_vm, "sky", split_axis=0, concat_axis=0, tiled=True)
    part_vm, send_im = lax.optimization_barrier((part_vm, send_im))
    got_vm = [part_vm.reshape(slots_all, tile + META, tile)]
    got_meta = got_vm[0][:, tile, :].astype(jnp.float32)
    got_coef = got_meta[:, :BASIS]
    place = got_meta[:, BASIS].astype(jnp.int32) - 1
    valid = place >= 0
    weight = (got_meta[:, BASIS + 1] + got_meta[:, BASIS + 2]) + got_meta[:, BASIS + 3]
    weight = jnp.where(valid, weight, 0.0)
    tile_row = jnp.where(valid, place // GRID, -1)
    tile_col = place % GRID
    bits = n_visit.bit_length() - 1
    me_visit = lax.axis_index("visit")
    where = (tile_row, bit_reverse((tile_col // per_dev) ^ me_visit, bits), tile_col % per_dev)
    psf_part = jnp.sum(weight[:, None] * got_coef, axis=0)
    weight_part = jnp.sum(weight)
    weight_pos = jnp.sum(
        jnp.where(jnp.arange(positions)[:, None] == place[None, :], weight[None, :], 0.0), axis=1
    )
    pos_lanes = weight_pos.reshape(GRID, n_visit, per_dev).transpose(1, 2, 0)
    pos_lanes = jnp.take(pos_lanes, bit_reverse(jnp.arange(n_visit), bits) ^ me_visit, axis=0)
    pos_lanes = jnp.concatenate(
        [pos_lanes, jnp.zeros((n_visit, per_dev, tile - GRID), jnp.float32)], axis=2
    ).reshape(n_visit, 1, per_dev * tile)
    psf_row = jnp.concatenate(
        [psf_part, weight_part[None], jnp.zeros((per_dev * tile - BASIS - 1,), jnp.float32)]
    )
    extra = jnp.concatenate(
        [
            pos_lanes,
            jnp.broadcast_to(psf_row[None, None, :], (n_visit, 1, per_dev * tile)),
            jnp.zeros((n_visit, EXTRA - 2, per_dev * tile), jnp.float32),
        ],
        axis=1,
    )
    var_pos = variance_field(
        where, weight * weight, got_vm, (n_visit, GRID * tile, per_dev * tile)
    )
    var_share = reduce_scatter_visit(var_pos, n_visit)

    part_im = lax.all_to_all(send_im, "sky", split_axis=0, concat_axis=0, tiled=True)
    var_share, part_im = lax.optimization_barrier((var_share, part_im))
    part_im = part_im.reshape(slots_all, tile, tile)
    image_pos = image_field(
        where, weight, got_coef.reshape(slots_all * BASIS), part_im,
        row_side, col_side, extra, (n_visit, GRID * tile + EXTRA, per_dev * tile),
    )
    image_share = reduce_scatter_visit(image_pos, n_visit)

    body_rows = GRID * tile
    pos_weight = image_share[body_rows, :].reshape(per_dev, tile)[:, :GRID]
    denom = jnp.maximum(pos_weight, weight_floor).T
    denom = jnp.broadcast_to(denom[:, None, :, None], (GRID, tile, per_dev, tile))
    denom = denom.reshape(body_rows, per_dev * tile)
    coadd_image = image_share[:body_rows, :] / denom
    coadd_variance = var_share / (denom * denom)

    psf_total = image_share[body_rows + 1, :BASIS]
    weight_total = image_share[body_rows + 1, BASIS]
    share = psf_total / weight_total
    high = lax.Precision.HIGHEST
    coadd_psf = jnp.einsum(
        "k,ka,kb->ab",
        share,
        col_taps.astype(jnp.float32),
        row_taps.astype(jnp.float32),
        precision=high,
    )[None]
    return (coadd_image, coadd_variance, coadd_psf)


def solution(mesh):
    return jax.shard_map(
        shards,
        mesh=mesh,
        in_specs=(
            P("visit", "sky", None, None),
            P("visit", "sky", None, None),
            P("visit", "sky", None),
            P("visit", "sky", None),
            P("visit", "sky"),
            P(),
            P(),
        ),
        out_specs=(P("sky", "visit"), P("sky", "visit"), P("sky", None, None)),
        check_vma=False,
    )
```

```python
import jax
import jax.numpy as jnp
from jax import lax
from jax.experimental import pallas as pl
from jax.experimental.pallas import tpu as pltpu
from jax.sharding import PartitionSpec as P

GRID = 8
BASIS = 9
META = 16
EXTRA = 8


weight_floor = 0.5


def band_table(taps, tile):
    span = taps.shape[1]
    offset = jnp.arange(tile)[:, None] - jnp.arange(tile)[None, :] + (span - 1) // 2
    select = (offset[None, :, :] == jnp.arange(span)[:, None, None]).astype(jnp.float32)
    return jnp.einsum("kt,tij->kij", taps.astype(jnp.float32), select).astype(jnp.bfloat16)


def place_tile(out_refs, row, group, sub, contrib):
    tile = contrib.shape[0]
    half = out_refs[0].shape[0]
    per_dev = out_refs[0].shape[2] // tile
    start = pl.multiple_of(row * tile, tile)
    for which, out_ref in enumerate(out_refs):
        for c in range(per_dev):

            @pl.when((sub == c) & (group >= which * half) & (group < (which + 1) * half))
            def _():
                out_ref[group - which * half, pl.ds(start, tile), c * tile:(c + 1) * tile] += contrib


def variance_kernel(row_ref, group_ref, sub_ref, w2_ref, *refs):
    chunks, out_refs = refs[:-2], refs[-2:]
    held = chunks[0].shape[0]
    tile = chunks[0].shape[2]
    for out_ref in out_refs:
        out_ref[...] = jnp.zeros(out_ref.shape, jnp.float32)
    for d, chunk in enumerate(chunks):

        def body(r, carry):
            t = d * held + r
            row = row_ref[t]

            @pl.when(row >= 0)
            def _():
                contrib = w2_ref[t] * chunk[r, :tile, :].astype(jnp.float32)
                place_tile(out_refs, row, group_ref[t], sub_ref[t], contrib)

            return carry

        lax.fori_loop(0, held, body, 0)


def image_kernel(order_ref, count_ref, row_ref, group_ref, sub_ref, w_ref, coef_ref, img_ref,
                 row_side_ref, col_side_ref, extra_ref, *out_refs):
    tile = img_ref.shape[2]
    half, height, width = out_refs[0].shape
    body_rows = height - extra_ref.shape[1]
    for which, out_ref in enumerate(out_refs):
        out_ref[:, :body_rows, :] = jnp.zeros((half, body_rows, width), jnp.float32)
        out_ref[:, body_rows:, :] = extra_ref[which * half:(which + 1) * half]

    def body(p, carry):
        pair = (order_ref[2 * p], order_ref[2 * p + 1])
        both = jnp.concatenate([img_ref[pair[0]], img_ref[pair[1]]], axis=0)
        first = jnp.dot(both, row_side_ref[...], preferred_element_type=jnp.float32)
        blocks = []
        for k in range(BASIS):
            halves = [
                (first[h * tile:(h + 1) * tile, k * tile:(k + 1) * tile]
                 * coef_ref[pair[h] * BASIS + k]).astype(jnp.bfloat16)
                for h in range(2)
            ]
            blocks.append(jnp.concatenate(halves, axis=1))
        scaled = jnp.concatenate(blocks, axis=0)
        matched = jnp.dot(col_side_ref[...], scaled, preferred_element_type=jnp.float32)
        for h in range(2):
            t = pair[h]
            row = row_ref[t]

            @pl.when(row >= 0)
            def _():
                place_tile(out_refs, row, group_ref[t], sub_ref[t],
                           w_ref[t] * matched[:, h * tile:(h + 1) * tile])

        return carry

    lax.fori_loop(0, (count_ref[0] + 1) // 2, body, 0)


def smem():
    return pl.BlockSpec(memory_space=pltpu.SMEM)


def vmem():
    return pl.BlockSpec(memory_space=pltpu.VMEM)


def halves_of(field_shape):
    half = jax.ShapeDtypeStruct((field_shape[0] // 2,) + tuple(field_shape[1:]), jnp.float32)
    return [half, half]


def variance_field(where, w2, chunks, field_shape):
    return pl.pallas_call(
        variance_kernel,
        out_shape=halves_of(field_shape),
        in_specs=[smem()] * 4 + [vmem()] * len(chunks),
        out_specs=[vmem(), vmem()],
    )(*where, w2, *chunks)


def image_field(where, w, coef, images, row_side, col_side, extra, field_shape):
    filled = where[0] >= 0
    order = jnp.argsort(jnp.logical_not(filled), stable=True).astype(jnp.int32)
    count = jnp.sum(filled.astype(jnp.int32))[None]
    return pl.pallas_call(
        image_kernel,
        out_shape=halves_of(field_shape),
        in_specs=[smem()] * 7 + [vmem()] * 4,
        out_specs=[vmem(), vmem()],
        cost_estimate=pl.CostEstimate(
            flops=4 * images.shape[0] * images.shape[2] ** 3 * BASIS,
            transcendentals=0,
            bytes_accessed=images.size * 2 + 4 * (field_shape[0] * field_shape[1] * field_shape[2]),
        ),
    )(order, count, *where, w, coef, images, row_side, col_side, extra)


def split_exact(value):
    high = lax.reduce_precision(value, exponent_bits=8, mantissa_bits=7)
    rest = value - high
    middle = lax.reduce_precision(rest, exponent_bits=8, mantissa_bits=7)
    low = rest - middle
    return tuple(part.astype(jnp.bfloat16) for part in (high, middle, low))


def bit_reverse(values, bits):
    out = jnp.zeros_like(values)
    for b in range(bits):
        out = out | (((values >> b) & 1) << (bits - 1 - b))
    return out


def reduce_scatter_visit(halves, n_visit):
    bits = n_visit.bit_length() - 1
    keep, send = halves
    for b in range(bits):
        pairs = [(i, i ^ (1 << b)) for i in range(n_visit)]
        field = keep + lax.ppermute(send, "visit", perm=pairs)
        half = field.shape[0] // 2
        keep, send = field[:half], field[half:]
    return field[0]


def shards(tile_image, tile_variance, match_coeffs, tile_patch, tile_offset, row_taps, col_taps):
    n_sky = lax.axis_size("sky")
    n_visit = lax.axis_size("visit")
    images = tile_image[0]
    variance = tile_variance[0]
    coeffs = match_coeffs[0]
    count = images.shape[0]
    tile = images.shape[1]
    held_most = max(2, 2 * count // n_sky)
    positions = GRID * GRID
    per_dev = GRID // n_visit
    dest = tile_patch[0, :, 0]
    offsets = tile_offset[0]
    band_row = band_table(row_taps, tile)
    band_col = band_table(col_taps, tile)
    row_side = band_row.transpose(1, 0, 2).reshape(tile, BASIS * tile)
    col_side = band_col.transpose(2, 0, 1).reshape(tile, BASIS * tile)
    order = jnp.arange(count)
    earlier = (dest[:, None] == dest[None, :]) & (order[None, :] < order[:, None])
    rank = jnp.sum(earlier.astype(jnp.int32), axis=1)
    slot = dest * held_most + rank
    slots_all = n_sky * held_most
    pick = (jnp.arange(slots_all)[:, None] == slot[None, :]).astype(jnp.bfloat16)
    weight_src = 1.0 / jnp.mean(variance.astype(jnp.float32), axis=(1, 2))
    w_parts = split_exact(weight_src)
    meta_row = jnp.concatenate(
        [coeffs, (offsets + 1).astype(jnp.bfloat16)[:, None]]
        + [part[:, None] for part in w_parts]
        + [jnp.zeros((count, tile - BASIS - 4), jnp.bfloat16)],
        axis=1,
    )
    meta = jnp.concatenate(
        [meta_row[:, None, :], jnp.zeros((count, META - 1, tile), jnp.bfloat16)], axis=1
    )
    var_meta = jnp.concatenate([variance, meta], axis=1)
    taken = (jnp.arange(slots_all)[:, None] == slot[None, :]).astype(jnp.int32)
    source_tile = jnp.sum(taken * order[None, :], axis=1) + count * (1 - jnp.sum(taken, axis=1))

    def gather_slots(values):
        padded = jnp.concatenate([values, jnp.zeros((1,) + values.shape[1:], values.dtype)])
        return jnp.take(padded, source_tile, axis=0, mode="clip").reshape(
            (n_sky, held_most) + values.shape[1:]
        )

    send_vm = gather_slots(var_meta)
    send_im = gather_slots(images)

    part_vm = lax.all_to_all(send_vm, "sky", split_axis=0, concat_axis=0, tiled=True)
    part_vm, send_im = lax.optimization_barrier((part_vm, send_im))
    got_vm = [part_vm.reshape(slots_all, tile + META, tile)]
    got_meta = got_vm[0][:, tile, :].astype(jnp.float32)
    got_coef = got_meta[:, :BASIS]
    place = got_meta[:, BASIS].astype(jnp.int32) - 1
    valid = place >= 0
    weight = (got_meta[:, BASIS + 1] + got_meta[:, BASIS + 2]) + got_meta[:, BASIS + 3]
    weight = jnp.where(valid, weight, 0.0)
    tile_row = jnp.where(valid, place // GRID, -1)
    tile_col = place % GRID
    bits = n_visit.bit_length() - 1
    me_visit = lax.axis_index("visit")
    where = (tile_row, bit_reverse((tile_col // per_dev) ^ me_visit, bits), tile_col % per_dev)
    psf_part = jnp.sum(weight[:, None] * got_coef, axis=0)
    weight_part = jnp.sum(weight)
    weight_pos = jnp.sum(
        jnp.where(jnp.arange(positions)[:, None] == place[None, :], weight[None, :], 0.0), axis=1
    )
    pos_lanes = weight_pos.reshape(GRID, n_visit, per_dev).transpose(1, 2, 0)
    pos_lanes = jnp.take(pos_lanes, bit_reverse(jnp.arange(n_visit), bits) ^ me_visit, axis=0)
    pos_lanes = jnp.concatenate(
        [pos_lanes, jnp.zeros((n_visit, per_dev, tile - GRID), jnp.float32)], axis=2
    ).reshape(n_visit, 1, per_dev * tile)
    psf_row = jnp.concatenate(
        [psf_part, weight_part[None], jnp.zeros((per_dev * tile - BASIS - 1,), jnp.float32)]
    )
    extra = jnp.concatenate(
        [
            pos_lanes,
            jnp.broadcast_to(psf_row[None, None, :], (n_visit, 1, per_dev * tile)),
            jnp.zeros((n_visit, EXTRA - 2, per_dev * tile), jnp.float32),
        ],
        axis=1,
    )
    var_pos = variance_field(
        where, weight * weight, got_vm, (n_visit, GRID * tile, per_dev * tile)
    )
    var_share = reduce_scatter_visit(var_pos, n_visit)

    part_im = lax.all_to_all(send_im, "sky", split_axis=0, concat_axis=0, tiled=True)
    var_share, part_im = lax.optimization_barrier((var_share, part_im))
    part_im = part_im.reshape(slots_all, tile, tile)
    image_pos = image_field(
        where, weight, got_coef.reshape(slots_all * BASIS), part_im,
        row_side, col_side, extra, (n_visit, GRID * tile + EXTRA, per_dev * tile),
    )
    image_share = reduce_scatter_visit(image_pos, n_visit)

    body_rows = GRID * tile
    pos_weight = image_share[body_rows, :].reshape(per_dev, tile)[:, :GRID]
    denom = jnp.maximum(pos_weight, weight_floor).T
    denom = jnp.broadcast_to(denom[:, None, :, None], (GRID, tile, per_dev, tile))
    denom = denom.reshape(body_rows, per_dev * tile)
    coadd_image = image_share[:body_rows, :] / denom
    coadd_variance = var_share / (denom * denom)

    psf_total = image_share[body_rows + 1, :BASIS]
    weight_total = image_share[body_rows + 1, BASIS]
    share = psf_total / weight_total
    high = lax.Precision.HIGHEST
    coadd_psf = jnp.einsum(
        "k,ka,kb->ab",
        share,
        col_taps.astype(jnp.float32),
        row_taps.astype(jnp.float32),
        precision=high,
    )[None]
    return (coadd_image, coadd_variance, coadd_psf)


def solution(mesh):
    return jax.shard_map(
        shards,
        mesh=mesh,
        in_specs=(
            P("visit", "sky", None, None),
            P("visit", "sky", None, None),
            P("visit", "sky", None),
            P("visit", "sky", None),
            P("visit", "sky"),
            P(),
            P(),
        ),
        out_specs=(P("sky", "visit"), P("sky", "visit"), P("sky", None, None)),
        check_vma=False,
    )
```

```python
import jax
import jax.numpy as jnp
from jax import lax
from jax.experimental import pallas as pl
from jax.experimental.pallas import tpu as pltpu
from jax.sharding import PartitionSpec as P

GRID = 8
BASIS = 9
META = 16
EXTRA = 8


weight_floor = 0.5


def band_table(taps, tile):
    span = taps.shape[1]
    offset = jnp.arange(tile)[:, None] - jnp.arange(tile)[None, :] + (span - 1) // 2
    select = (offset[None, :, :] == jnp.arange(span)[:, None, None]).astype(jnp.float32)
    return jnp.einsum("kt,tij->kij", taps.astype(jnp.float32), select).astype(jnp.bfloat16)


def place_tile(out_refs, row, group, sub, contrib):
    tile = contrib.shape[0]
    half = out_refs[0].shape[0]
    per_dev = out_refs[0].shape[2] // tile
    start = pl.multiple_of(row * tile, tile)
    for which, out_ref in enumerate(out_refs):
        for c in range(per_dev):

            @pl.when((sub == c) & (group >= which * half) & (group < (which + 1) * half))
            def _():
                out_ref[group - which * half, pl.ds(start, tile), c * tile:(c + 1) * tile] += contrib


def variance_kernel(row_ref, group_ref, sub_ref, w2_ref, *refs):
    chunks, out_refs = refs[:-2], refs[-2:]
    held = chunks[0].shape[0]
    tile = chunks[0].shape[2]
    for out_ref in out_refs:
        out_ref[...] = jnp.zeros(out_ref.shape, jnp.float32)
    for d, chunk in enumerate(chunks):

        def body(r, carry):
            t = d * held + r
            row = row_ref[t]

            @pl.when(row >= 0)
            def _():
                contrib = w2_ref[t] * chunk[r, :tile, :].astype(jnp.float32)
                place_tile(out_refs, row, group_ref[t], sub_ref[t], contrib)

            return carry

        lax.fori_loop(0, held, body, 0)


def image_kernel(order_ref, count_ref, row_ref, group_ref, sub_ref, w_ref, coef_ref, img_ref,
                 row_side_ref, col_side_ref, extra_ref, *out_refs):
    tile = img_ref.shape[2]
    half, height, width = out_refs[0].shape
    body_rows = height - extra_ref.shape[1]
    for which, out_ref in enumerate(out_refs):
        out_ref[:, :body_rows, :] = jnp.zeros((half, body_rows, width), jnp.float32)
        out_ref[:, body_rows:, :] = extra_ref[which * half:(which + 1) * half]

    def body(p, carry):
        pair = (order_ref[2 * p], order_ref[2 * p + 1])
        both = jnp.concatenate([img_ref[pair[0]], img_ref[pair[1]]], axis=0)
        first = jnp.dot(both, row_side_ref[...], preferred_element_type=jnp.float32)
        blocks = []
        for k in range(BASIS):
            halves = [
                (first[h * tile:(h + 1) * tile, k * tile:(k + 1) * tile]
                 * coef_ref[pair[h] * BASIS + k]).astype(jnp.bfloat16)
                for h in range(2)
            ]
            blocks.append(jnp.concatenate(halves, axis=1))
        scaled = jnp.concatenate(blocks, axis=0)
        matched = jnp.dot(col_side_ref[...], scaled, preferred_element_type=jnp.float32)
        for h in range(2):
            t = pair[h]
            row = row_ref[t]

            @pl.when(row >= 0)
            def _():
                place_tile(out_refs, row, group_ref[t], sub_ref[t],
                           w_ref[t] * matched[:, h * tile:(h + 1) * tile])

        return carry

    lax.fori_loop(0, (count_ref[0] + 1) // 2, body, 0)


def smem():
    return pl.BlockSpec(memory_space=pltpu.SMEM)


def vmem():
    return pl.BlockSpec(memory_space=pltpu.VMEM)


def halves_of(field_shape):
    half = jax.ShapeDtypeStruct((field_shape[0] // 2,) + tuple(field_shape[1:]), jnp.float32)
    return [half, half]


def variance_field(where, w2, chunks, field_shape):
    return pl.pallas_call(
        variance_kernel,
        out_shape=halves_of(field_shape),
        in_specs=[smem()] * 4 + [vmem()] * len(chunks),
        out_specs=[vmem(), vmem()],
    )(*where, w2, *chunks)


def image_field(where, w, coef, images, row_side, col_side, extra, field_shape, parts=2):
    filled = where[0] >= 0
    order = jnp.argsort(jnp.logical_not(filled), stable=True).astype(jnp.int32)
    count = jnp.sum(filled.astype(jnp.int32))[None]
    return pl.pallas_call(
        image_kernel,
        out_shape=halves_of(field_shape) if parts == 2 else [
            jax.ShapeDtypeStruct(field_shape, jnp.float32)
        ],
        in_specs=[smem()] * 7 + [vmem()] * 4,
        out_specs=[vmem()] * parts,
        cost_estimate=pl.CostEstimate(
            flops=4 * images.shape[0] * images.shape[2] ** 3 * BASIS,
            transcendentals=0,
            bytes_accessed=images.size * 2 + 4 * (field_shape[0] * field_shape[1] * field_shape[2]),
        ),
    )(order, count, *where, w, coef, images, row_side, col_side, extra)


def split_exact(value):
    high = lax.reduce_precision(value, exponent_bits=8, mantissa_bits=7)
    rest = value - high
    middle = lax.reduce_precision(rest, exponent_bits=8, mantissa_bits=7)
    low = rest - middle
    return tuple(part.astype(jnp.bfloat16) for part in (high, middle, low))


def bit_reverse(values, bits):
    out = jnp.zeros_like(values)
    for b in range(bits):
        out = out | (((values >> b) & 1) << (bits - 1 - b))
    return out


def reduce_scatter_visit(halves, n_visit):
    bits = n_visit.bit_length() - 1
    keep, send = halves
    for b in range(bits):
        pairs = [(i, i ^ (1 << b)) for i in range(n_visit)]
        field = keep + lax.ppermute(send, "visit", perm=pairs)
        half = field.shape[0] // 2
        keep, send = field[:half], field[half:]
    return field[0]


def shards(tile_image, tile_variance, match_coeffs, tile_patch, tile_offset, row_taps, col_taps):
    n_sky = lax.axis_size("sky")
    n_visit = lax.axis_size("visit")
    images = tile_image[0]
    variance = tile_variance[0]
    coeffs = match_coeffs[0]
    count = images.shape[0]
    tile = images.shape[1]
    held_most = max(2, 2 * count // n_sky)
    positions = GRID * GRID
    per_dev = GRID // n_visit
    dest = tile_patch[0, :, 0]
    offsets = tile_offset[0]
    band_row = band_table(row_taps, tile)
    band_col = band_table(col_taps, tile)
    row_side = band_row.transpose(1, 0, 2).reshape(tile, BASIS * tile)
    col_side = band_col.transpose(2, 0, 1).reshape(tile, BASIS * tile)
    order = jnp.arange(count)
    earlier = (dest[:, None] == dest[None, :]) & (order[None, :] < order[:, None])
    rank = jnp.sum(earlier.astype(jnp.int32), axis=1)
    slot = dest * held_most + rank
    slots_all = n_sky * held_most
    pick = (jnp.arange(slots_all)[:, None] == slot[None, :]).astype(jnp.bfloat16)
    weight_src = 1.0 / jnp.mean(variance.astype(jnp.float32), axis=(1, 2))
    w_parts = split_exact(weight_src)
    meta_row = jnp.concatenate(
        [coeffs, (offsets + 1).astype(jnp.bfloat16)[:, None]]
        + [part[:, None] for part in w_parts]
        + [jnp.zeros((count, tile - BASIS - 4), jnp.bfloat16)],
        axis=1,
    )
    meta = jnp.concatenate(
        [meta_row[:, None, :], jnp.zeros((count, META - 1, tile), jnp.bfloat16)], axis=1
    )
    var_meta = jnp.concatenate([variance, meta], axis=1)
    taken = (jnp.arange(slots_all)[:, None] == slot[None, :]).astype(jnp.int32)
    source_tile = jnp.sum(taken * order[None, :], axis=1) + count * (1 - jnp.sum(taken, axis=1))

    def gather_slots(values):
        padded = jnp.concatenate([values, jnp.zeros((1,) + values.shape[1:], values.dtype)])
        return jnp.take(padded, source_tile, axis=0, mode="clip").reshape(
            (n_sky, held_most) + values.shape[1:]
        )

    send_vm = gather_slots(var_meta)
    send_im = gather_slots(images)

    part_vm = lax.all_to_all(send_vm, "sky", split_axis=0, concat_axis=0, tiled=True)
    part_vm, send_im = lax.optimization_barrier((part_vm, send_im))
    got_vm = [part_vm.reshape(slots_all, tile + META, tile)]
    got_meta = got_vm[0][:, tile, :].astype(jnp.float32)
    got_coef = got_meta[:, :BASIS]
    place = got_meta[:, BASIS].astype(jnp.int32) - 1
    valid = place >= 0
    weight = (got_meta[:, BASIS + 1] + got_meta[:, BASIS + 2]) + got_meta[:, BASIS + 3]
    weight = jnp.where(valid, weight, 0.0)
    tile_row = jnp.where(valid, place // GRID, -1)
    tile_col = place % GRID
    bits = n_visit.bit_length() - 1
    me_visit = lax.axis_index("visit")
    where = (tile_row, bit_reverse((tile_col // per_dev) ^ me_visit, bits), tile_col % per_dev)
    psf_part = jnp.sum(weight[:, None] * got_coef, axis=0)
    weight_part = jnp.sum(weight)
    weight_pos = jnp.sum(
        jnp.where(jnp.arange(positions)[:, None] == place[None, :], weight[None, :], 0.0), axis=1
    )
    pos_lanes = weight_pos.reshape(GRID, n_visit, per_dev).transpose(1, 2, 0)
    pos_lanes = jnp.take(pos_lanes, bit_reverse(jnp.arange(n_visit), bits) ^ me_visit, axis=0)
    pos_lanes = jnp.concatenate(
        [pos_lanes, jnp.zeros((n_visit, per_dev, tile - GRID), jnp.float32)], axis=2
    ).reshape(n_visit, 1, per_dev * tile)
    psf_row = jnp.concatenate(
        [psf_part, weight_part[None], jnp.zeros((per_dev * tile - BASIS - 1,), jnp.float32)]
    )
    extra = jnp.concatenate(
        [
            pos_lanes,
            jnp.broadcast_to(psf_row[None, None, :], (n_visit, 1, per_dev * tile)),
            jnp.zeros((n_visit, EXTRA - 2, per_dev * tile), jnp.float32),
        ],
        axis=1,
    )
    var_pos = variance_field(
        where, weight * weight, got_vm, (n_visit, GRID * tile, per_dev * tile)
    )
    var_share = reduce_scatter_visit(var_pos, n_visit)

    part_im = lax.all_to_all(send_im, "sky", split_axis=0, concat_axis=0, tiled=True)
    var_share, part_im = lax.optimization_barrier((var_share, part_im))
    part_im = part_im.reshape(slots_all, tile, tile)
    im_coef = got_coef.reshape(slots_all * BASIS)
    own = where[1] == 0
    others_pos = image_field(
        (jnp.where(own, -1, where[0]),) + where[1:], weight, im_coef, part_im,
        row_side, col_side, extra, (n_visit, GRID * tile + EXTRA, per_dev * tile),
    )
    own_pos = image_field(
        (jnp.where(own, where[0], -1),) + where[1:], weight, im_coef, part_im,
        row_side, col_side, jnp.zeros_like(extra[:1]), (1, GRID * tile + EXTRA, per_dev * tile),
        parts=1,
    )
    image_share = reduce_scatter_visit(others_pos, n_visit) + own_pos[0][0]

    body_rows = GRID * tile
    pos_weight = image_share[body_rows, :].reshape(per_dev, tile)[:, :GRID]
    denom = jnp.maximum(pos_weight, weight_floor).T
    denom = jnp.broadcast_to(denom[:, None, :, None], (GRID, tile, per_dev, tile))
    denom = denom.reshape(body_rows, per_dev * tile)
    coadd_image = image_share[:body_rows, :] / denom
    coadd_variance = var_share / (denom * denom)

    psf_total = image_share[body_rows + 1, :BASIS]
    weight_total = image_share[body_rows + 1, BASIS]
    share = psf_total / weight_total
    high = lax.Precision.HIGHEST
    coadd_psf = jnp.einsum(
        "k,ka,kb->ab",
        share,
        col_taps.astype(jnp.float32),
        row_taps.astype(jnp.float32),
        precision=high,
    )[None]
    return (coadd_image, coadd_variance, coadd_psf)


def solution(mesh):
    return jax.shard_map(
        shards,
        mesh=mesh,
        in_specs=(
            P("visit", "sky", None, None),
            P("visit", "sky", None, None),
            P("visit", "sky", None),
            P("visit", "sky", None),
            P("visit", "sky"),
            P(),
            P(),
        ),
        out_specs=(P("sky", "visit"), P("sky", "visit"), P("sky", None, None)),
        check_vma=False,
    )
```

```python
import jax
import jax.numpy as jnp
from jax import lax
from jax.experimental import pallas as pl
from jax.experimental.pallas import tpu as pltpu
from jax.sharding import PartitionSpec as P

GRID = 8
BASIS = 9
META = 16
EXTRA = 8


weight_floor = 0.5


def band_table(taps, tile):
    span = taps.shape[1]
    offset = jnp.arange(tile)[:, None] - jnp.arange(tile)[None, :] + (span - 1) // 2
    select = (offset[None, :, :] == jnp.arange(span)[:, None, None]).astype(jnp.float32)
    return jnp.einsum("kt,tij->kij", taps.astype(jnp.float32), select).astype(jnp.bfloat16)


def place_tile(out_refs, row, group, sub, contrib):
    tile = contrib.shape[0]
    half = out_refs[0].shape[0]
    per_dev = out_refs[0].shape[2] // tile
    start = pl.multiple_of(row * tile, tile)
    for which, out_ref in enumerate(out_refs):
        for c in range(per_dev):

            @pl.when((sub == c) & (group >= which * half) & (group < (which + 1) * half))
            def _():
                out_ref[group - which * half, pl.ds(start, tile), c * tile:(c + 1) * tile] += contrib


def variance_kernel(row_ref, group_ref, sub_ref, w2_ref, *refs):
    chunks, out_refs = refs[:-2], refs[-2:]
    held = chunks[0].shape[0]
    tile = chunks[0].shape[2]
    for out_ref in out_refs:
        out_ref[...] = jnp.zeros(out_ref.shape, jnp.float32)
    for d, chunk in enumerate(chunks):

        def body(r, carry):
            t = d * held + r
            row = row_ref[t]

            @pl.when(row >= 0)
            def _():
                contrib = w2_ref[t] * chunk[r, :tile, :].astype(jnp.float32)
                place_tile(out_refs, row, group_ref[t], sub_ref[t], contrib)

            return carry

        lax.fori_loop(0, held, body, 0)


def image_kernel(order_ref, count_ref, row_ref, group_ref, sub_ref, w_ref, coef_ref, img_ref,
                 row_side_ref, col_side_ref, extra_ref, *out_refs):
    tile = img_ref.shape[2]
    half, height, width = out_refs[0].shape
    body_rows = height - extra_ref.shape[1]
    for which, out_ref in enumerate(out_refs):
        out_ref[:, :body_rows, :] = jnp.zeros((half, body_rows, width), jnp.float32)
        out_ref[:, body_rows:, :] = extra_ref[which * half:(which + 1) * half]

    def body(p, carry):
        pair = (order_ref[2 * p], order_ref[2 * p + 1])
        both = jnp.concatenate([img_ref[pair[0]], img_ref[pair[1]]], axis=0)
        first = jnp.dot(both, row_side_ref[...], preferred_element_type=jnp.float32)
        blocks = []
        for k in range(BASIS):
            halves = [
                (first[h * tile:(h + 1) * tile, k * tile:(k + 1) * tile]
                 * coef_ref[pair[h] * BASIS + k]).astype(jnp.bfloat16)
                for h in range(2)
            ]
            blocks.append(jnp.concatenate(halves, axis=1))
        scaled = jnp.concatenate(blocks, axis=0)
        matched = jnp.dot(col_side_ref[...], scaled, preferred_element_type=jnp.float32)
        for h in range(2):
            t = pair[h]
            row = row_ref[t]

            @pl.when(row >= 0)
            def _():
                place_tile(out_refs, row, group_ref[t], sub_ref[t],
                           w_ref[t] * matched[:, h * tile:(h + 1) * tile])

        return carry

    lax.fori_loop(0, (count_ref[0] + 1) // 2, body, 0)


def smem():
    return pl.BlockSpec(memory_space=pltpu.SMEM)


def vmem():
    return pl.BlockSpec(memory_space=pltpu.VMEM)


def halves_of(field_shape):
    half = jax.ShapeDtypeStruct((field_shape[0] // 2,) + tuple(field_shape[1:]), jnp.float32)
    return [half, half]


def variance_field(where, w2, chunks, field_shape):
    return pl.pallas_call(
        variance_kernel,
        out_shape=halves_of(field_shape),
        in_specs=[smem()] * 4 + [vmem()] * len(chunks),
        out_specs=[vmem(), vmem()],
    )(*where, w2, *chunks)


def image_field(where, w, coef, images, row_side, col_side, extra, field_shape):
    filled = where[0] >= 0
    order = jnp.argsort(jnp.logical_not(filled), stable=True).astype(jnp.int32)
    count = jnp.sum(filled.astype(jnp.int32))[None]
    return pl.pallas_call(
        image_kernel,
        out_shape=halves_of(field_shape),
        in_specs=[smem()] * 7 + [vmem()] * 4,
        out_specs=[vmem(), vmem()],
        cost_estimate=pl.CostEstimate(
            flops=4 * images.shape[0] * images.shape[2] ** 3 * BASIS,
            transcendentals=0,
            bytes_accessed=images.size * 2 + 4 * (field_shape[0] * field_shape[1] * field_shape[2]),
        ),
    )(order, count, *where, w, coef, images, row_side, col_side, extra)


def bit_reverse(values, bits):
    out = jnp.zeros_like(values)
    for b in range(bits):
        out = out | (((values >> b) & 1) << (bits - 1 - b))
    return out


def reduce_scatter_visit(halves, n_visit):
    bits = n_visit.bit_length() - 1
    keep, send = halves
    for b in range(bits):
        pairs = [(i, i ^ (1 << b)) for i in range(n_visit)]
        field = keep + lax.ppermute(send, "visit", perm=pairs)
        half = field.shape[0] // 2
        keep, send = field[:half], field[half:]
    return field[0]


def shards(tile_image, tile_variance, match_coeffs, tile_patch, tile_offset, row_taps, col_taps):
    n_sky = lax.axis_size("sky")
    n_visit = lax.axis_size("visit")
    images = tile_image[0]
    variance = tile_variance[0]
    coeffs = match_coeffs[0]
    count = images.shape[0]
    tile = images.shape[1]
    held_most = max(2, 2 * count // n_sky)
    positions = GRID * GRID
    per_dev = GRID // n_visit
    dest = tile_patch[0, :, 0]
    offsets = tile_offset[0]
    band_row = band_table(row_taps, tile)
    band_col = band_table(col_taps, tile)
    row_side = band_row.transpose(1, 0, 2).reshape(tile, BASIS * tile)
    col_side = band_col.transpose(2, 0, 1).reshape(tile, BASIS * tile)
    order = jnp.arange(count)
    earlier = (dest[:, None] == dest[None, :]) & (order[None, :] < order[:, None])
    rank = jnp.sum(earlier.astype(jnp.int32), axis=1)
    slot = dest * held_most + rank
    slots_all = n_sky * held_most
    pick = (jnp.arange(slots_all)[:, None] == slot[None, :]).astype(jnp.bfloat16)
    meta_row = jnp.concatenate(
        [coeffs, (offsets + 1).astype(jnp.bfloat16)[:, None],
         jnp.zeros((count, tile - BASIS - 1), jnp.bfloat16)],
        axis=1,
    )
    meta = jnp.concatenate(
        [meta_row[:, None, :], jnp.zeros((count, META - 1, tile), jnp.bfloat16)], axis=1
    )
    var_meta = jnp.concatenate([variance, meta], axis=1)
    taken = (jnp.arange(slots_all)[:, None] == slot[None, :]).astype(jnp.int32)
    source_tile = jnp.sum(taken * order[None, :], axis=1) + count * (1 - jnp.sum(taken, axis=1))

    def gather_slots(values):
        padded = jnp.concatenate([values, jnp.zeros((1,) + values.shape[1:], values.dtype)])
        return jnp.take(padded, source_tile, axis=0, mode="clip").reshape(
            (n_sky, held_most) + values.shape[1:]
        )

    send_vm = gather_slots(var_meta)
    send_im = gather_slots(images)

    part_vm = lax.all_to_all(send_vm, "sky", split_axis=0, concat_axis=0, tiled=True)
    part_vm, send_im = lax.optimization_barrier((part_vm, send_im))
    got_vm = [part_vm.reshape(slots_all, tile + META, tile)]
    got_meta = got_vm[0][:, tile, :].astype(jnp.float32)
    got_coef = got_meta[:, :BASIS]
    place = got_meta[:, BASIS].astype(jnp.int32) - 1
    valid = place >= 0
    mean_var = jnp.mean(got_vm[0][:, :tile, :].astype(jnp.float32), axis=(1, 2))
    weight = jnp.where(valid, 1.0 / jnp.where(valid, mean_var, 1.0), 0.0)
    tile_row = jnp.where(valid, place // GRID, -1)
    tile_col = place % GRID
    bits = n_visit.bit_length() - 1
    me_visit = lax.axis_index("visit")
    where = (tile_row, bit_reverse((tile_col // per_dev) ^ me_visit, bits), tile_col % per_dev)
    psf_part = jnp.sum(weight[:, None] * got_coef, axis=0)
    weight_part = jnp.sum(weight)
    weight_pos = jnp.sum(
        jnp.where(jnp.arange(positions)[:, None] == place[None, :], weight[None, :], 0.0), axis=1
    )
    pos_lanes = weight_pos.reshape(GRID, n_visit, per_dev).transpose(1, 2, 0)
    pos_lanes = jnp.take(pos_lanes, bit_reverse(jnp.arange(n_visit), bits) ^ me_visit, axis=0)
    pos_lanes = jnp.concatenate(
        [pos_lanes, jnp.zeros((n_visit, per_dev, tile - GRID), jnp.float32)], axis=2
    ).reshape(n_visit, 1, per_dev * tile)
    psf_row = jnp.concatenate(
        [psf_part, weight_part[None], jnp.zeros((per_dev * tile - BASIS - 1,), jnp.float32)]
    )
    extra = jnp.concatenate(
        [
            pos_lanes,
            jnp.broadcast_to(psf_row[None, None, :], (n_visit, 1, per_dev * tile)),
            jnp.zeros((n_visit, EXTRA - 2, per_dev * tile), jnp.float32),
        ],
        axis=1,
    )
    var_pos = variance_field(
        where, weight * weight, got_vm, (n_visit, GRID * tile, per_dev * tile)
    )
    var_share = reduce_scatter_visit(var_pos, n_visit)

    part_im = lax.all_to_all(send_im, "sky", split_axis=0, concat_axis=0, tiled=True)
    var_share, part_im = lax.optimization_barrier((var_share, part_im))
    part_im = part_im.reshape(slots_all, tile, tile)
    image_pos = image_field(
        where, weight, got_coef.reshape(slots_all * BASIS), part_im,
        row_side, col_side, extra, (n_visit, GRID * tile + EXTRA, per_dev * tile),
    )
    image_share = reduce_scatter_visit(image_pos, n_visit)

    body_rows = GRID * tile
    pos_weight = image_share[body_rows, :].reshape(per_dev, tile)[:, :GRID]
    denom = jnp.maximum(pos_weight, weight_floor).T
    denom = jnp.broadcast_to(denom[:, None, :, None], (GRID, tile, per_dev, tile))
    denom = denom.reshape(body_rows, per_dev * tile)
    coadd_image = image_share[:body_rows, :] / denom
    coadd_variance = var_share / (denom * denom)

    psf_total = image_share[body_rows + 1, :BASIS]
    weight_total = image_share[body_rows + 1, BASIS]
    share = psf_total / weight_total
    high = lax.Precision.HIGHEST
    coadd_psf = jnp.einsum(
        "k,ka,kb->ab",
        share,
        col_taps.astype(jnp.float32),
        row_taps.astype(jnp.float32),
        precision=high,
    )[None]
    return (coadd_image, coadd_variance, coadd_psf)


def solution(mesh):
    return jax.shard_map(
        shards,
        mesh=mesh,
        in_specs=(
            P("visit", "sky", None, None),
            P("visit", "sky", None, None),
            P("visit", "sky", None),
            P("visit", "sky", None),
            P("visit", "sky"),
            P(),
            P(),
        ),
        out_specs=(P("sky", "visit"), P("sky", "visit"), P("sky", None, None)),
        check_vma=False,
    )
```

```python
import jax
import jax.numpy as jnp
from jax import lax
from jax.experimental import pallas as pl
from jax.experimental.pallas import tpu as pltpu
from jax.sharding import PartitionSpec as P

GRID = 8
BASIS = 9
META = 16
EXTRA = 8


weight_floor = 0.5


def band_table(taps, tile):
    span = taps.shape[1]
    offset = jnp.arange(tile)[:, None] - jnp.arange(tile)[None, :] + (span - 1) // 2
    select = (offset[None, :, :] == jnp.arange(span)[:, None, None]).astype(jnp.float32)
    return jnp.einsum("kt,tij->kij", taps.astype(jnp.float32), select).astype(jnp.bfloat16)


def place_tile(out_refs, row, group, sub, contrib):
    tile = contrib.shape[0]
    half = out_refs[0].shape[0]
    per_dev = out_refs[0].shape[2] // tile
    start = pl.multiple_of(row * tile, tile)
    for which, out_ref in enumerate(out_refs):
        for c in range(per_dev):

            @pl.when((sub == c) & (group >= which * half) & (group < (which + 1) * half))
            def _():
                out_ref[group - which * half, pl.ds(start, tile), c * tile:(c + 1) * tile] += contrib


def variance_kernel(row_ref, group_ref, sub_ref, w2_ref, *refs):
    chunks, out_refs = refs[:-2], refs[-2:]
    held = chunks[0].shape[0]
    tile = chunks[0].shape[2]
    for out_ref in out_refs:
        out_ref[...] = jnp.zeros(out_ref.shape, jnp.float32)
    for d, chunk in enumerate(chunks):

        def body(r, carry):
            t = d * held + r
            row = row_ref[t]

            @pl.when(row >= 0)
            def _():
                contrib = w2_ref[t] * chunk[r, :tile, :].astype(jnp.float32)
                place_tile(out_refs, row, group_ref[t], sub_ref[t], contrib)

            return carry

        lax.fori_loop(0, held, body, 0)


def image_kernel(order_ref, count_ref, row_ref, group_ref, sub_ref, w_ref, coef_ref, img_ref,
                 row_side_ref, col_side_ref, extra_ref, *refs):
    tile = img_ref.shape[2]
    out_refs = refs[-2:]
    half, height, width = out_refs[0].shape
    body_rows = height - extra_ref.shape[1]
    for which, out_ref in enumerate(out_refs):
        if len(refs) == 4:
            out_ref[...] = refs[which][...]
        else:
            out_ref[:, :body_rows, :] = jnp.zeros((half, body_rows, width), jnp.float32)
            out_ref[:, body_rows:, :] = extra_ref[which * half:(which + 1) * half]

    def body(p, carry):
        pair = (order_ref[2 * p], order_ref[2 * p + 1])
        both = jnp.concatenate([img_ref[pair[0]], img_ref[pair[1]]], axis=0)
        first = jnp.dot(both, row_side_ref[...], preferred_element_type=jnp.float32)
        blocks = []
        for k in range(BASIS):
            halves = [
                (first[h * tile:(h + 1) * tile, k * tile:(k + 1) * tile]
                 * coef_ref[pair[h] * BASIS + k]).astype(jnp.bfloat16)
                for h in range(2)
            ]
            blocks.append(jnp.concatenate(halves, axis=1))
        scaled = jnp.concatenate(blocks, axis=0)
        matched = jnp.dot(col_side_ref[...], scaled, preferred_element_type=jnp.float32)
        for h in range(2):
            t = pair[h]
            row = row_ref[t]

            @pl.when(row >= 0)
            def _():
                place_tile(out_refs, row, group_ref[t], sub_ref[t],
                           w_ref[t] * matched[:, h * tile:(h + 1) * tile])

        return carry

    lax.fori_loop(0, (count_ref[0] + 1) // 2, body, 0)


def smem():
    return pl.BlockSpec(memory_space=pltpu.SMEM)


def vmem():
    return pl.BlockSpec(memory_space=pltpu.VMEM)


def halves_of(field_shape):
    half = jax.ShapeDtypeStruct((field_shape[0] // 2,) + tuple(field_shape[1:]), jnp.float32)
    return [half, half]


def variance_field(where, w2, chunks, field_shape):
    return pl.pallas_call(
        variance_kernel,
        out_shape=halves_of(field_shape),
        in_specs=[smem()] * 4 + [vmem()] * len(chunks),
        out_specs=[vmem(), vmem()],
    )(*where, w2, *chunks)


def image_field(where, w, coef, images, row_side, col_side, extra, field_shape, field=()):
    filled = where[0] >= 0
    order = jnp.argsort(jnp.logical_not(filled), stable=True).astype(jnp.int32)
    count = jnp.sum(filled.astype(jnp.int32))[None]
    return pl.pallas_call(
        image_kernel,
        out_shape=halves_of(field_shape),
        in_specs=[smem()] * 7 + [vmem()] * (4 + len(field)),
        out_specs=[vmem(), vmem()],
        input_output_aliases={11 + i: i for i in range(len(field))},
        cost_estimate=pl.CostEstimate(
            flops=4 * images.shape[0] * images.shape[2] ** 3 * BASIS,
            transcendentals=0,
            bytes_accessed=images.size * 2 + 4 * (field_shape[0] * field_shape[1] * field_shape[2]),
        ),
    )(order, count, *where, w, coef, images, row_side, col_side, extra, *field)


def bit_reverse(values, bits):
    out = jnp.zeros_like(values)
    for b in range(bits):
        out = out | (((values >> b) & 1) << (bits - 1 - b))
    return out


def reduce_scatter_visit(halves, n_visit):
    bits = n_visit.bit_length() - 1
    keep, send = halves
    for b in range(bits):
        pairs = [(i, i ^ (1 << b)) for i in range(n_visit)]
        field = keep + lax.ppermute(send, "visit", perm=pairs)
        half = field.shape[0] // 2
        keep, send = field[:half], field[half:]
    return field[0]


def shards(tile_image, tile_variance, match_coeffs, tile_patch, tile_offset, row_taps, col_taps):
    n_sky = lax.axis_size("sky")
    n_visit = lax.axis_size("visit")
    images = tile_image[0]
    variance = tile_variance[0]
    coeffs = match_coeffs[0]
    count = images.shape[0]
    tile = images.shape[1]
    held_most = max(2, 2 * count // n_sky)
    positions = GRID * GRID
    per_dev = GRID // n_visit
    dest = tile_patch[0, :, 0]
    offsets = tile_offset[0]
    band_row = band_table(row_taps, tile)
    band_col = band_table(col_taps, tile)
    row_side = band_row.transpose(1, 0, 2).reshape(tile, BASIS * tile)
    col_side = band_col.transpose(2, 0, 1).reshape(tile, BASIS * tile)
    order = jnp.arange(count)
    earlier = (dest[:, None] == dest[None, :]) & (order[None, :] < order[:, None])
    rank = jnp.sum(earlier.astype(jnp.int32), axis=1)
    slot = dest * held_most + rank
    slots_all = n_sky * held_most
    pick = (jnp.arange(slots_all)[:, None] == slot[None, :]).astype(jnp.bfloat16)
    meta_row = jnp.concatenate(
        [coeffs, (offsets + 1).astype(jnp.bfloat16)[:, None],
         jnp.zeros((count, tile - BASIS - 1), jnp.bfloat16)],
        axis=1,
    )
    meta = jnp.concatenate(
        [meta_row[:, None, :], jnp.zeros((count, META - 1, tile), jnp.bfloat16)], axis=1
    )
    var_meta = jnp.concatenate([variance, meta], axis=1)
    taken = (jnp.arange(slots_all)[:, None] == slot[None, :]).astype(jnp.int32)
    source_tile = jnp.sum(taken * order[None, :], axis=1) + count * (1 - jnp.sum(taken, axis=1))

    def gather_slots(values):
        padded = jnp.concatenate([values, jnp.zeros((1,) + values.shape[1:], values.dtype)])
        return jnp.take(padded, source_tile, axis=0, mode="clip").reshape(
            (n_sky, held_most) + values.shape[1:]
        )

    send_vm = gather_slots(var_meta)
    send_im = gather_slots(images)

    part_vm = lax.all_to_all(send_vm, "sky", split_axis=0, concat_axis=0, tiled=True)
    part_vm, send_im = lax.optimization_barrier((part_vm, send_im))
    got_vm = [part_vm.reshape(slots_all, tile + META, tile)]
    got_meta = got_vm[0][:, tile, :].astype(jnp.float32)
    got_coef = got_meta[:, :BASIS]
    place = got_meta[:, BASIS].astype(jnp.int32) - 1
    valid = place >= 0
    mean_var = jnp.mean(got_vm[0][:, :tile, :].astype(jnp.float32), axis=(1, 2))
    weight = jnp.where(valid, 1.0 / jnp.where(valid, mean_var, 1.0), 0.0)
    tile_row = jnp.where(valid, place // GRID, -1)
    tile_col = place % GRID
    bits = n_visit.bit_length() - 1
    me_visit = lax.axis_index("visit")
    where = (tile_row, bit_reverse((tile_col // per_dev) ^ me_visit, bits), tile_col % per_dev)
    psf_part = jnp.sum(weight[:, None] * got_coef, axis=0)
    weight_part = jnp.sum(weight)
    weight_pos = jnp.sum(
        jnp.where(jnp.arange(positions)[:, None] == place[None, :], weight[None, :], 0.0), axis=1
    )
    pos_lanes = weight_pos.reshape(GRID, n_visit, per_dev).transpose(1, 2, 0)
    pos_lanes = jnp.take(pos_lanes, bit_reverse(jnp.arange(n_visit), bits) ^ me_visit, axis=0)
    pos_lanes = jnp.concatenate(
        [pos_lanes, jnp.zeros((n_visit, per_dev, tile - GRID), jnp.float32)], axis=2
    ).reshape(n_visit, 1, per_dev * tile)
    psf_row = jnp.concatenate(
        [psf_part, weight_part[None], jnp.zeros((per_dev * tile - BASIS - 1,), jnp.float32)]
    )
    extra = jnp.concatenate(
        [
            pos_lanes,
            jnp.broadcast_to(psf_row[None, None, :], (n_visit, 1, per_dev * tile)),
            jnp.zeros((n_visit, EXTRA - 2, per_dev * tile), jnp.float32),
        ],
        axis=1,
    )
    var_pos = variance_field(
        where, weight * weight, got_vm, (n_visit, GRID * tile, per_dev * tile)
    )
    var_share = reduce_scatter_visit(var_pos, n_visit)

    low = held_most // 2
    part_a = lax.all_to_all(send_im[:, :low], "sky", split_axis=0, concat_axis=0, tiled=True)
    part_a, send_b = lax.optimization_barrier((part_a, send_im[:, low:]))
    part_b = lax.all_to_all(send_b, "sky", split_axis=0, concat_axis=0, tiled=True)
    var_share, part_b = lax.optimization_barrier((var_share, part_b))

    def ranks(values, lower, upper):
        return values.reshape(n_sky, held_most, -1)[:, lower:upper].reshape(n_sky * (upper - lower), -1)

    image_pos = ()
    for lower, upper, part in ((0, low, part_a), (low, held_most, part_b)):
        image_pos = image_field(
            tuple(ranks(values, lower, upper)[:, 0] for values in where),
            ranks(weight, lower, upper)[:, 0],
            ranks(got_coef, lower, upper).reshape(-1),
            part.reshape(n_sky * (upper - lower), tile, tile),
            row_side, col_side, extra, (n_visit, GRID * tile + EXTRA, per_dev * tile), image_pos,
        )
    image_share = reduce_scatter_visit(image_pos, n_visit)

    body_rows = GRID * tile
    pos_weight = image_share[body_rows, :].reshape(per_dev, tile)[:, :GRID]
    denom = jnp.maximum(pos_weight, weight_floor).T
    denom = jnp.broadcast_to(denom[:, None, :, None], (GRID, tile, per_dev, tile))
    denom = denom.reshape(body_rows, per_dev * tile)
    coadd_image = image_share[:body_rows, :] / denom
    coadd_variance = var_share / (denom * denom)

    psf_total = image_share[body_rows + 1, :BASIS]
    weight_total = image_share[body_rows + 1, BASIS]
    share = psf_total / weight_total
    high = lax.Precision.HIGHEST
    coadd_psf = jnp.einsum(
        "k,ka,kb->ab",
        share,
        col_taps.astype(jnp.float32),
        row_taps.astype(jnp.float32),
        precision=high,
    )[None]
    return (coadd_image, coadd_variance, coadd_psf)


def solution(mesh):
    return jax.shard_map(
        shards,
        mesh=mesh,
        in_specs=(
            P("visit", "sky", None, None),
            P("visit", "sky", None, None),
            P("visit", "sky", None),
            P("visit", "sky", None),
            P("visit", "sky"),
            P(),
            P(),
        ),
        out_specs=(P("sky", "visit"), P("sky", "visit"), P("sky", None, None)),
        check_vma=False,
    )
```

```python
import jax
import jax.numpy as jnp
from jax import lax
from jax.experimental import pallas as pl
from jax.experimental.pallas import tpu as pltpu
from jax.sharding import PartitionSpec as P

GRID = 8
BASIS = 9
META = 16
EXTRA = 8


weight_floor = 0.5


def band_table(taps, tile):
    span = taps.shape[1]
    offset = jnp.arange(tile)[:, None] - jnp.arange(tile)[None, :] + (span - 1) // 2
    select = (offset[None, :, :] == jnp.arange(span)[:, None, None]).astype(jnp.float32)
    return jnp.einsum("kt,tij->kij", taps.astype(jnp.float32), select).astype(jnp.bfloat16)


def place_tile(out_refs, row, group, sub, contrib):
    tile = contrib.shape[0]
    half = out_refs[0].shape[0]
    per_dev = out_refs[0].shape[2] // tile
    start = pl.multiple_of(row * tile, tile)
    for which, out_ref in enumerate(out_refs):
        for c in range(per_dev):

            @pl.when((sub == c) & (group >= which * half) & (group < (which + 1) * half))
            def _():
                out_ref[group - which * half, pl.ds(start, tile), c * tile:(c + 1) * tile] += contrib


def variance_kernel(row_ref, group_ref, sub_ref, w2_ref, *refs):
    chunks, out_refs = refs[:-2], refs[-2:]
    held = chunks[0].shape[0]
    tile = chunks[0].shape[2]
    for out_ref in out_refs:
        out_ref[...] = jnp.zeros(out_ref.shape, jnp.float32)
    for d, chunk in enumerate(chunks):

        def body(r, carry):
            t = d * held + r
            row = row_ref[t]

            @pl.when(row >= 0)
            def _():
                contrib = w2_ref[t] * chunk[r, :tile, :].astype(jnp.float32)
                place_tile(out_refs, row, group_ref[t], sub_ref[t], contrib)

            return carry

        lax.fori_loop(0, held, body, 0)


def image_kernel(order_ref, count_ref, row_ref, group_ref, sub_ref, w_ref, coef_ref, img_ref,
                 row_side_ref, col_side_ref, extra_ref, *out_refs):
    tile = img_ref.shape[2]
    half, height, width = out_refs[0].shape
    body_rows = height - extra_ref.shape[1]
    for which, out_ref in enumerate(out_refs):
        out_ref[:, :body_rows, :] = jnp.zeros((half, body_rows, width), jnp.float32)
        out_ref[:, body_rows:, :] = extra_ref[which * half:(which + 1) * half]

    def body(p, carry):
        pair = (order_ref[2 * p], order_ref[2 * p + 1])
        both = jnp.concatenate([img_ref[pair[0]], img_ref[pair[1]]], axis=0)
        first = jnp.dot(both, row_side_ref[...], preferred_element_type=jnp.float32)
        blocks = []
        for k in range(BASIS):
            halves = [
                (first[h * tile:(h + 1) * tile, k * tile:(k + 1) * tile]
                 * coef_ref[pair[h] * BASIS + k]).astype(jnp.bfloat16)
                for h in range(2)
            ]
            blocks.append(jnp.concatenate(halves, axis=1))
        matched = jnp.dot(col_side_ref[:, :tile], blocks[0], preferred_element_type=jnp.float32)
        for k in range(1, BASIS):
            matched = matched + jnp.dot(
                col_side_ref[:, k * tile:(k + 1) * tile], blocks[k],
                preferred_element_type=jnp.float32,
            )
        for h in range(2):
            t = pair[h]
            row = row_ref[t]

            @pl.when(row >= 0)
            def _():
                place_tile(out_refs, row, group_ref[t], sub_ref[t],
                           w_ref[t] * matched[:, h * tile:(h + 1) * tile])

        return carry

    lax.fori_loop(0, (count_ref[0] + 1) // 2, body, 0)


def smem():
    return pl.BlockSpec(memory_space=pltpu.SMEM)


def vmem():
    return pl.BlockSpec(memory_space=pltpu.VMEM)


def halves_of(field_shape):
    half = jax.ShapeDtypeStruct((field_shape[0] // 2,) + tuple(field_shape[1:]), jnp.float32)
    return [half, half]


def variance_field(where, w2, chunks, field_shape):
    return pl.pallas_call(
        variance_kernel,
        out_shape=halves_of(field_shape),
        in_specs=[smem()] * 4 + [vmem()] * len(chunks),
        out_specs=[vmem(), vmem()],
    )(*where, w2, *chunks)


def image_field(where, w, coef, images, row_side, col_side, extra, field_shape):
    filled = where[0] >= 0
    order = jnp.argsort(jnp.logical_not(filled), stable=True).astype(jnp.int32)
    count = jnp.sum(filled.astype(jnp.int32))[None]
    return pl.pallas_call(
        image_kernel,
        out_shape=halves_of(field_shape),
        in_specs=[smem()] * 7 + [vmem()] * 4,
        out_specs=[vmem(), vmem()],
        cost_estimate=pl.CostEstimate(
            flops=4 * images.shape[0] * images.shape[2] ** 3 * BASIS,
            transcendentals=0,
            bytes_accessed=images.size * 2 + 4 * (field_shape[0] * field_shape[1] * field_shape[2]),
        ),
    )(order, count, *where, w, coef, images, row_side, col_side, extra)


def bit_reverse(values, bits):
    out = jnp.zeros_like(values)
    for b in range(bits):
        out = out | (((values >> b) & 1) << (bits - 1 - b))
    return out


def reduce_scatter_visit(halves, n_visit):
    bits = n_visit.bit_length() - 1
    keep, send = halves
    for b in range(bits):
        pairs = [(i, i ^ (1 << b)) for i in range(n_visit)]
        field = keep + lax.ppermute(send, "visit", perm=pairs)
        half = field.shape[0] // 2
        keep, send = field[:half], field[half:]
    return field[0]


def shards(tile_image, tile_variance, match_coeffs, tile_patch, tile_offset, row_taps, col_taps):
    n_sky = lax.axis_size("sky")
    n_visit = lax.axis_size("visit")
    images = tile_image[0]
    variance = tile_variance[0]
    coeffs = match_coeffs[0]
    count = images.shape[0]
    tile = images.shape[1]
    held_most = max(2, 2 * count // n_sky)
    positions = GRID * GRID
    per_dev = GRID // n_visit
    dest = tile_patch[0, :, 0]
    offsets = tile_offset[0]
    band_row = band_table(row_taps, tile)
    band_col = band_table(col_taps, tile)
    row_side = band_row.transpose(1, 0, 2).reshape(tile, BASIS * tile)
    col_side = band_col.transpose(2, 0, 1).reshape(tile, BASIS * tile)
    order = jnp.arange(count)
    earlier = (dest[:, None] == dest[None, :]) & (order[None, :] < order[:, None])
    rank = jnp.sum(earlier.astype(jnp.int32), axis=1)
    slot = dest * held_most + rank
    slots_all = n_sky * held_most
    pick = (jnp.arange(slots_all)[:, None] == slot[None, :]).astype(jnp.bfloat16)
    meta_row = jnp.concatenate(
        [coeffs, (offsets + 1).astype(jnp.bfloat16)[:, None],
         jnp.zeros((count, tile - BASIS - 1), jnp.bfloat16)],
        axis=1,
    )
    meta = jnp.concatenate(
        [meta_row[:, None, :], jnp.zeros((count, META - 1, tile), jnp.bfloat16)], axis=1
    )
    var_meta = jnp.concatenate([variance, meta], axis=1)
    taken = (jnp.arange(slots_all)[:, None] == slot[None, :]).astype(jnp.int32)
    source_tile = jnp.sum(taken * order[None, :], axis=1) + count * (1 - jnp.sum(taken, axis=1))

    def gather_slots(values):
        padded = jnp.concatenate([values, jnp.zeros((1,) + values.shape[1:], values.dtype)])
        return jnp.take(padded, source_tile, axis=0, mode="clip").reshape(
            (n_sky, held_most) + values.shape[1:]
        )

    send_vm = gather_slots(var_meta)
    send_im = gather_slots(images)

    part_vm = lax.all_to_all(send_vm, "sky", split_axis=0, concat_axis=0, tiled=True)
    part_vm, send_im = lax.optimization_barrier((part_vm, send_im))
    got_vm = [part_vm.reshape(slots_all, tile + META, tile)]
    got_meta = got_vm[0][:, tile, :].astype(jnp.float32)
    got_coef = got_meta[:, :BASIS]
    place = got_meta[:, BASIS].astype(jnp.int32) - 1
    valid = place >= 0
    mean_var = jnp.mean(got_vm[0][:, :tile, :].astype(jnp.float32), axis=(1, 2))
    weight = jnp.where(valid, 1.0 / jnp.where(valid, mean_var, 1.0), 0.0)
    tile_row = jnp.where(valid, place // GRID, -1)
    tile_col = place % GRID
    bits = n_visit.bit_length() - 1
    me_visit = lax.axis_index("visit")
    where = (tile_row, bit_reverse((tile_col // per_dev) ^ me_visit, bits), tile_col % per_dev)
    psf_part = jnp.sum(weight[:, None] * got_coef, axis=0)
    weight_part = jnp.sum(weight)
    weight_pos = jnp.sum(
        jnp.where(jnp.arange(positions)[:, None] == place[None, :], weight[None, :], 0.0), axis=1
    )
    pos_lanes = weight_pos.reshape(GRID, n_visit, per_dev).transpose(1, 2, 0)
    pos_lanes = jnp.take(pos_lanes, bit_reverse(jnp.arange(n_visit), bits) ^ me_visit, axis=0)
    pos_lanes = jnp.concatenate(
        [pos_lanes, jnp.zeros((n_visit, per_dev, tile - GRID), jnp.float32)], axis=2
    ).reshape(n_visit, 1, per_dev * tile)
    psf_row = jnp.concatenate(
        [psf_part, weight_part[None], jnp.zeros((per_dev * tile - BASIS - 1,), jnp.float32)]
    )
    extra = jnp.concatenate(
        [
            pos_lanes,
            jnp.broadcast_to(psf_row[None, None, :], (n_visit, 1, per_dev * tile)),
            jnp.zeros((n_visit, EXTRA - 2, per_dev * tile), jnp.float32),
        ],
        axis=1,
    )
    var_pos = variance_field(
        where, weight * weight, got_vm, (n_visit, GRID * tile, per_dev * tile)
    )
    var_share = reduce_scatter_visit(var_pos, n_visit)

    part_im = lax.all_to_all(send_im, "sky", split_axis=0, concat_axis=0, tiled=True)
    var_share, part_im = lax.optimization_barrier((var_share, part_im))
    part_im = part_im.reshape(slots_all, tile, tile)
    image_pos = image_field(
        where, weight, got_coef.reshape(slots_all * BASIS), part_im,
        row_side, col_side, extra, (n_visit, GRID * tile + EXTRA, per_dev * tile),
    )
    image_share = reduce_scatter_visit(image_pos, n_visit)

    body_rows = GRID * tile
    pos_weight = image_share[body_rows, :].reshape(per_dev, tile)[:, :GRID]
    denom = jnp.maximum(pos_weight, weight_floor).T
    denom = jnp.broadcast_to(denom[:, None, :, None], (GRID, tile, per_dev, tile))
    denom = denom.reshape(body_rows, per_dev * tile)
    coadd_image = image_share[:body_rows, :] / denom
    coadd_variance = var_share / (denom * denom)

    psf_total = image_share[body_rows + 1, :BASIS]
    weight_total = image_share[body_rows + 1, BASIS]
    share = psf_total / weight_total
    high = lax.Precision.HIGHEST
    coadd_psf = jnp.einsum(
        "k,ka,kb->ab",
        share,
        col_taps.astype(jnp.float32),
        row_taps.astype(jnp.float32),
        precision=high,
    )[None]
    return (coadd_image, coadd_variance, coadd_psf)


def solution(mesh):
    return jax.shard_map(
        shards,
        mesh=mesh,
        in_specs=(
            P("visit", "sky", None, None),
            P("visit", "sky", None, None),
            P("visit", "sky", None),
            P("visit", "sky", None),
            P("visit", "sky"),
            P(),
            P(),
        ),
        out_specs=(P("sky", "visit"), P("sky", "visit"), P("sky", None, None)),
        check_vma=False,
    )
```

```python
import jax
import jax.numpy as jnp
from jax import lax
from jax.experimental import pallas as pl
from jax.experimental.pallas import tpu as pltpu
from jax.sharding import PartitionSpec as P

GRID = 8
BASIS = 9
META = 16
EXTRA = 8
GANG = 4


weight_floor = 0.5


def band_table(taps, tile):
    span = taps.shape[1]
    offset = jnp.arange(tile)[:, None] - jnp.arange(tile)[None, :] + (span - 1) // 2
    select = (offset[None, :, :] == jnp.arange(span)[:, None, None]).astype(jnp.float32)
    return jnp.einsum("kt,tij->kij", taps.astype(jnp.float32), select).astype(jnp.bfloat16)


def place_tile(out_refs, row, group, sub, contrib):
    tile = contrib.shape[0]
    half = out_refs[0].shape[0]
    per_dev = out_refs[0].shape[2] // tile
    start = pl.multiple_of(row * tile, tile)
    for which, out_ref in enumerate(out_refs):
        for c in range(per_dev):

            @pl.when((sub == c) & (group >= which * half) & (group < (which + 1) * half))
            def _():
                out_ref[group - which * half, pl.ds(start, tile), c * tile:(c + 1) * tile] += contrib


def variance_kernel(row_ref, group_ref, sub_ref, w2_ref, *refs):
    chunks, out_refs = refs[:-2], refs[-2:]
    held = chunks[0].shape[0]
    tile = chunks[0].shape[2]
    for out_ref in out_refs:
        out_ref[...] = jnp.zeros(out_ref.shape, jnp.float32)
    for d, chunk in enumerate(chunks):

        def body(r, carry):
            t = d * held + r
            row = row_ref[t]

            @pl.when(row >= 0)
            def _():
                contrib = w2_ref[t] * chunk[r, :tile, :].astype(jnp.float32)
                place_tile(out_refs, row, group_ref[t], sub_ref[t], contrib)

            return carry

        lax.fori_loop(0, held, body, 0)


def image_kernel(order_ref, count_ref, row_ref, group_ref, sub_ref, w_ref, coef_ref, img_ref,
                 row_side_ref, col_side_ref, extra_ref, *out_refs):
    tile = img_ref.shape[2]
    half, height, width = out_refs[0].shape
    body_rows = height - extra_ref.shape[1]
    for which, out_ref in enumerate(out_refs):
        out_ref[:, :body_rows, :] = jnp.zeros((half, body_rows, width), jnp.float32)
        out_ref[:, body_rows:, :] = extra_ref[which * half:(which + 1) * half]

    def body(p, carry):
        pair = tuple(order_ref[GANG * p + h] for h in range(GANG))
        both = jnp.concatenate([img_ref[t] for t in pair], axis=0)
        first = jnp.dot(both, row_side_ref[...], preferred_element_type=jnp.float32)
        blocks = []
        for k in range(BASIS):
            halves = [
                (first[h * tile:(h + 1) * tile, k * tile:(k + 1) * tile]
                 * coef_ref[pair[h] * BASIS + k]).astype(jnp.bfloat16)
                for h in range(GANG)
            ]
            blocks.append(jnp.concatenate(halves, axis=1))
        scaled = jnp.concatenate(blocks, axis=0)
        matched = jnp.dot(col_side_ref[...], scaled, preferred_element_type=jnp.float32)
        for h in range(GANG):
            t = pair[h]
            row = row_ref[t]

            @pl.when(row >= 0)
            def _():
                place_tile(out_refs, row, group_ref[t], sub_ref[t],
                           w_ref[t] * matched[:, h * tile:(h + 1) * tile])

        return carry

    lax.fori_loop(0, (count_ref[0] + GANG - 1) // GANG, body, 0)


def smem():
    return pl.BlockSpec(memory_space=pltpu.SMEM)


def vmem():
    return pl.BlockSpec(memory_space=pltpu.VMEM)


def halves_of(field_shape):
    half = jax.ShapeDtypeStruct((field_shape[0] // 2,) + tuple(field_shape[1:]), jnp.float32)
    return [half, half]


def variance_field(where, w2, chunks, field_shape):
    return pl.pallas_call(
        variance_kernel,
        out_shape=halves_of(field_shape),
        in_specs=[smem()] * 4 + [vmem()] * len(chunks),
        out_specs=[vmem(), vmem()],
    )(*where, w2, *chunks)


def image_field(where, w, coef, images, row_side, col_side, extra, field_shape):
    filled = where[0] >= 0
    order = jnp.argsort(jnp.logical_not(filled), stable=True).astype(jnp.int32)
    count = jnp.sum(filled.astype(jnp.int32))[None]
    return pl.pallas_call(
        image_kernel,
        out_shape=halves_of(field_shape),
        in_specs=[smem()] * 7 + [vmem()] * 4,
        out_specs=[vmem(), vmem()],
        cost_estimate=pl.CostEstimate(
            flops=4 * images.shape[0] * images.shape[2] ** 3 * BASIS,
            transcendentals=0,
            bytes_accessed=images.size * 2 + 4 * (field_shape[0] * field_shape[1] * field_shape[2]),
        ),
    )(order, count, *where, w, coef, images, row_side, col_side, extra)


def bit_reverse(values, bits):
    out = jnp.zeros_like(values)
    for b in range(bits):
        out = out | (((values >> b) & 1) << (bits - 1 - b))
    return out


def reduce_scatter_visit(halves, n_visit):
    bits = n_visit.bit_length() - 1
    keep, send = halves
    for b in range(bits):
        pairs = [(i, i ^ (1 << b)) for i in range(n_visit)]
        field = keep + lax.ppermute(send, "visit", perm=pairs)
        half = field.shape[0] // 2
        keep, send = field[:half], field[half:]
    return field[0]


def shards(tile_image, tile_variance, match_coeffs, tile_patch, tile_offset, row_taps, col_taps):
    n_sky = lax.axis_size("sky")
    n_visit = lax.axis_size("visit")
    images = tile_image[0]
    variance = tile_variance[0]
    coeffs = match_coeffs[0]
    count = images.shape[0]
    tile = images.shape[1]
    held_most = max(2, 2 * count // n_sky)
    positions = GRID * GRID
    per_dev = GRID // n_visit
    dest = tile_patch[0, :, 0]
    offsets = tile_offset[0]
    band_row = band_table(row_taps, tile)
    band_col = band_table(col_taps, tile)
    row_side = band_row.transpose(1, 0, 2).reshape(tile, BASIS * tile)
    col_side = band_col.transpose(2, 0, 1).reshape(tile, BASIS * tile)
    order = jnp.arange(count)
    earlier = (dest[:, None] == dest[None, :]) & (order[None, :] < order[:, None])
    rank = jnp.sum(earlier.astype(jnp.int32), axis=1)
    slot = dest * held_most + rank
    slots_all = n_sky * held_most
    pick = (jnp.arange(slots_all)[:, None] == slot[None, :]).astype(jnp.bfloat16)
    meta_row = jnp.concatenate(
        [coeffs, (offsets + 1).astype(jnp.bfloat16)[:, None],
         jnp.zeros((count, tile - BASIS - 1), jnp.bfloat16)],
        axis=1,
    )
    meta = jnp.concatenate(
        [meta_row[:, None, :], jnp.zeros((count, META - 1, tile), jnp.bfloat16)], axis=1
    )
    var_meta = jnp.concatenate([variance, meta], axis=1)
    taken = (jnp.arange(slots_all)[:, None] == slot[None, :]).astype(jnp.int32)
    source_tile = jnp.sum(taken * order[None, :], axis=1) + count * (1 - jnp.sum(taken, axis=1))

    def gather_slots(values):
        padded = jnp.concatenate([values, jnp.zeros((1,) + values.shape[1:], values.dtype)])
        return jnp.take(padded, source_tile, axis=0, mode="clip").reshape(
            (n_sky, held_most) + values.shape[1:]
        )

    send_vm = gather_slots(var_meta)
    send_im = gather_slots(images)

    part_vm = lax.all_to_all(send_vm, "sky", split_axis=0, concat_axis=0, tiled=True)
    part_vm, send_im = lax.optimization_barrier((part_vm, send_im))
    got_vm = [part_vm.reshape(slots_all, tile + META, tile)]
    got_meta = got_vm[0][:, tile, :].astype(jnp.float32)
    got_coef = got_meta[:, :BASIS]
    place = got_meta[:, BASIS].astype(jnp.int32) - 1
    valid = place >= 0
    mean_var = jnp.mean(got_vm[0][:, :tile, :].astype(jnp.float32), axis=(1, 2))
    weight = jnp.where(valid, 1.0 / jnp.where(valid, mean_var, 1.0), 0.0)
    tile_row = jnp.where(valid, place // GRID, -1)
    tile_col = place % GRID
    bits = n_visit.bit_length() - 1
    me_visit = lax.axis_index("visit")
    where = (tile_row, bit_reverse((tile_col // per_dev) ^ me_visit, bits), tile_col % per_dev)
    psf_part = jnp.sum(weight[:, None] * got_coef, axis=0)
    weight_part = jnp.sum(weight)
    weight_pos = jnp.sum(
        jnp.where(jnp.arange(positions)[:, None] == place[None, :], weight[None, :], 0.0), axis=1
    )
    pos_lanes = weight_pos.reshape(GRID, n_visit, per_dev).transpose(1, 2, 0)
    pos_lanes = jnp.take(pos_lanes, bit_reverse(jnp.arange(n_visit), bits) ^ me_visit, axis=0)
    pos_lanes = jnp.concatenate(
        [pos_lanes, jnp.zeros((n_visit, per_dev, tile - GRID), jnp.float32)], axis=2
    ).reshape(n_visit, 1, per_dev * tile)
    psf_row = jnp.concatenate(
        [psf_part, weight_part[None], jnp.zeros((per_dev * tile - BASIS - 1,), jnp.float32)]
    )
    extra = jnp.concatenate(
        [
            pos_lanes,
            jnp.broadcast_to(psf_row[None, None, :], (n_visit, 1, per_dev * tile)),
            jnp.zeros((n_visit, EXTRA - 2, per_dev * tile), jnp.float32),
        ],
        axis=1,
    )
    var_pos = variance_field(
        where, weight * weight, got_vm, (n_visit, GRID * tile, per_dev * tile)
    )
    var_share = reduce_scatter_visit(var_pos, n_visit)

    part_im = lax.all_to_all(send_im, "sky", split_axis=0, concat_axis=0, tiled=True)
    var_share, part_im = lax.optimization_barrier((var_share, part_im))
    part_im = part_im.reshape(slots_all, tile, tile)
    image_pos = image_field(
        where, weight, got_coef.reshape(slots_all * BASIS), part_im,
        row_side, col_side, extra, (n_visit, GRID * tile + EXTRA, per_dev * tile),
    )
    image_share = reduce_scatter_visit(image_pos, n_visit)

    body_rows = GRID * tile
    pos_weight = image_share[body_rows, :].reshape(per_dev, tile)[:, :GRID]
    denom = jnp.maximum(pos_weight, weight_floor).T
    denom = jnp.broadcast_to(denom[:, None, :, None], (GRID, tile, per_dev, tile))
    denom = denom.reshape(body_rows, per_dev * tile)
    coadd_image = image_share[:body_rows, :] / denom
    coadd_variance = var_share / (denom * denom)

    psf_total = image_share[body_rows + 1, :BASIS]
    weight_total = image_share[body_rows + 1, BASIS]
    share = psf_total / weight_total
    high = lax.Precision.HIGHEST
    coadd_psf = jnp.einsum(
        "k,ka,kb->ab",
        share,
        col_taps.astype(jnp.float32),
        row_taps.astype(jnp.float32),
        precision=high,
    )[None]
    return (coadd_image, coadd_variance, coadd_psf)


def solution(mesh):
    return jax.shard_map(
        shards,
        mesh=mesh,
        in_specs=(
            P("visit", "sky", None, None),
            P("visit", "sky", None, None),
            P("visit", "sky", None),
            P("visit", "sky", None),
            P("visit", "sky"),
            P(),
            P(),
        ),
        out_specs=(P("sky", "visit"), P("sky", "visit"), P("sky", None, None)),
        check_vma=False,
    )
```

```python
import jax
import jax.numpy as jnp
from jax import lax
from jax.experimental import pallas as pl
from jax.experimental.pallas import tpu as pltpu
from jax.sharding import PartitionSpec as P

GRID = 8
BASIS = 9
META = 16
EXTRA = 8
GANG = 8


weight_floor = 0.5


def band_table(taps, tile):
    span = taps.shape[1]
    offset = jnp.arange(tile)[:, None] - jnp.arange(tile)[None, :] + (span - 1) // 2
    select = (offset[None, :, :] == jnp.arange(span)[:, None, None]).astype(jnp.float32)
    return jnp.einsum("kt,tij->kij", taps.astype(jnp.float32), select).astype(jnp.bfloat16)


def place_tile(out_refs, row, group, sub, contrib):
    tile = contrib.shape[0]
    half = out_refs[0].shape[0]
    per_dev = out_refs[0].shape[2] // tile
    start = pl.multiple_of(row * tile, tile)
    for which, out_ref in enumerate(out_refs):
        for c in range(per_dev):

            @pl.when((sub == c) & (group >= which * half) & (group < (which + 1) * half))
            def _():
                out_ref[group - which * half, pl.ds(start, tile), c * tile:(c + 1) * tile] += contrib


def variance_kernel(row_ref, group_ref, sub_ref, w2_ref, *refs):
    chunks, out_refs = refs[:-2], refs[-2:]
    held = chunks[0].shape[0]
    tile = chunks[0].shape[2]
    for out_ref in out_refs:
        out_ref[...] = jnp.zeros(out_ref.shape, jnp.float32)
    for d, chunk in enumerate(chunks):

        def body(r, carry):
            t = d * held + r
            row = row_ref[t]

            @pl.when(row >= 0)
            def _():
                contrib = w2_ref[t] * chunk[r, :tile, :].astype(jnp.float32)
                place_tile(out_refs, row, group_ref[t], sub_ref[t], contrib)

            return carry

        lax.fori_loop(0, held, body, 0)


def image_kernel(order_ref, count_ref, row_ref, group_ref, sub_ref, w_ref, coef_ref, img_ref,
                 row_side_ref, col_side_ref, extra_ref, *out_refs):
    tile = img_ref.shape[2]
    half, height, width = out_refs[0].shape
    body_rows = height - extra_ref.shape[1]
    for which, out_ref in enumerate(out_refs):
        out_ref[:, :body_rows, :] = jnp.zeros((half, body_rows, width), jnp.float32)
        out_ref[:, body_rows:, :] = extra_ref[which * half:(which + 1) * half]

    def body(p, carry):
        pair = tuple(order_ref[GANG * p + h] for h in range(GANG))
        both = jnp.concatenate([img_ref[t] for t in pair], axis=0)
        first = jnp.dot(both, row_side_ref[...], preferred_element_type=jnp.float32)
        blocks = []
        for k in range(BASIS):
            halves = [
                (first[h * tile:(h + 1) * tile, k * tile:(k + 1) * tile]
                 * coef_ref[pair[h] * BASIS + k]).astype(jnp.bfloat16)
                for h in range(GANG)
            ]
            blocks.append(jnp.concatenate(halves, axis=1))
        scaled = jnp.concatenate(blocks, axis=0)
        matched = jnp.dot(col_side_ref[...], scaled, preferred_element_type=jnp.float32)
        for h in range(GANG):
            t = pair[h]
            row = row_ref[t]

            @pl.when(row >= 0)
            def _():
                place_tile(out_refs, row, group_ref[t], sub_ref[t],
                           w_ref[t] * matched[:, h * tile:(h + 1) * tile])

        return carry

    lax.fori_loop(0, (count_ref[0] + GANG - 1) // GANG, body, 0)


def smem():
    return pl.BlockSpec(memory_space=pltpu.SMEM)


def vmem():
    return pl.BlockSpec(memory_space=pltpu.VMEM)


def halves_of(field_shape):
    half = jax.ShapeDtypeStruct((field_shape[0] // 2,) + tuple(field_shape[1:]), jnp.float32)
    return [half, half]


def variance_field(where, w2, chunks, field_shape):
    return pl.pallas_call(
        variance_kernel,
        out_shape=halves_of(field_shape),
        in_specs=[smem()] * 4 + [vmem()] * len(chunks),
        out_specs=[vmem(), vmem()],
    )(*where, w2, *chunks)


def image_field(where, w, coef, images, row_side, col_side, extra, field_shape):
    filled = where[0] >= 0
    order = jnp.argsort(jnp.logical_not(filled), stable=True).astype(jnp.int32)
    count = jnp.sum(filled.astype(jnp.int32))[None]
    return pl.pallas_call(
        image_kernel,
        out_shape=halves_of(field_shape),
        in_specs=[smem()] * 7 + [vmem()] * 4,
        out_specs=[vmem(), vmem()],
        cost_estimate=pl.CostEstimate(
            flops=4 * images.shape[0] * images.shape[2] ** 3 * BASIS,
            transcendentals=0,
            bytes_accessed=images.size * 2 + 4 * (field_shape[0] * field_shape[1] * field_shape[2]),
        ),
    )(order, count, *where, w, coef, images, row_side, col_side, extra)


def bit_reverse(values, bits):
    out = jnp.zeros_like(values)
    for b in range(bits):
        out = out | (((values >> b) & 1) << (bits - 1 - b))
    return out


def reduce_scatter_visit(halves, n_visit):
    bits = n_visit.bit_length() - 1
    keep, send = halves
    for b in range(bits):
        pairs = [(i, i ^ (1 << b)) for i in range(n_visit)]
        field = keep + lax.ppermute(send, "visit", perm=pairs)
        half = field.shape[0] // 2
        keep, send = field[:half], field[half:]
    return field[0]


def shards(tile_image, tile_variance, match_coeffs, tile_patch, tile_offset, row_taps, col_taps):
    n_sky = lax.axis_size("sky")
    n_visit = lax.axis_size("visit")
    images = tile_image[0]
    variance = tile_variance[0]
    coeffs = match_coeffs[0]
    count = images.shape[0]
    tile = images.shape[1]
    held_most = max(2, 2 * count // n_sky)
    positions = GRID * GRID
    per_dev = GRID // n_visit
    dest = tile_patch[0, :, 0]
    offsets = tile_offset[0]
    band_row = band_table(row_taps, tile)
    band_col = band_table(col_taps, tile)
    row_side = band_row.transpose(1, 0, 2).reshape(tile, BASIS * tile)
    col_side = band_col.transpose(2, 0, 1).reshape(tile, BASIS * tile)
    order = jnp.arange(count)
    earlier = (dest[:, None] == dest[None, :]) & (order[None, :] < order[:, None])
    rank = jnp.sum(earlier.astype(jnp.int32), axis=1)
    slot = dest * held_most + rank
    slots_all = n_sky * held_most
    pick = (jnp.arange(slots_all)[:, None] == slot[None, :]).astype(jnp.bfloat16)
    meta_row = jnp.concatenate(
        [coeffs, (offsets + 1).astype(jnp.bfloat16)[:, None],
         jnp.zeros((count, tile - BASIS - 1), jnp.bfloat16)],
        axis=1,
    )
    meta = jnp.concatenate(
        [meta_row[:, None, :], jnp.zeros((count, META - 1, tile), jnp.bfloat16)], axis=1
    )
    var_meta = jnp.concatenate([variance, meta], axis=1)
    taken = (jnp.arange(slots_all)[:, None] == slot[None, :]).astype(jnp.int32)
    source_tile = jnp.sum(taken * order[None, :], axis=1) + count * (1 - jnp.sum(taken, axis=1))

    def gather_slots(values):
        padded = jnp.concatenate([values, jnp.zeros((1,) + values.shape[1:], values.dtype)])
        return jnp.take(padded, source_tile, axis=0, mode="clip").reshape(
            (n_sky, held_most) + values.shape[1:]
        )

    send_vm = gather_slots(var_meta)
    send_im = gather_slots(images)

    part_vm = lax.all_to_all(send_vm, "sky", split_axis=0, concat_axis=0, tiled=True)
    part_vm, send_im = lax.optimization_barrier((part_vm, send_im))
    got_vm = [part_vm.reshape(slots_all, tile + META, tile)]
    got_meta = got_vm[0][:, tile, :].astype(jnp.float32)
    got_coef = got_meta[:, :BASIS]
    place = got_meta[:, BASIS].astype(jnp.int32) - 1
    valid = place >= 0
    mean_var = jnp.mean(got_vm[0][:, :tile, :].astype(jnp.float32), axis=(1, 2))
    weight = jnp.where(valid, 1.0 / jnp.where(valid, mean_var, 1.0), 0.0)
    tile_row = jnp.where(valid, place // GRID, -1)
    tile_col = place % GRID
    bits = n_visit.bit_length() - 1
    me_visit = lax.axis_index("visit")
    where = (tile_row, bit_reverse((tile_col // per_dev) ^ me_visit, bits), tile_col % per_dev)
    psf_part = jnp.sum(weight[:, None] * got_coef, axis=0)
    weight_part = jnp.sum(weight)
    weight_pos = jnp.sum(
        jnp.where(jnp.arange(positions)[:, None] == place[None, :], weight[None, :], 0.0), axis=1
    )
    pos_lanes = weight_pos.reshape(GRID, n_visit, per_dev).transpose(1, 2, 0)
    pos_lanes = jnp.take(pos_lanes, bit_reverse(jnp.arange(n_visit), bits) ^ me_visit, axis=0)
    pos_lanes = jnp.concatenate(
        [pos_lanes, jnp.zeros((n_visit, per_dev, tile - GRID), jnp.float32)], axis=2
    ).reshape(n_visit, 1, per_dev * tile)
    psf_row = jnp.concatenate(
        [psf_part, weight_part[None], jnp.zeros((per_dev * tile - BASIS - 1,), jnp.float32)]
    )
    extra = jnp.concatenate(
        [
            pos_lanes,
            jnp.broadcast_to(psf_row[None, None, :], (n_visit, 1, per_dev * tile)),
            jnp.zeros((n_visit, EXTRA - 2, per_dev * tile), jnp.float32),
        ],
        axis=1,
    )
    var_pos = variance_field(
        where, weight * weight, got_vm, (n_visit, GRID * tile, per_dev * tile)
    )
    var_share = reduce_scatter_visit(var_pos, n_visit)

    part_im = lax.all_to_all(send_im, "sky", split_axis=0, concat_axis=0, tiled=True)
    var_share, part_im = lax.optimization_barrier((var_share, part_im))
    part_im = part_im.reshape(slots_all, tile, tile)
    image_pos = image_field(
        where, weight, got_coef.reshape(slots_all * BASIS), part_im,
        row_side, col_side, extra, (n_visit, GRID * tile + EXTRA, per_dev * tile),
    )
    image_share = reduce_scatter_visit(image_pos, n_visit)

    body_rows = GRID * tile
    pos_weight = image_share[body_rows, :].reshape(per_dev, tile)[:, :GRID]
    denom = jnp.maximum(pos_weight, weight_floor).T
    denom = jnp.broadcast_to(denom[:, None, :, None], (GRID, tile, per_dev, tile))
    denom = denom.reshape(body_rows, per_dev * tile)
    coadd_image = image_share[:body_rows, :] / denom
    coadd_variance = var_share / (denom * denom)

    psf_total = image_share[body_rows + 1, :BASIS]
    weight_total = image_share[body_rows + 1, BASIS]
    share = psf_total / weight_total
    high = lax.Precision.HIGHEST
    coadd_psf = jnp.einsum(
        "k,ka,kb->ab",
        share,
        col_taps.astype(jnp.float32),
        row_taps.astype(jnp.float32),
        precision=high,
    )[None]
    return (coadd_image, coadd_variance, coadd_psf)


def solution(mesh):
    return jax.shard_map(
        shards,
        mesh=mesh,
        in_specs=(
            P("visit", "sky", None, None),
            P("visit", "sky", None, None),
            P("visit", "sky", None),
            P("visit", "sky", None),
            P("visit", "sky"),
            P(),
            P(),
        ),
        out_specs=(P("sky", "visit"), P("sky", "visit"), P("sky", None, None)),
        check_vma=False,
    )
```

```python
import jax
import jax.numpy as jnp
from jax import lax
from jax.experimental import pallas as pl
from jax.experimental.pallas import tpu as pltpu
from jax.sharding import PartitionSpec as P

GRID = 8
BASIS = 9
META = 16
EXTRA = 8
GANG = 4


weight_floor = 0.5


def band_table(taps, tile):
    span = taps.shape[1]
    offset = jnp.arange(tile)[:, None] - jnp.arange(tile)[None, :] + (span - 1) // 2
    select = (offset[None, :, :] == jnp.arange(span)[:, None, None]).astype(jnp.float32)
    return jnp.einsum("kt,tij->kij", taps.astype(jnp.float32), select).astype(jnp.bfloat16)


def place_tile(out_refs, row, group, sub, contrib):
    tile = contrib.shape[0]
    half = out_refs[0].shape[0]
    per_dev = out_refs[0].shape[2] // tile
    start = pl.multiple_of(row * tile, tile)
    for which, out_ref in enumerate(out_refs):
        for c in range(per_dev):

            @pl.when((sub == c) & (group >= which * half) & (group < (which + 1) * half))
            def _():
                out_ref[group - which * half, pl.ds(start, tile), c * tile:(c + 1) * tile] += contrib


def variance_kernel(row_ref, group_ref, sub_ref, w2_ref, *refs):
    chunks, out_refs = refs[:-2], refs[-2:]
    held = chunks[0].shape[0]
    tile = chunks[0].shape[2]
    for out_ref in out_refs:
        out_ref[...] = jnp.zeros(out_ref.shape, jnp.float32)
    for d, chunk in enumerate(chunks):

        def body(r, carry):
            t = d * held + r
            row = row_ref[t]

            @pl.when(row >= 0)
            def _():
                contrib = w2_ref[t] * chunk[r, :tile, :].astype(jnp.float32)
                place_tile(out_refs, row, group_ref[t], sub_ref[t], contrib)

            return carry

        lax.fori_loop(0, held, body, 0)


def image_kernel(order_ref, count_ref, row_ref, group_ref, sub_ref, w_ref, coef_ref, img_ref,
                 row_side_ref, col_side_ref, extra_ref, *out_refs):
    tile = img_ref.shape[2]
    half, height, width = out_refs[0].shape
    body_rows = height - extra_ref.shape[1]
    for which, out_ref in enumerate(out_refs):
        out_ref[:, :body_rows, :] = jnp.zeros((half, body_rows, width), jnp.float32)
        out_ref[:, body_rows:, :] = extra_ref[which * half:(which + 1) * half]

    def body(p, carry):
        pair = tuple(order_ref[GANG * p + h] for h in range(GANG))
        both = jnp.concatenate([img_ref[t] for t in pair], axis=0)
        first = jnp.dot(both, row_side_ref[...], preferred_element_type=jnp.float32)
        blocks = []
        for k in range(BASIS):
            halves = [
                (first[h * tile:(h + 1) * tile, k * tile:(k + 1) * tile]
                 * coef_ref[pair[h] * BASIS + k]).astype(jnp.bfloat16)
                for h in range(GANG)
            ]
            blocks.append(jnp.concatenate(halves, axis=1))
        scaled = jnp.concatenate(blocks, axis=0)
        matched = jnp.dot(col_side_ref[...], scaled, preferred_element_type=jnp.float32)
        for h in range(GANG):
            t = pair[h]
            row = row_ref[t]

            @pl.when(row >= 0)
            def _():
                place_tile(out_refs, row, group_ref[t], sub_ref[t],
                           w_ref[t] * matched[:, h * tile:(h + 1) * tile])

        return carry

    lax.fori_loop(0, (count_ref[0] + GANG - 1) // GANG, body, 0)


def smem():
    return pl.BlockSpec(memory_space=pltpu.SMEM)


def vmem():
    return pl.BlockSpec(memory_space=pltpu.VMEM)


def halves_of(field_shape):
    half = jax.ShapeDtypeStruct((field_shape[0] // 2,) + tuple(field_shape[1:]), jnp.float32)
    return [half, half]


def variance_field(where, w2, chunks, field_shape):
    return pl.pallas_call(
        variance_kernel,
        out_shape=halves_of(field_shape),
        in_specs=[smem()] * 4 + [vmem()] * len(chunks),
        out_specs=[vmem(), vmem()],
    )(*where, w2, *chunks)


def image_field(where, w, coef, images, row_side, col_side, extra, field_shape):
    filled = where[0] >= 0
    order = jnp.argsort(jnp.logical_not(filled), stable=True).astype(jnp.int32)
    count = jnp.sum(filled.astype(jnp.int32))[None]
    return pl.pallas_call(
        image_kernel,
        out_shape=halves_of(field_shape),
        in_specs=[smem()] * 7 + [vmem()] * 4,
        out_specs=[vmem(), vmem()],
        cost_estimate=pl.CostEstimate(
            flops=4 * images.shape[0] * images.shape[2] ** 3 * BASIS,
            transcendentals=0,
            bytes_accessed=images.size * 2 + 4 * (field_shape[0] * field_shape[1] * field_shape[2]),
        ),
    )(order, count, *where, w, coef, images, row_side, col_side, extra)


def bit_reverse(values, bits):
    out = jnp.zeros_like(values)
    for b in range(bits):
        out = out | (((values >> b) & 1) << (bits - 1 - b))
    return out


def reduce_scatter_visit(halves, n_visit):
    bits = n_visit.bit_length() - 1
    keep, send = halves
    for b in range(bits):
        pairs = [(i, i ^ (1 << b)) for i in range(n_visit)]
        got = lax.ppermute(send, "visit", perm=pairs)
        half = keep.shape[0] // 2
        if half == 0:
            return (keep + got)[0]
        send = keep[half:] + got[half:]
        keep = keep[:half] + got[:half]


def shards(tile_image, tile_variance, match_coeffs, tile_patch, tile_offset, row_taps, col_taps):
    n_sky = lax.axis_size("sky")
    n_visit = lax.axis_size("visit")
    images = tile_image[0]
    variance = tile_variance[0]
    coeffs = match_coeffs[0]
    count = images.shape[0]
    tile = images.shape[1]
    held_most = max(2, 2 * count // n_sky)
    positions = GRID * GRID
    per_dev = GRID // n_visit
    dest = tile_patch[0, :, 0]
    offsets = tile_offset[0]
    band_row = band_table(row_taps, tile)
    band_col = band_table(col_taps, tile)
    row_side = band_row.transpose(1, 0, 2).reshape(tile, BASIS * tile)
    col_side = band_col.transpose(2, 0, 1).reshape(tile, BASIS * tile)
    order = jnp.arange(count)
    earlier = (dest[:, None] == dest[None, :]) & (order[None, :] < order[:, None])
    rank = jnp.sum(earlier.astype(jnp.int32), axis=1)
    slot = dest * held_most + rank
    slots_all = n_sky * held_most
    pick = (jnp.arange(slots_all)[:, None] == slot[None, :]).astype(jnp.bfloat16)
    meta_row = jnp.concatenate(
        [coeffs, (offsets + 1).astype(jnp.bfloat16)[:, None],
         jnp.zeros((count, tile - BASIS - 1), jnp.bfloat16)],
        axis=1,
    )
    meta = jnp.concatenate(
        [meta_row[:, None, :], jnp.zeros((count, META - 1, tile), jnp.bfloat16)], axis=1
    )
    var_meta = jnp.concatenate([variance, meta], axis=1)
    taken = (jnp.arange(slots_all)[:, None] == slot[None, :]).astype(jnp.int32)
    source_tile = jnp.sum(taken * order[None, :], axis=1) + count * (1 - jnp.sum(taken, axis=1))

    def gather_slots(values):
        padded = jnp.concatenate([values, jnp.zeros((1,) + values.shape[1:], values.dtype)])
        return jnp.take(padded, source_tile, axis=0, mode="clip").reshape(
            (n_sky, held_most) + values.shape[1:]
        )

    send_vm = gather_slots(var_meta)
    send_im = gather_slots(images)

    part_vm = lax.all_to_all(send_vm, "sky", split_axis=0, concat_axis=0, tiled=True)
    part_vm, send_im = lax.optimization_barrier((part_vm, send_im))
    got_vm = [part_vm.reshape(slots_all, tile + META, tile)]
    got_meta = got_vm[0][:, tile, :].astype(jnp.float32)
    got_coef = got_meta[:, :BASIS]
    place = got_meta[:, BASIS].astype(jnp.int32) - 1
    valid = place >= 0
    mean_var = jnp.mean(got_vm[0][:, :tile, :].astype(jnp.float32), axis=(1, 2))
    weight = jnp.where(valid, 1.0 / jnp.where(valid, mean_var, 1.0), 0.0)
    tile_row = jnp.where(valid, place // GRID, -1)
    tile_col = place % GRID
    bits = n_visit.bit_length() - 1
    me_visit = lax.axis_index("visit")
    where = (tile_row, bit_reverse((tile_col // per_dev) ^ me_visit, bits), tile_col % per_dev)
    psf_part = jnp.sum(weight[:, None] * got_coef, axis=0)
    weight_part = jnp.sum(weight)
    weight_pos = jnp.sum(
        jnp.where(jnp.arange(positions)[:, None] == place[None, :], weight[None, :], 0.0), axis=1
    )
    pos_lanes = weight_pos.reshape(GRID, n_visit, per_dev).transpose(1, 2, 0)
    pos_lanes = jnp.take(pos_lanes, bit_reverse(jnp.arange(n_visit), bits) ^ me_visit, axis=0)
    pos_lanes = jnp.concatenate(
        [pos_lanes, jnp.zeros((n_visit, per_dev, tile - GRID), jnp.float32)], axis=2
    ).reshape(n_visit, 1, per_dev * tile)
    psf_row = jnp.concatenate(
        [psf_part, weight_part[None], jnp.zeros((per_dev * tile - BASIS - 1,), jnp.float32)]
    )
    extra = jnp.concatenate(
        [
            pos_lanes,
            jnp.broadcast_to(psf_row[None, None, :], (n_visit, 1, per_dev * tile)),
            jnp.zeros((n_visit, EXTRA - 2, per_dev * tile), jnp.float32),
        ],
        axis=1,
    )
    var_pos = variance_field(
        where, weight * weight, got_vm, (n_visit, GRID * tile, per_dev * tile)
    )
    var_share = reduce_scatter_visit(var_pos, n_visit)

    part_im = lax.all_to_all(send_im, "sky", split_axis=0, concat_axis=0, tiled=True)
    var_share, part_im = lax.optimization_barrier((var_share, part_im))
    part_im = part_im.reshape(slots_all, tile, tile)
    image_pos = image_field(
        where, weight, got_coef.reshape(slots_all * BASIS), part_im,
        row_side, col_side, extra, (n_visit, GRID * tile + EXTRA, per_dev * tile),
    )
    image_share = reduce_scatter_visit(image_pos, n_visit)

    body_rows = GRID * tile
    pos_weight = image_share[body_rows, :].reshape(per_dev, tile)[:, :GRID]
    denom = jnp.maximum(pos_weight, weight_floor).T
    denom = jnp.broadcast_to(denom[:, None, :, None], (GRID, tile, per_dev, tile))
    denom = denom.reshape(body_rows, per_dev * tile)
    coadd_image = image_share[:body_rows, :] / denom
    coadd_variance = var_share / (denom * denom)

    psf_total = image_share[body_rows + 1, :BASIS]
    weight_total = image_share[body_rows + 1, BASIS]
    share = psf_total / weight_total
    high = lax.Precision.HIGHEST
    coadd_psf = jnp.einsum(
        "k,ka,kb->ab",
        share,
        col_taps.astype(jnp.float32),
        row_taps.astype(jnp.float32),
        precision=high,
    )[None]
    return (coadd_image, coadd_variance, coadd_psf)


def solution(mesh):
    return jax.shard_map(
        shards,
        mesh=mesh,
        in_specs=(
            P("visit", "sky", None, None),
            P("visit", "sky", None, None),
            P("visit", "sky", None),
            P("visit", "sky", None),
            P("visit", "sky"),
            P(),
            P(),
        ),
        out_specs=(P("sky", "visit"), P("sky", "visit"), P("sky", None, None)),
        check_vma=False,
    )
```

```python
import jax
import jax.numpy as jnp
from jax import lax
from jax.experimental import pallas as pl
from jax.experimental.pallas import tpu as pltpu
from jax.sharding import PartitionSpec as P

GRID = 8
BASIS = 9
META = 16
EXTRA = 8
GANG = 4


weight_floor = 0.5


def band_table(taps, tile):
    span = taps.shape[1]
    offset = jnp.arange(tile)[:, None] - jnp.arange(tile)[None, :] + (span - 1) // 2
    select = (offset[None, :, :] == jnp.arange(span)[:, None, None]).astype(jnp.float32)
    return jnp.einsum("kt,tij->kij", taps.astype(jnp.float32), select).astype(jnp.bfloat16)


def place_tile(out_refs, row, group, sub, contrib):
    tile = contrib.shape[0]
    half = out_refs[0].shape[0]
    per_dev = out_refs[0].shape[2] // tile
    start = pl.multiple_of(row * tile, tile)
    for which, out_ref in enumerate(out_refs):
        for c in range(per_dev):

            @pl.when((sub == c) & (group >= which * half) & (group < (which + 1) * half))
            def _():
                out_ref[group - which * half, pl.ds(start, tile), c * tile:(c + 1) * tile] += contrib


def variance_kernel(row_ref, group_ref, sub_ref, w2_ref, *refs):
    chunks, out_refs = refs[:-2], refs[-2:]
    held = chunks[0].shape[0]
    tile = chunks[0].shape[2]
    for out_ref in out_refs:
        out_ref[...] = jnp.zeros(out_ref.shape, jnp.float32)
    for d, chunk in enumerate(chunks):

        def body(r, carry):
            t = d * held + r
            row = row_ref[t]

            @pl.when(row >= 0)
            def _():
                contrib = w2_ref[t] * chunk[r, :tile, :].astype(jnp.float32)
                place_tile(out_refs, row, group_ref[t], sub_ref[t], contrib)

            return carry

        lax.fori_loop(0, held, body, 0)


def image_kernel(order_ref, count_ref, row_ref, group_ref, sub_ref, w_ref, coef_ref, img_ref,
                 row_side_ref, col_side_ref, extra_ref, *out_refs):
    tile = img_ref.shape[2]
    half, height, width = out_refs[0].shape
    body_rows = height - extra_ref.shape[1]
    for which, out_ref in enumerate(out_refs):
        out_ref[:, :body_rows, :] = jnp.zeros((half, body_rows, width), jnp.float32)
        out_ref[:, body_rows:, :] = extra_ref[which * half:(which + 1) * half]

    def body(p, carry):
        pair = tuple(order_ref[GANG * p + h] for h in range(GANG))
        both = img_ref[pl.ds(GANG * p, GANG)].reshape(GANG * tile, tile)
        first = jnp.dot(both, row_side_ref[...], preferred_element_type=jnp.float32)
        blocks = []
        for k in range(BASIS):
            halves = [
                (first[h * tile:(h + 1) * tile, k * tile:(k + 1) * tile]
                 * coef_ref[pair[h] * BASIS + k]).astype(jnp.bfloat16)
                for h in range(GANG)
            ]
            blocks.append(jnp.concatenate(halves, axis=1))
        scaled = jnp.concatenate(blocks, axis=0)
        matched = jnp.dot(col_side_ref[...], scaled, preferred_element_type=jnp.float32)
        for h in range(GANG):
            t = pair[h]
            row = row_ref[t]

            @pl.when(row >= 0)
            def _():
                place_tile(out_refs, row, group_ref[t], sub_ref[t],
                           w_ref[t] * matched[:, h * tile:(h + 1) * tile])

        return carry

    lax.fori_loop(0, (count_ref[0] + GANG - 1) // GANG, body, 0)


def smem():
    return pl.BlockSpec(memory_space=pltpu.SMEM)


def vmem():
    return pl.BlockSpec(memory_space=pltpu.VMEM)


def halves_of(field_shape):
    half = jax.ShapeDtypeStruct((field_shape[0] // 2,) + tuple(field_shape[1:]), jnp.float32)
    return [half, half]


def variance_field(where, w2, chunks, field_shape):
    return pl.pallas_call(
        variance_kernel,
        out_shape=halves_of(field_shape),
        in_specs=[smem()] * 4 + [vmem()] * len(chunks),
        out_specs=[vmem(), vmem()],
    )(*where, w2, *chunks)


def image_field(where, w, coef, images, row_side, col_side, extra, field_shape):
    filled = where[0] >= 0
    order = jnp.argsort(jnp.logical_not(filled), stable=True).astype(jnp.int32)
    count = jnp.sum(filled.astype(jnp.int32))[None]
    return pl.pallas_call(
        image_kernel,
        out_shape=halves_of(field_shape),
        in_specs=[smem()] * 7 + [vmem()] * 4,
        out_specs=[vmem(), vmem()],
        cost_estimate=pl.CostEstimate(
            flops=4 * images.shape[0] * images.shape[2] ** 3 * BASIS,
            transcendentals=0,
            bytes_accessed=images.size * 2 + 4 * (field_shape[0] * field_shape[1] * field_shape[2]),
        ),
    )(order, count, *where, w, coef, jnp.take(images, order, axis=0), row_side, col_side, extra)


def bit_reverse(values, bits):
    out = jnp.zeros_like(values)
    for b in range(bits):
        out = out | (((values >> b) & 1) << (bits - 1 - b))
    return out


def reduce_scatter_visit(halves, n_visit):
    bits = n_visit.bit_length() - 1
    keep, send = halves
    for b in range(bits):
        pairs = [(i, i ^ (1 << b)) for i in range(n_visit)]
        field = keep + lax.ppermute(send, "visit", perm=pairs)
        half = field.shape[0] // 2
        keep, send = field[:half], field[half:]
    return field[0]


def shards(tile_image, tile_variance, match_coeffs, tile_patch, tile_offset, row_taps, col_taps):
    n_sky = lax.axis_size("sky")
    n_visit = lax.axis_size("visit")
    images = tile_image[0]
    variance = tile_variance[0]
    coeffs = match_coeffs[0]
    count = images.shape[0]
    tile = images.shape[1]
    held_most = max(2, 2 * count // n_sky)
    positions = GRID * GRID
    per_dev = GRID // n_visit
    dest = tile_patch[0, :, 0]
    offsets = tile_offset[0]
    band_row = band_table(row_taps, tile)
    band_col = band_table(col_taps, tile)
    row_side = band_row.transpose(1, 0, 2).reshape(tile, BASIS * tile)
    col_side = band_col.transpose(2, 0, 1).reshape(tile, BASIS * tile)
    order = jnp.arange(count)
    earlier = (dest[:, None] == dest[None, :]) & (order[None, :] < order[:, None])
    rank = jnp.sum(earlier.astype(jnp.int32), axis=1)
    slot = dest * held_most + rank
    slots_all = n_sky * held_most
    pick = (jnp.arange(slots_all)[:, None] == slot[None, :]).astype(jnp.bfloat16)
    meta_row = jnp.concatenate(
        [coeffs, (offsets + 1).astype(jnp.bfloat16)[:, None],
         jnp.zeros((count, tile - BASIS - 1), jnp.bfloat16)],
        axis=1,
    )
    meta = jnp.concatenate(
        [meta_row[:, None, :], jnp.zeros((count, META - 1, tile), jnp.bfloat16)], axis=1
    )
    var_meta = jnp.concatenate([variance, meta], axis=1)
    taken = (jnp.arange(slots_all)[:, None] == slot[None, :]).astype(jnp.int32)
    source_tile = jnp.sum(taken * order[None, :], axis=1) + count * (1 - jnp.sum(taken, axis=1))

    def gather_slots(values):
        padded = jnp.concatenate([values, jnp.zeros((1,) + values.shape[1:], values.dtype)])
        return jnp.take(padded, source_tile, axis=0, mode="clip").reshape(
            (n_sky, held_most) + values.shape[1:]
        )

    send_vm = gather_slots(var_meta)
    send_im = gather_slots(images)

    part_vm = lax.all_to_all(send_vm, "sky", split_axis=0, concat_axis=0, tiled=True)
    part_vm, send_im = lax.optimization_barrier((part_vm, send_im))
    got_vm = [part_vm.reshape(slots_all, tile + META, tile)]
    got_meta = got_vm[0][:, tile, :].astype(jnp.float32)
    got_coef = got_meta[:, :BASIS]
    place = got_meta[:, BASIS].astype(jnp.int32) - 1
    valid = place >= 0
    mean_var = jnp.mean(got_vm[0][:, :tile, :].astype(jnp.float32), axis=(1, 2))
    weight = jnp.where(valid, 1.0 / jnp.where(valid, mean_var, 1.0), 0.0)
    tile_row = jnp.where(valid, place // GRID, -1)
    tile_col = place % GRID
    bits = n_visit.bit_length() - 1
    me_visit = lax.axis_index("visit")
    where = (tile_row, bit_reverse((tile_col // per_dev) ^ me_visit, bits), tile_col % per_dev)
    psf_part = jnp.sum(weight[:, None] * got_coef, axis=0)
    weight_part = jnp.sum(weight)
    weight_pos = jnp.sum(
        jnp.where(jnp.arange(positions)[:, None] == place[None, :], weight[None, :], 0.0), axis=1
    )
    pos_lanes = weight_pos.reshape(GRID, n_visit, per_dev).transpose(1, 2, 0)
    pos_lanes = jnp.take(pos_lanes, bit_reverse(jnp.arange(n_visit), bits) ^ me_visit, axis=0)
    pos_lanes = jnp.concatenate(
        [pos_lanes, jnp.zeros((n_visit, per_dev, tile - GRID), jnp.float32)], axis=2
    ).reshape(n_visit, 1, per_dev * tile)
    psf_row = jnp.concatenate(
        [psf_part, weight_part[None], jnp.zeros((per_dev * tile - BASIS - 1,), jnp.float32)]
    )
    extra = jnp.concatenate(
        [
            pos_lanes,
            jnp.broadcast_to(psf_row[None, None, :], (n_visit, 1, per_dev * tile)),
            jnp.zeros((n_visit, EXTRA - 2, per_dev * tile), jnp.float32),
        ],
        axis=1,
    )
    var_pos = variance_field(
        where, weight * weight, got_vm, (n_visit, GRID * tile, per_dev * tile)
    )
    var_share = reduce_scatter_visit(var_pos, n_visit)

    part_im = lax.all_to_all(send_im, "sky", split_axis=0, concat_axis=0, tiled=True)
    var_share, part_im = lax.optimization_barrier((var_share, part_im))
    part_im = part_im.reshape(slots_all, tile, tile)
    image_pos = image_field(
        where, weight, got_coef.reshape(slots_all * BASIS), part_im,
        row_side, col_side, extra, (n_visit, GRID * tile + EXTRA, per_dev * tile),
    )
    image_share = reduce_scatter_visit(image_pos, n_visit)

    body_rows = GRID * tile
    pos_weight = image_share[body_rows, :].reshape(per_dev, tile)[:, :GRID]
    denom = jnp.maximum(pos_weight, weight_floor).T
    denom = jnp.broadcast_to(denom[:, None, :, None], (GRID, tile, per_dev, tile))
    denom = denom.reshape(body_rows, per_dev * tile)
    coadd_image = image_share[:body_rows, :] / denom
    coadd_variance = var_share / (denom * denom)

    psf_total = image_share[body_rows + 1, :BASIS]
    weight_total = image_share[body_rows + 1, BASIS]
    share = psf_total / weight_total
    high = lax.Precision.HIGHEST
    coadd_psf = jnp.einsum(
        "k,ka,kb->ab",
        share,
        col_taps.astype(jnp.float32),
        row_taps.astype(jnp.float32),
        precision=high,
    )[None]
    return (coadd_image, coadd_variance, coadd_psf)


def solution(mesh):
    return jax.shard_map(
        shards,
        mesh=mesh,
        in_specs=(
            P("visit", "sky", None, None),
            P("visit", "sky", None, None),
            P("visit", "sky", None),
            P("visit", "sky", None),
            P("visit", "sky"),
            P(),
            P(),
        ),
        out_specs=(P("sky", "visit"), P("sky", "visit"), P("sky", None, None)),
        check_vma=False,
    )
```
